32 devices in a mesh: rows: 4 (over y, x), cols: 8 (over z, core).
Axes of the slice: x: 2, y: 2, z: 4, core: 2. Of those that a mesh axis runs over, the one named last changes fastest.
Arguments:
- features: bfloat16 [32, 128, 1024], P('rows', 'cols'), may hold values from -24 to 24
- w_query: bfloat16 [1024, 1024], replicated, may hold values from -0.1875 to 0.1875
- w_key: bfloat16 [1024, 1024], replicated, may hold values from -0.1875 to 0.1875
- w_value: bfloat16 [1024, 1024], replicated, may hold values from -0.1875 to 0.1875
- w_out: bfloat16 [1024, 1024], replicated, may hold values from -0.1875 to 0.1875
- reg_pos: int32 [32], replicated, may hold values from 0 to 4095, as said below
- grad_out: bfloat16 [32, 128, 1024], P('rows', 'cols'), may hold values from -6 to 6
Outputs:
- layer_out: bfloat16 [32, 128, 1024], P('rows', 'cols')
- grad_in: bfloat16 [32, 128, 1024], P('rows', 'cols')
The draws below stay inside these ranges and needn't reach their ends.
Inputs may be any that keep to these rules, and one draw needn't show every extreme that they name: The 32 global tokens are distinct, one in each tile of 128 tokens: reg_pos[r] lies in tile row r // 8 and tile column r % 8, tiles counted row by row.
All inputs are finite; a program needn't handle non-finite values.
Results may differ from the reference program's by a relative error of at most 0.03.
The reference program's roundings to bfloat16 on the way count: a program that leaves them out, or rounds other values in their place, can miss the bound.
Values may be sent and summed in bfloat16 or wider, within the bound.
No kernel may reach another device: no remote copies, remote signals or barrier semaphores. Data moves between devices by JAX's collectives and lax.ppermute only.
A program may use at most 128 MiB of HBM per device.

```python
import math
import jax
import jax.numpy as jnp
from jax import lax

D = 1024
HEADS = 16
KW = 13
RAD = 6
BLK = 8
TR = 8
TC = 16
HR = 32
HC = 128
R = 32


def draw_features(key, part):
    return jnp.clip(jax.random.normal(key, (HR, HC, D), jnp.float32), -6.0, 6.0).astype(jnp.bfloat16)


def draw_reg_pos(key, part):
    tiles_across = HC // TC
    tile_ids = jnp.arange(R, dtype=jnp.int32)
    row_key, col_key = jax.random.split(jax.random.fold_in(key, 5))
    row_offset = jax.random.randint(row_key, (R,), 0, TR, dtype=jnp.int32)
    col_offset = jax.random.randint(col_key, (R,), 0, TC, dtype=jnp.int32)
    row_cell = tile_ids // tiles_across * TR + row_offset
    col_cell = tile_ids % tiles_across * TC + col_offset
    return row_cell * HC + col_cell


def levels(own_key, shape, cuts, smallest, largest):
    def one(dim, blocks):
        heights = jax.random.uniform(jax.random.fold_in(jax.random.fold_in(own_key, 6), dim), (blocks,), jnp.float32, smallest / len(cuts), largest / len(cuts))
        return jnp.repeat(jnp.exp(heights), shape[dim] // blocks).reshape((-1,) + (1,) * (len(shape) - dim - 1))

    gain = one(*cuts[0])
    for cut in cuts[1:]:
        gain = gain * one(*cut)
    return gain


def centred(rng, shape, spread, most, cuts=(), kind=jnp.bfloat16):
    values = spread * jax.random.normal(rng, shape, jnp.float32)
    if cuts:
        values = values * levels(rng, shape, cuts, -0.22, 0.18)
    return jnp.clip(values, -most, most).astype(kind)


def setup_inputs(seed: int = 0) -> dict:
    arg_keys = jax.random.split(jax.random.key(seed), 8)
    features = draw_features(jax.random.fold_in(arg_keys[7], 71), 0)
    w_query = centred(arg_keys[1], (D, D), D ** -0.5, 0.1875)
    w_key = centred(arg_keys[2], (D, D), D ** -0.5, 0.1875)
    w_value = centred(arg_keys[3], (D, D), D ** -0.5, 0.1875)
    w_out = centred(arg_keys[4], (D, D), D ** -0.5, 0.1875)
    reg_pos = draw_reg_pos(jax.random.fold_in(arg_keys[7], 71), 0)
    grad_out = centred(arg_keys[6], (HR, HC, D), 1.0, 6.0, ((0, 4), (1, 8)))
    return dict(features=features, w_query=w_query, w_key=w_key, w_value=w_value, w_out=w_out, reg_pos=reg_pos, grad_out=grad_out)


def einsum_exact(form, left, right):
    return jnp.einsum(form, left.astype(jnp.float32), right.astype(jnp.float32), precision=lax.Precision.HIGHEST)

def axis_mask(first_cell, extent, block_count):
    block_ids = jnp.arange(block_count, dtype=jnp.int32)[:, None, None]
    within = jnp.arange(BLK, dtype=jnp.int32)[None, :, None]
    offsets = jnp.arange(BLK + 2 * RAD, dtype=jnp.int32)[None, None, :]
    query_cell = first_cell + BLK * block_ids + within
    window_start = jnp.clip(query_cell - RAD, 0, extent - KW)
    key_cell = first_cell + BLK * block_ids - RAD + offsets
    return (key_cell >= window_start) & (key_cell <= window_start + KW - 1)

def block_mask(row_mask, col_mask):
    row_blocks = row_mask.shape[0]
    col_blocks = col_mask.shape[0]
    span_cells = BLK + 2 * RAD
    joined = row_mask[:, None, :, None, :, None] & col_mask[None, :, None, :, None, :]
    return joined.reshape(row_blocks * col_blocks, BLK * BLK, span_cells * span_cells)

def to_blocks(cell_grid, row_blocks, col_blocks):
    channels = cell_grid.shape[-1]
    shaped = cell_grid.reshape(row_blocks, BLK, col_blocks, BLK, channels).transpose(0, 2, 1, 3, 4)
    return shaped.reshape(row_blocks * col_blocks, BLK * BLK, channels)

def from_blocks(blocks, row_blocks, col_blocks):
    channels = blocks.shape[-1]
    shaped = blocks.reshape(row_blocks, col_blocks, BLK, BLK, channels).transpose(0, 2, 1, 3, 4)
    return shaped.reshape(row_blocks * BLK, col_blocks * BLK, channels)

def windows(framed, row_blocks, col_blocks):
    channels = framed.shape[-1]
    span_cells = BLK + 2 * RAD
    width_cells = framed.shape[1]
    row_slabs = framed.reshape(row_blocks + 2, BLK, width_cells, channels)
    banded = jnp.concatenate([row_slabs[0:row_blocks], row_slabs[1:row_blocks + 1], row_slabs[2:row_blocks + 2]], axis=1)[:, :span_cells]
    pieces = banded.reshape(row_blocks, span_cells, col_blocks + 2, BLK, channels)
    boxed_kv = jnp.concatenate([pieces[:, :, 0:col_blocks], pieces[:, :, 1:col_blocks + 1], pieces[:, :, 2:col_blocks + 2]], axis=3)[:, :, :, :span_cells]
    return boxed_kv.transpose(0, 2, 1, 3, 4).reshape(row_blocks * col_blocks, span_cells * span_cells, channels)

def windows_adjoint(block_grads, row_blocks, col_blocks):
    channels = block_grads.shape[-1]
    span_cells = BLK + 2 * RAD
    spare_cells = 3 * BLK - span_cells
    keep_dim = (0, 0)
    boxed_grads = block_grads.reshape(row_blocks, col_blocks, span_cells, span_cells, channels).transpose(0, 2, 1, 3, 4)
    boxed_grads = jnp.pad(boxed_grads, (keep_dim, keep_dim, keep_dim, (0, spare_cells), keep_dim))
    pieces = boxed_grads.reshape(row_blocks, span_cells, col_blocks, 3, BLK, channels)
    col_sum = jnp.pad(pieces[:, :, :, 0], (keep_dim, keep_dim, (0, 2), keep_dim, keep_dim)) + jnp.pad(pieces[:, :, :, 1], (keep_dim, keep_dim, (1, 1), keep_dim, keep_dim)) + jnp.pad(pieces[:, :, :, 2], (keep_dim, keep_dim, (2, 0), keep_dim, keep_dim))
    col_sum = col_sum.reshape(row_blocks, span_cells, (col_blocks + 2) * BLK, channels)
    col_sum = jnp.pad(col_sum, (keep_dim, (0, spare_cells), keep_dim, keep_dim))
    row_pieces = col_sum.reshape(row_blocks, 3, BLK, (col_blocks + 2) * BLK, channels)
    row_sum = jnp.pad(row_pieces[:, 0], ((0, 2), keep_dim, keep_dim, keep_dim)) + jnp.pad(row_pieces[:, 1], ((1, 1), keep_dim, keep_dim, keep_dim)) + jnp.pad(row_pieces[:, 2], ((2, 0), keep_dim, keep_dim, keep_dim))
    return row_sum.reshape((row_blocks + 2) * BLK, (col_blocks + 2) * BLK, channels)

def split_heads(query_blocks, window_kv, global_kv):
    block_count, query_count, model_width = query_blocks.shape
    head_size = model_width // HEADS
    query_heads = query_blocks.reshape(block_count, query_count, HEADS, head_size)
    window_keys = window_kv[:, :, :model_width].reshape(block_count, -1, HEADS, head_size)
    window_values = window_kv[:, :, model_width:].reshape(block_count, -1, HEADS, head_size)
    global_keys = global_kv[:, :model_width].reshape(-1, HEADS, head_size)
    global_values = global_kv[:, model_width:].reshape(-1, HEADS, head_size)
    return (query_heads, window_keys, window_values, global_keys, global_values)

def forward_block(query_blocks, window_kv, global_kv, window_mask):
    block_count, query_count, model_width = query_blocks.shape
    score_scale = 1.0 / math.sqrt(model_width // HEADS)
    query_heads, window_keys, window_values, global_keys, global_values = split_heads(query_blocks, window_kv, global_kv)
    window_scores = einsum_exact('bqhd,bkhd->bhqk', query_heads, window_keys) * score_scale
    window_scores = jnp.where(window_mask[:, None], window_scores, -1e+30)
    global_scores = einsum_exact('bqhd,rhd->bhqr', query_heads, global_keys) * score_scale
    row_max = jnp.maximum(lax.optimization_barrier(jnp.max(window_scores, axis=-1, keepdims=True)), lax.optimization_barrier(jnp.max(global_scores, axis=-1, keepdims=True)))
    window_exp = jnp.exp(window_scores - row_max)
    global_exp = jnp.exp(global_scores - row_max)
    denominator = lax.optimization_barrier(jnp.sum(window_exp, axis=-1, keepdims=True)) + lax.optimization_barrier(jnp.sum(global_exp, axis=-1, keepdims=True))
    window_probs = window_exp / denominator
    global_probs = global_exp / denominator
    window_rounded = window_probs.astype(jnp.bfloat16)
    global_rounded = global_probs.astype(jnp.bfloat16)
    attended = einsum_exact('bhqk,bkhd->bqhd', window_rounded, window_values) + einsum_exact('bhqr,rhd->bqhd', global_rounded, global_values)
    attended = attended.astype(jnp.bfloat16).reshape(block_count, query_count, model_width)
    return ((window_probs, global_probs, window_rounded, global_rounded), attended)

def backward_block(query_blocks, window_kv, global_kv, probs, attended, grad_blocks):
    block_count, query_count, model_width = query_blocks.shape
    head_size = model_width // HEADS
    score_scale = 1.0 / math.sqrt(head_size)
    window_probs, global_probs, window_rounded, global_rounded = probs
    query_heads, window_keys, window_values, global_keys, global_values = split_heads(query_blocks, window_kv, global_kv)
    grad_heads = grad_blocks.reshape(block_count, query_count, HEADS, head_size)
    attended_heads = attended.reshape(block_count, query_count, HEADS, head_size)
    delta_terms = einsum_exact('bqhd,bqhd->bhq', grad_heads, attended_heads)[..., None]
    window_dots = einsum_exact('bqhd,bkhd->bhqk', grad_heads, window_values)
    global_dots = einsum_exact('bqhd,rhd->bhqr', grad_heads, global_values)
    window_slopes = (window_probs * (window_dots - delta_terms) * score_scale).astype(jnp.bfloat16)
    global_slopes = (global_probs * (global_dots - delta_terms) * score_scale).astype(jnp.bfloat16)
    query_grads = einsum_exact('bhqk,bkhd->bqhd', window_slopes, window_keys) + einsum_exact('bhqr,rhd->bqhd', global_slopes, global_keys)
    query_grads = query_grads.astype(jnp.bfloat16).reshape(block_count, query_count, model_width)
    window_key_grads = einsum_exact('bhqk,bqhd->bkhd', window_slopes, query_heads).reshape(block_count, -1, model_width)
    window_value_grads = einsum_exact('bhqk,bqhd->bkhd', window_rounded, grad_heads).reshape(block_count, -1, model_width)
    global_key_grads = einsum_exact('bhqr,bqhd->rhd', global_slopes, query_heads).reshape(-1, model_width)
    global_value_grads = einsum_exact('bhqr,bqhd->rhd', global_rounded, grad_heads).reshape(-1, model_width)
    return (query_grads, jnp.concatenate([window_key_grads, window_value_grads], axis=-1), jnp.concatenate([global_key_grads, global_value_grads], axis=-1))

def reference(features, w_query, w_key, w_value, w_out, reg_pos, grad_out):
    band_rows, band_cols, model_width = features.shape
    flat_tokens = features.reshape(-1, model_width)
    queries = jnp.dot(flat_tokens, w_query, preferred_element_type=jnp.float32).astype(jnp.bfloat16)
    keys_all = jnp.dot(flat_tokens, w_key, preferred_element_type=jnp.float32).astype(jnp.bfloat16)
    values_all = jnp.dot(flat_tokens, w_value, preferred_element_type=jnp.float32).astype(jnp.bfloat16)
    key_value = jnp.concatenate([keys_all, values_all], axis=1)
    global_kv = jnp.take(key_value, reg_pos, axis=0)
    grad_attended = jnp.dot(grad_out.reshape(-1, model_width), w_out.T, preferred_element_type=jnp.float32).astype(jnp.bfloat16)
    spare_cells = 3 * BLK - (BLK + 2 * RAD)
    padded_kv = jnp.pad(key_value.reshape(band_rows, band_cols, 2 * model_width), ((RAD, RAD + spare_cells), (RAD, RAD + spare_cells), (0, 0)))
    query_cells = queries.reshape(band_rows, band_cols, model_width)
    grad_cells = grad_attended.reshape(band_rows, band_cols, model_width)
    col_blocks = band_cols // BLK
    row_blocks = band_rows // BLK
    group_blocks = math.gcd(col_blocks, 16)
    group_count = col_blocks // group_blocks
    zero_index = jnp.int32(0)

    def one_step(state_pair, step_index):
        frame_grads, global_grads = state_pair
        first_row = step_index // group_count * BLK
        first_col = step_index % group_count * (group_blocks * BLK)
        query_part = lax.dynamic_slice(query_cells, (first_row, first_col, zero_index), (BLK, group_blocks * BLK, model_width))
        grad_part = lax.dynamic_slice(grad_cells, (first_row, first_col, zero_index), (BLK, group_blocks * BLK, model_width))
        frame_part = lax.dynamic_slice(padded_kv, (first_row, first_col, zero_index), (3 * BLK, (group_blocks + 2) * BLK, 2 * model_width))
        window_kv = windows(frame_part, 1, group_blocks)
        window_mask = block_mask(axis_mask(first_row, band_rows, 1), axis_mask(first_col, band_cols, group_blocks))
        query_blocks = to_blocks(query_part, 1, group_blocks)
        grad_blocks = to_blocks(grad_part, 1, group_blocks)
        probs, attended = forward_block(query_blocks, window_kv, global_kv, window_mask)
        query_grads, window_grads, step_global = backward_block(query_blocks, window_kv, global_kv, probs, attended, grad_blocks)
        returned = windows_adjoint(window_grads, 1, group_blocks)
        current = lax.dynamic_slice(frame_grads, (first_row, first_col, zero_index), returned.shape)
        frame_grads = lax.dynamic_update_slice(frame_grads, current + returned, (first_row, first_col, zero_index))
        return ((frame_grads, global_grads + step_global), (from_blocks(attended, 1, group_blocks), from_blocks(query_grads, 1, group_blocks)))
    initial = (jnp.zeros(padded_kv.shape, jnp.float32), jnp.zeros(global_kv.shape, jnp.float32))
    (frame_grads, global_grads), (attended_parts, query_parts) = lax.scan(one_step, initial, jnp.arange(row_blocks * group_count, dtype=jnp.int32))

    def to_tokens(parts):
        shaped = parts.reshape(row_blocks, group_count, BLK, group_blocks * BLK, model_width).transpose(0, 2, 1, 3, 4)
        return shaped.reshape(band_rows * band_cols, model_width)
    attended_flat = to_tokens(attended_parts)
    query_flat = to_tokens(query_parts)
    layer_out = jnp.dot(attended_flat, w_out, preferred_element_type=jnp.float32).astype(jnp.bfloat16).reshape(features.shape)
    window_part = frame_grads[RAD:RAD + band_rows, RAD:RAD + band_cols].reshape(-1, 2 * model_width)
    kv_grads = window_part.at[reg_pos].add(global_grads).astype(jnp.bfloat16)
    grad_in = jnp.dot(query_flat, w_query.T, preferred_element_type=jnp.float32) + jnp.dot(kv_grads[:, :model_width], w_key.T, preferred_element_type=jnp.float32) + jnp.dot(kv_grads[:, model_width:], w_value.T, preferred_element_type=jnp.float32)
    grad_in = grad_in.astype(jnp.bfloat16).reshape(features.shape)
    return (layer_out, grad_in)
```

```python
import math

import jax
import jax.numpy as jnp
from jax import lax
from jax.sharding import PartitionSpec as P

HEADS = 16
KW = 13
RAD = 6


def with_halo(block, sides, width):
    for axis, dim in sides:
        count = lax.axis_size(axis)
        forward = [(i, i + 1) for i in range(count - 1)]
        backward = [(target, source) for source, target in forward]
        low = lax.ppermute(
            lax.slice_in_dim(block, block.shape[dim] - width, None, axis=dim), axis, forward
        )
        high = lax.ppermute(lax.slice_in_dim(block, 0, width, axis=dim), axis, backward)
        block = jnp.concatenate([low, block, high], axis=dim)
    return block


def from_behind(x, axis, by):
    size = lax.axis_size(axis)
    pairs = [(i, i + by) for i in range(size) if 0 <= i + by < size]
    return lax.ppermute(x, axis, pairs)


def axis_valid(first_cell, tile, extent):
    query_cell = first_cell + jnp.arange(tile, dtype=jnp.int32)[:, None]
    key_cell = first_cell - RAD + jnp.arange(tile + 2 * RAD, dtype=jnp.int32)[None, :]
    window_start = jnp.clip(query_cell - RAD, 0, extent - KW)
    return (key_cell >= window_start) & (key_cell <= window_start + KW - 1)


def einsum_wide(form, left, right):
    return jnp.einsum(form, left, right, preferred_element_type=jnp.float32)


def to_heads(x):
    count, width = x.shape
    return x.reshape(count, HEADS, width // HEADS).transpose(1, 0, 2)


def from_heads(x):
    heads, count, size = x.shape
    return x.transpose(1, 0, 2).reshape(count, heads * size)


def shards(features, w_query, w_key, w_value, w_out, reg_pos, grad_out):
    tile_rows, tile_cols, model_width = features.shape
    head_size = model_width // HEADS
    score_scale = 1.0 / math.sqrt(head_size)
    row_count = lax.axis_size("rows")
    col_count = lax.axis_size("cols")
    row_index = lax.axis_index("rows")
    col_index = lax.axis_index("cols")
    band_cols = tile_cols * col_count
    first_row = row_index * tile_rows
    first_col = col_index * tile_cols
    tokens = tile_rows * tile_cols
    frame_rows = tile_rows + 2 * RAD
    frame_cols = tile_cols + 2 * RAD

    flat_tokens = features.reshape(-1, model_width)
    queries = jnp.dot(flat_tokens, w_query, preferred_element_type=jnp.float32).astype(jnp.bfloat16)
    keys_local = jnp.dot(flat_tokens, w_key, preferred_element_type=jnp.float32).astype(
        jnp.bfloat16
    )
    values_local = jnp.dot(flat_tokens, w_value, preferred_element_type=jnp.float32).astype(
        jnp.bfloat16
    )
    key_value = jnp.concatenate([keys_local, values_local], axis=1)

    own_index = row_index * col_count + col_index
    own_place = lax.dynamic_index_in_dim(reg_pos, own_index, 0, keepdims=False)
    own_local = (own_place // band_cols - first_row) * tile_cols + (own_place % band_cols - first_col)
    own_kv = lax.dynamic_slice_in_dim(key_value, own_local, 1, 0)
    global_kv = lax.all_gather(own_kv, ("rows", "cols"), axis=0, tiled=True)

    framed = with_halo(
        key_value.reshape(tile_rows, tile_cols, 2 * model_width), (("rows", 0), ("cols", 1)), RAD
    ).reshape(frame_rows * frame_cols, 2 * model_width)
    all_kv = jnp.concatenate([framed, global_kv], axis=0)
    key_count = all_kv.shape[0]

    row_valid = axis_valid(first_row, tile_rows, tile_rows * row_count)
    col_valid = axis_valid(first_col, tile_cols, band_cols)
    window_mask = (row_valid[:, None, :, None] & col_valid[None, :, None, :]).reshape(
        tokens, frame_rows * frame_cols
    )
    full_mask = jnp.concatenate(
        [window_mask, jnp.ones((tokens, key_count - frame_rows * frame_cols), jnp.bool_)], axis=1
    )

    query_heads = to_heads(queries)
    key_heads = to_heads(all_kv[:, :model_width])
    value_heads = to_heads(all_kv[:, model_width:])

    scores = einsum_wide("hqd,hkd->hqk", query_heads, key_heads) * score_scale
    scores = jnp.where(full_mask[None], scores, -1e30)
    row_max = jnp.max(scores, axis=-1, keepdims=True)
    exps = jnp.exp(scores - row_max)
    denominator = jnp.sum(exps, axis=-1, keepdims=True)
    probs = exps / denominator
    rounded = probs.astype(jnp.bfloat16)
    attended_heads = einsum_wide("hqk,hkd->hqd", rounded, value_heads).astype(jnp.bfloat16)
    attended = from_heads(attended_heads)

    layer_out = (
        jnp.dot(attended, w_out, preferred_element_type=jnp.float32)
        .astype(jnp.bfloat16)
        .reshape(features.shape)
    )
    grad_attended = jnp.dot(
        grad_out.reshape(-1, model_width), w_out.T, preferred_element_type=jnp.float32
    ).astype(jnp.bfloat16)
    grad_heads = to_heads(grad_attended)

    delta = einsum_wide("hqd,hqd->hq", grad_heads, attended_heads)[..., None]
    dots = einsum_wide("hqd,hkd->hqk", grad_heads, value_heads)
    slopes = (probs * (dots - delta) * score_scale).astype(jnp.bfloat16)
    query_grads = from_heads(
        einsum_wide("hqk,hkd->hqd", slopes, key_heads).astype(jnp.bfloat16)
    )
    key_grads = from_heads(einsum_wide("hqk,hqd->hkd", slopes, query_heads))
    value_grads = from_heads(einsum_wide("hqk,hqd->hkd", rounded, grad_heads))
    kv_grads_all = jnp.concatenate([key_grads, value_grads], axis=1)

    global_grads = kv_grads_all[frame_rows * frame_cols :]
    own_grads = lax.psum_scatter(global_grads, ("rows", "cols"), scatter_dimension=0, tiled=True)

    frame_grads = kv_grads_all[: frame_rows * frame_cols].reshape(
        frame_rows, frame_cols, 2 * model_width
    )
    left_rim = frame_grads[:, :RAD]
    right_rim = frame_grads[:, tile_cols + RAD :]
    centre = frame_grads[:, RAD : tile_cols + RAD]
    from_right = from_behind(left_rim.astype(jnp.bfloat16), "cols", -1).astype(left_rim.dtype)
    from_left = from_behind(right_rim.astype(jnp.bfloat16), "cols", 1).astype(right_rim.dtype)
    centre = centre.at[:, tile_cols - RAD :].add(from_right).at[:, :RAD].add(from_left)
    upper_rim = centre[:RAD]
    lower_rim = centre[tile_rows + RAD :]
    middle = centre[RAD : tile_rows + RAD]
    from_below = from_behind(upper_rim.astype(jnp.bfloat16), "rows", -1).astype(upper_rim.dtype)
    from_above = from_behind(lower_rim.astype(jnp.bfloat16), "rows", 1).astype(lower_rim.dtype)
    middle = middle.at[tile_rows - RAD :].add(from_below).at[:RAD].add(from_above)
    middle = middle.reshape(tokens, 2 * model_width)
    own_row = lax.dynamic_slice_in_dim(middle, own_local, 1, 0) + own_grads
    kv_grads = lax.dynamic_update_slice_in_dim(middle, own_row, own_local, 0).astype(jnp.bfloat16)

    grad_in = (
        jnp.dot(query_grads, w_query.T, preferred_element_type=jnp.float32)
        + jnp.dot(kv_grads[:, :model_width], w_key.T, preferred_element_type=jnp.float32)
        + jnp.dot(kv_grads[:, model_width:], w_value.T, preferred_element_type=jnp.float32)
    )
    grad_in = grad_in.astype(jnp.bfloat16).reshape(features.shape)
    return (layer_out, grad_in)


def solution(mesh):
    placed = (P("rows", "cols", None), P(), P(), P(), P(), P(), P("rows", "cols", None))
    return jax.shard_map(
        shards,
        mesh=mesh,
        in_specs=placed,
        out_specs=(P("rows", "cols", None), P("rows", "cols", None)),
        check_vma=False,
    )
```

```python
import math

import jax
import jax.numpy as jnp
from jax import lax
from jax.sharding import PartitionSpec as P

HEADS = 16
KW = 13
RAD = 6


def shifted(x, axes, steps):
    sizes = [lax.axis_size(a) for a in axes]
    pairs = []
    for source in range(math.prod(sizes)):
        coords, rest = [], source
        for size in reversed(sizes):
            coords.append(rest % size)
            rest //= size
        coords = coords[::-1]
        target = [c + s for c, s in zip(coords, steps)]
        if all(0 <= t < size for t, size in zip(target, sizes)):
            linear = 0
            for t, size in zip(target, sizes):
                linear = linear * size + t
            pairs.append((source, linear))
    return lax.ppermute(x, tuple(axes), pairs)


def with_halo(tile, width):
    rows, cols = tile.shape[0], tile.shape[1]
    top, bottom = tile[rows - width :], tile[:width]
    both = ("rows", "cols")
    mid = jnp.concatenate(
        [
            shifted(tile[:, cols - width :], ("cols",), (1,)),
            tile,
            shifted(tile[:, :width], ("cols",), (-1,)),
        ],
        axis=1,
    )
    upper = jnp.concatenate(
        [
            shifted(top[:, cols - width :], both, (1, 1)),
            shifted(top, ("rows",), (1,)),
            shifted(top[:, :width], both, (1, -1)),
        ],
        axis=1,
    )
    lower = jnp.concatenate(
        [
            shifted(bottom[:, cols - width :], both, (-1, 1)),
            shifted(bottom, ("rows",), (-1,)),
            shifted(bottom[:, :width], both, (-1, -1)),
        ],
        axis=1,
    )
    return jnp.concatenate([upper, mid, lower], axis=0)


def fold_halo(frame, width):
    rows, cols = frame.shape[0] - 2 * width, frame.shape[1] - 2 * width
    both = ("rows", "cols")
    w = width

    def sent(piece, axes, steps):
        return shifted(piece.astype(jnp.bfloat16), axes, steps).astype(frame.dtype)

    def placed(piece, row_at, col_at):
        return jnp.pad(
            piece,
            ((row_at, rows - row_at - piece.shape[0]), (col_at, cols - col_at - piece.shape[1]), (0, 0)),
        )

    total = frame[w : w + rows, w : w + cols]
    total = total + placed(sent(frame[:w, w : w + cols], ("rows",), (-1,)), rows - w, 0)
    total = total + placed(sent(frame[w + rows :, w : w + cols], ("rows",), (1,)), 0, 0)
    total = total + placed(sent(frame[w : w + rows, :w], ("cols",), (-1,)), 0, cols - w)
    total = total + placed(sent(frame[w : w + rows, w + cols :], ("cols",), (1,)), 0, 0)
    total = total + placed(sent(frame[:w, :w], both, (-1, -1)), rows - w, cols - w)
    total = total + placed(sent(frame[:w, w + cols :], both, (-1, 1)), rows - w, 0)
    total = total + placed(sent(frame[w + rows :, :w], both, (1, -1)), 0, cols - w)
    total = total + placed(sent(frame[w + rows :, w + cols :], both, (1, 1)), 0, 0)
    return total


def tree_gather(x, axes):
    for axis in reversed(axes):
        size = lax.axis_size(axis)
        index = lax.axis_index(axis)
        step = 1
        while step < size:
            other = lax.ppermute(x, axis, [(i, i ^ step) for i in range(size)])
            low = (index // step) % 2 == 0
            x = jnp.where(low, jnp.concatenate([x, other]), jnp.concatenate([other, x]))
            step *= 2
    return x


def tree_reduce_scatter(x, axes):
    for axis in axes:
        size = lax.axis_size(axis)
        index = lax.axis_index(axis)
        x = x.reshape((size, -1) + x.shape[1:])
        step = size // 2
        while step >= 1:
            high = (index // step) % 2 == 1
            lower, upper = x[:step], x[step : 2 * step]
            keep = jnp.where(high, upper, lower)
            send = jnp.where(high, lower, upper)
            x = keep + lax.ppermute(send, axis, [(i, i ^ step) for i in range(size)])
            step //= 2
        x = x.reshape(x.shape[1:])
    return x


def power_of_two(n):
    return n & (n - 1) == 0


def axis_valid(first_cell, tile, extent):
    query_cell = first_cell + jnp.arange(tile, dtype=jnp.int32)[:, None]
    key_cell = first_cell - RAD + jnp.arange(tile + 2 * RAD, dtype=jnp.int32)[None, :]
    window_start = jnp.clip(query_cell - RAD, 0, extent - KW)
    return (key_cell >= window_start) & (key_cell <= window_start + KW - 1)


def einsum_wide(form, left, right):
    return jnp.einsum(form, left, right, preferred_element_type=jnp.float32)


def to_heads(x):
    count, width = x.shape
    return x.reshape(count, HEADS, width // HEADS).transpose(1, 0, 2)


def from_heads(x):
    heads, count, size = x.shape
    return x.transpose(1, 0, 2).reshape(count, heads * size)


def shards(features, w_query, w_key, w_value, w_out, reg_pos, grad_out):
    tile_rows, tile_cols, model_width = features.shape
    head_size = model_width // HEADS
    score_scale = 1.0 / math.sqrt(head_size)
    row_count = lax.axis_size("rows")
    col_count = lax.axis_size("cols")
    row_index = lax.axis_index("rows")
    col_index = lax.axis_index("cols")
    band_cols = tile_cols * col_count
    first_row = row_index * tile_rows
    first_col = col_index * tile_cols
    tokens = tile_rows * tile_cols
    frame_rows = tile_rows + 2 * RAD
    frame_cols = tile_cols + 2 * RAD

    flat_tokens = features.reshape(-1, model_width)
    queries = jnp.dot(flat_tokens, w_query, preferred_element_type=jnp.float32).astype(jnp.bfloat16)
    keys_local = jnp.dot(flat_tokens, w_key, preferred_element_type=jnp.float32).astype(
        jnp.bfloat16
    )
    values_local = jnp.dot(flat_tokens, w_value, preferred_element_type=jnp.float32).astype(
        jnp.bfloat16
    )
    key_value = jnp.concatenate([keys_local, values_local], axis=1)

    own_index = row_index * col_count + col_index
    own_place = lax.dynamic_index_in_dim(reg_pos, own_index, 0, keepdims=False)
    own_local = (own_place // band_cols - first_row) * tile_cols + (own_place % band_cols - first_col)
    own_kv = lax.dynamic_slice_in_dim(key_value, own_local, 1, 0)
    if power_of_two(row_count) and power_of_two(col_count):
        global_kv = tree_gather(own_kv, ("rows", "cols"))
    else:
        global_kv = lax.all_gather(own_kv, ("rows", "cols"), axis=0, tiled=True)

    framed = with_halo(key_value.reshape(tile_rows, tile_cols, 2 * model_width), RAD).reshape(
        frame_rows * frame_cols, 2 * model_width
    )
    all_kv = jnp.concatenate([framed, global_kv], axis=0)
    key_count = all_kv.shape[0]

    row_valid = axis_valid(first_row, tile_rows, tile_rows * row_count)
    col_valid = axis_valid(first_col, tile_cols, band_cols)
    window_mask = (row_valid[:, None, :, None] & col_valid[None, :, None, :]).reshape(
        tokens, frame_rows * frame_cols
    )
    full_mask = jnp.concatenate(
        [window_mask, jnp.ones((tokens, key_count - frame_rows * frame_cols), jnp.bool_)], axis=1
    )

    query_heads = to_heads(queries)
    key_heads = to_heads(all_kv[:, :model_width])
    value_heads = to_heads(all_kv[:, model_width:])

    scores = einsum_wide("hqd,hkd->hqk", query_heads, key_heads) * score_scale
    scores = jnp.where(full_mask[None], scores, -1e30)
    row_max = jnp.max(scores, axis=-1, keepdims=True)
    exps = jnp.exp(scores - row_max)
    denominator = jnp.sum(exps, axis=-1, keepdims=True)
    probs = exps / denominator
    rounded = probs.astype(jnp.bfloat16)
    attended_heads = einsum_wide("hqk,hkd->hqd", rounded, value_heads).astype(jnp.bfloat16)
    attended = from_heads(attended_heads)

    layer_out = (
        jnp.dot(attended, w_out, preferred_element_type=jnp.float32)
        .astype(jnp.bfloat16)
        .reshape(features.shape)
    )
    grad_attended = jnp.dot(
        grad_out.reshape(-1, model_width), w_out.T, preferred_element_type=jnp.float32
    ).astype(jnp.bfloat16)
    grad_heads = to_heads(grad_attended)

    delta = einsum_wide("hqd,hqd->hq", grad_heads, attended_heads)[..., None]
    dots = einsum_wide("hqd,hkd->hqk", grad_heads, value_heads)
    slopes = (probs * (dots - delta) * score_scale).astype(jnp.bfloat16)
    query_grads = from_heads(
        einsum_wide("hqk,hkd->hqd", slopes, key_heads).astype(jnp.bfloat16)
    )
    key_grads = from_heads(einsum_wide("hqk,hqd->hkd", slopes, query_heads))
    value_grads = from_heads(einsum_wide("hqk,hqd->hkd", rounded, grad_heads))
    kv_grads_all = jnp.concatenate([key_grads, value_grads], axis=1)

    global_grads = kv_grads_all[frame_rows * frame_cols :]
    if power_of_two(row_count) and power_of_two(col_count):
        own_grads = tree_reduce_scatter(global_grads, ("rows", "cols"))
    else:
        own_grads = lax.psum_scatter(
            global_grads, ("rows", "cols"), scatter_dimension=0, tiled=True
        )

    frame_grads = kv_grads_all[: frame_rows * frame_cols].reshape(
        frame_rows, frame_cols, 2 * model_width
    )
    middle = fold_halo(frame_grads, RAD)
    middle = middle.reshape(tokens, 2 * model_width)
    own_row = lax.dynamic_slice_in_dim(middle, own_local, 1, 0) + own_grads
    kv_grads = lax.dynamic_update_slice_in_dim(middle, own_row, own_local, 0).astype(jnp.bfloat16)

    grad_in = (
        jnp.dot(query_grads, w_query.T, preferred_element_type=jnp.float32)
        + jnp.dot(kv_grads[:, :model_width], w_key.T, preferred_element_type=jnp.float32)
        + jnp.dot(kv_grads[:, model_width:], w_value.T, preferred_element_type=jnp.float32)
    )
    grad_in = grad_in.astype(jnp.bfloat16).reshape(features.shape)
    return (layer_out, grad_in)


def solution(mesh):
    placed = (P("rows", "cols", None), P(), P(), P(), P(), P(), P("rows", "cols", None))
    return jax.shard_map(
        shards,
        mesh=mesh,
        in_specs=placed,
        out_specs=(P("rows", "cols", None), P("rows", "cols", None)),
        check_vma=False,
    )
```

```python
import math

import jax
import jax.numpy as jnp
from jax import lax
from jax.experimental import pallas as pl
from jax.sharding import PartitionSpec as P

HEADS = 16
KW = 13
RAD = 6


def shifted(x, axes, steps):
    sizes = [lax.axis_size(a) for a in axes]
    pairs = []
    for source in range(math.prod(sizes)):
        coords, rest = [], source
        for size in reversed(sizes):
            coords.append(rest % size)
            rest //= size
        coords = coords[::-1]
        target = [c + s for c, s in zip(coords, steps)]
        if all(0 <= t < size for t, size in zip(target, sizes)):
            linear = 0
            for t, size in zip(target, sizes):
                linear = linear * size + t
            pairs.append((source, linear))
    return lax.ppermute(x, tuple(axes), pairs)


def with_halo(tile, width):
    rows, cols = tile.shape[0], tile.shape[1]
    top, bottom = tile[rows - width :], tile[:width]
    both = ("rows", "cols")
    mid = jnp.concatenate(
        [
            shifted(tile[:, cols - width :], ("cols",), (1,)),
            tile,
            shifted(tile[:, :width], ("cols",), (-1,)),
        ],
        axis=1,
    )
    upper = jnp.concatenate(
        [
            shifted(top[:, cols - width :], both, (1, 1)),
            shifted(top, ("rows",), (1,)),
            shifted(top[:, :width], both, (1, -1)),
        ],
        axis=1,
    )
    lower = jnp.concatenate(
        [
            shifted(bottom[:, cols - width :], both, (-1, 1)),
            shifted(bottom, ("rows",), (-1,)),
            shifted(bottom[:, :width], both, (-1, -1)),
        ],
        axis=1,
    )
    return jnp.concatenate([upper, mid, lower], axis=0)


def fold_halo(frame, width):
    rows, cols = frame.shape[0] - 2 * width, frame.shape[1] - 2 * width
    both = ("rows", "cols")
    w = width

    def sent(piece, axes, steps):
        return shifted(piece.astype(jnp.bfloat16), axes, steps).astype(frame.dtype)

    def placed(piece, row_at, col_at):
        return jnp.pad(
            piece,
            ((row_at, rows - row_at - piece.shape[0]), (col_at, cols - col_at - piece.shape[1]), (0, 0)),
        )

    total = frame[w : w + rows, w : w + cols]
    total = total + placed(sent(frame[:w, w : w + cols], ("rows",), (-1,)), rows - w, 0)
    total = total + placed(sent(frame[w + rows :, w : w + cols], ("rows",), (1,)), 0, 0)
    total = total + placed(sent(frame[w : w + rows, :w], ("cols",), (-1,)), 0, cols - w)
    total = total + placed(sent(frame[w : w + rows, w + cols :], ("cols",), (1,)), 0, 0)
    total = total + placed(sent(frame[:w, :w], both, (-1, -1)), rows - w, cols - w)
    total = total + placed(sent(frame[:w, w + cols :], both, (-1, 1)), rows - w, 0)
    total = total + placed(sent(frame[w + rows :, :w], both, (1, -1)), 0, cols - w)
    total = total + placed(sent(frame[w + rows :, w + cols :], both, (1, 1)), 0, 0)
    return total


def tree_gather(x, axes):
    for axis in reversed(axes):
        size = lax.axis_size(axis)
        index = lax.axis_index(axis)
        step = 1
        while step < size:
            other = lax.ppermute(x, axis, [(i, i ^ step) for i in range(size)])
            low = (index // step) % 2 == 0
            x = jnp.where(low, jnp.concatenate([x, other]), jnp.concatenate([other, x]))
            step *= 2
    return x


def tree_reduce_scatter(x, axes):
    for axis in axes:
        size = lax.axis_size(axis)
        index = lax.axis_index(axis)
        x = x.reshape((size, -1) + x.shape[1:])
        step = size // 2
        while step >= 1:
            high = (index // step) % 2 == 1
            lower, upper = x[:step], x[step : 2 * step]
            keep = jnp.where(high, upper, lower)
            send = jnp.where(high, lower, upper)
            x = keep + lax.ppermute(send, axis, [(i, i ^ step) for i in range(size)])
            step //= 2
        x = x.reshape(x.shape[1:])
    return x


def power_of_two(n):
    return n & (n - 1) == 0


def axis_valid(first_cell, tile, extent):
    query_cell = first_cell + jnp.arange(tile, dtype=jnp.int32)[:, None]
    key_cell = first_cell - RAD + jnp.arange(tile + 2 * RAD, dtype=jnp.int32)[None, :]
    window_start = jnp.clip(query_cell - RAD, 0, extent - KW)
    return (key_cell >= window_start) & (key_cell <= window_start + KW - 1)


def attention_kernel(q_ref, k_ref, v_ref, g_ref, mask_ref, o_ref, dq_ref, dk_ref, dv_ref):
    head_size = q_ref.shape[1] // 2
    score_scale = 1.0 / math.sqrt(head_size)
    q = q_ref[...]
    k = k_ref[...]
    v = v_ref[...]
    g = g_ref[...]
    keep = mask_ref[...] > 0
    lane_head = lax.broadcasted_iota(jnp.int32, q.shape, 1) // head_size
    lane_head_keys = lax.broadcasted_iota(jnp.int32, k.shape, 1) // head_size
    rows = (((1,), (1,)), ((), ()))
    cols = (((0,), (0,)), ((), ()))
    out = jnp.zeros(q.shape, jnp.float32)
    dq = jnp.zeros(q.shape, jnp.float32)
    dk = jnp.zeros(k.shape, jnp.float32)
    dv = jnp.zeros(k.shape, jnp.float32)
    for head in range(2):
        mine = lane_head == head
        mine_keys = lane_head_keys == head
        q_head = jnp.where(mine, q, jnp.zeros_like(q))
        g_head = jnp.where(mine, g, jnp.zeros_like(g))
        scores = lax.dot_general(q_head, k, rows, preferred_element_type=jnp.float32) * score_scale
        scores = jnp.where(keep, scores, -1e30)
        row_max = jnp.max(scores, axis=1, keepdims=True)
        exps = jnp.exp(scores - row_max)
        probs = exps / jnp.sum(exps, axis=1, keepdims=True)
        rounded = probs.astype(jnp.bfloat16)
        attended = jnp.dot(rounded, v, preferred_element_type=jnp.float32)
        attended = attended.astype(jnp.bfloat16).astype(jnp.float32)
        out = jnp.where(mine, attended, out)
        delta = jnp.sum(
            jnp.where(mine, g.astype(jnp.float32) * attended, 0.0), axis=1, keepdims=True
        )
        dots = lax.dot_general(g_head, v, rows, preferred_element_type=jnp.float32)
        slopes = (probs * (dots - delta) * score_scale).astype(jnp.bfloat16)
        dq = jnp.where(mine, jnp.dot(slopes, k, preferred_element_type=jnp.float32), dq)
        dk = jnp.where(
            mine_keys, lax.dot_general(slopes, q, cols, preferred_element_type=jnp.float32), dk
        )
        dv = jnp.where(
            mine_keys, lax.dot_general(rounded, g, cols, preferred_element_type=jnp.float32), dv
        )
    o_ref[...] = out.astype(o_ref.dtype)
    dq_ref[...] = dq.astype(dq_ref.dtype)
    dk_ref[...] = dk
    dv_ref[...] = dv


def attention(queries, all_kv, grad_attended, keep):
    tokens, model_width = queries.shape
    key_count = all_kv.shape[0]
    lanes = 2 * (model_width // HEADS)
    steps = model_width // lanes
    token_block = pl.BlockSpec((tokens, lanes), lambda i: (0, i))
    key_block = pl.BlockSpec((key_count, lanes), lambda i: (0, i))
    value_block = pl.BlockSpec((key_count, lanes), lambda i: (0, i + steps))
    mask_block = pl.BlockSpec((tokens, key_count), lambda i: (0, 0))
    flops = 2 * 2 * 6 * tokens * key_count * model_width
    moved = 2 * (3 * tokens * model_width + 2 * key_count * model_width) + 4 * (
        tokens * key_count + 2 * key_count * model_width
    )
    return pl.pallas_call(
        attention_kernel,
        grid=(steps,),
        in_specs=[token_block, key_block, value_block, token_block, mask_block],
        out_specs=[token_block, token_block, key_block, key_block],
        out_shape=[
            jax.ShapeDtypeStruct((tokens, model_width), jnp.bfloat16),
            jax.ShapeDtypeStruct((tokens, model_width), jnp.bfloat16),
            jax.ShapeDtypeStruct((key_count, model_width), jnp.float32),
            jax.ShapeDtypeStruct((key_count, model_width), jnp.float32),
        ],
        cost_estimate=pl.CostEstimate(
            flops=flops, transcendentals=HEADS * tokens * key_count, bytes_accessed=moved
        ),
    )(queries, all_kv, all_kv, grad_attended, keep)


def shards(features, w_query, w_key, w_value, w_out, reg_pos, grad_out):
    tile_rows, tile_cols, model_width = features.shape
    head_size = model_width // HEADS
    score_scale = 1.0 / math.sqrt(head_size)
    row_count = lax.axis_size("rows")
    col_count = lax.axis_size("cols")
    row_index = lax.axis_index("rows")
    col_index = lax.axis_index("cols")
    band_cols = tile_cols * col_count
    first_row = row_index * tile_rows
    first_col = col_index * tile_cols
    tokens = tile_rows * tile_cols
    frame_rows = tile_rows + 2 * RAD
    frame_cols = tile_cols + 2 * RAD

    flat_tokens = features.reshape(-1, model_width)
    queries = jnp.dot(flat_tokens, w_query, preferred_element_type=jnp.float32).astype(jnp.bfloat16)
    keys_local = jnp.dot(flat_tokens, w_key, preferred_element_type=jnp.float32).astype(
        jnp.bfloat16
    )
    values_local = jnp.dot(flat_tokens, w_value, preferred_element_type=jnp.float32).astype(
        jnp.bfloat16
    )
    key_value = jnp.concatenate([keys_local, values_local], axis=1)

    own_index = row_index * col_count + col_index
    own_place = lax.dynamic_index_in_dim(reg_pos, own_index, 0, keepdims=False)
    own_local = (own_place // band_cols - first_row) * tile_cols + (own_place % band_cols - first_col)
    own_kv = lax.dynamic_slice_in_dim(key_value, own_local, 1, 0)
    if power_of_two(row_count) and power_of_two(col_count):
        global_kv = tree_gather(own_kv, ("rows", "cols"))
    else:
        global_kv = lax.all_gather(own_kv, ("rows", "cols"), axis=0, tiled=True)

    framed = with_halo(key_value.reshape(tile_rows, tile_cols, 2 * model_width), RAD).reshape(
        frame_rows * frame_cols, 2 * model_width
    )
    frame_cells = frame_rows * frame_cols
    used = frame_cells + global_kv.shape[0]
    key_count = -(-used // 128) * 128
    all_kv = jnp.concatenate(
        [framed, global_kv, jnp.zeros((key_count - used, 2 * model_width), framed.dtype)], axis=0
    )

    row_valid = axis_valid(first_row, tile_rows, tile_rows * row_count)
    col_valid = axis_valid(first_col, tile_cols, band_cols)
    window_mask = (row_valid[:, None, :, None] & col_valid[None, :, None, :]).reshape(
        tokens, frame_cells
    )
    keep = jnp.concatenate(
        [
            window_mask.astype(jnp.float32),
            jnp.ones((tokens, used - frame_cells), jnp.float32),
            jnp.zeros((tokens, key_count - used), jnp.float32),
        ],
        axis=1,
    )

    grad_attended = jnp.dot(
        grad_out.reshape(-1, model_width), w_out.T, preferred_element_type=jnp.float32
    ).astype(jnp.bfloat16)
    attended, query_grads, key_grads, value_grads = attention(
        queries, all_kv, grad_attended, keep
    )
    layer_out = (
        jnp.dot(attended, w_out, preferred_element_type=jnp.float32)
        .astype(jnp.bfloat16)
        .reshape(features.shape)
    )

    global_grads = jnp.concatenate(
        [key_grads[frame_cells:used], value_grads[frame_cells:used]], axis=1
    )
    if power_of_two(row_count) and power_of_two(col_count):
        own_grads = tree_reduce_scatter(global_grads, ("rows", "cols"))
    else:
        own_grads = lax.psum_scatter(
            global_grads, ("rows", "cols"), scatter_dimension=0, tiled=True
        )

    middle = jnp.concatenate(
        [
            fold_halo(key_grads[:frame_cells].reshape(frame_rows, frame_cols, model_width), RAD),
            fold_halo(value_grads[:frame_cells].reshape(frame_rows, frame_cols, model_width), RAD),
        ],
        axis=2,
    ).reshape(tokens, 2 * model_width)
    own_row = lax.dynamic_slice_in_dim(middle, own_local, 1, 0) + own_grads
    kv_grads = lax.dynamic_update_slice_in_dim(middle, own_row, own_local, 0).astype(jnp.bfloat16)

    grad_in = (
        jnp.dot(query_grads, w_query.T, preferred_element_type=jnp.float32)
        + jnp.dot(kv_grads[:, :model_width], w_key.T, preferred_element_type=jnp.float32)
        + jnp.dot(kv_grads[:, model_width:], w_value.T, preferred_element_type=jnp.float32)
    )
    grad_in = grad_in.astype(jnp.bfloat16).reshape(features.shape)
    return (layer_out, grad_in)


def solution(mesh):
    placed = (P("rows", "cols", None), P(), P(), P(), P(), P(), P("rows", "cols", None))
    return jax.shard_map(
        shards,
        mesh=mesh,
        in_specs=placed,
        out_specs=(P("rows", "cols", None), P("rows", "cols", None)),
        check_vma=False,
    )
```

```python
import math

import jax
import jax.numpy as jnp
import numpy as np
from jax import lax
from jax.experimental import pallas as pl
from jax.sharding import PartitionSpec as P

HEADS = 16
KW = 13
RAD = 6


def bits(n):
    return n.bit_length() - 1


def device_bit(position):
    col_bits = bits(lax.axis_size("cols"))
    if position < col_bits:
        return "cols", position
    return "rows", position - col_bits


def own_bit(position):
    axis, bit = device_bit(position)
    return (lax.axis_index(axis) >> bit) % 2


def partner(x, position):
    axis, bit = device_bit(position)
    size = lax.axis_size(axis)
    return lax.ppermute(x, axis, [(i, i ^ (1 << bit)) for i in range(size)])


def exchange(to_lower, to_higher, axis, rider=None, rider_dim=0):
    size = lax.axis_size(axis)
    even = lax.axis_index(axis) % 2 == 0
    first = jnp.where(even, to_higher, to_lower)
    length = first.shape[rider_dim]
    if rider is not None:
        first = jnp.concatenate([first, rider], axis=rider_dim)
    got_first = lax.ppermute(first, axis, [(i, i ^ 1) for i in range(size)])
    links = [(i, i + 1) for i in range(1, size - 1, 2)] + [(i, i - 1) for i in range(2, size, 2)]
    got_second = lax.ppermute(jnp.where(even, to_lower, to_higher), axis, links)
    rider_got = None
    if rider is not None:
        rider_got = lax.slice_in_dim(got_first, length, None, axis=rider_dim)
        got_first = lax.slice_in_dim(got_first, 0, length, axis=rider_dim)
    from_lower = jnp.where(even, got_second, got_first)
    from_higher = jnp.where(even, got_first, got_second)
    return from_lower, from_higher, rider_got


def gather_step(x, other, position):
    low = own_bit(position) == 0
    return jnp.where(low, jnp.concatenate([x, other]), jnp.concatenate([other, x]))


def gather_order(order, count):
    where = np.zeros(count, np.int32)
    for l in range(count):
        where[l] = sum(((l >> bit) & 1) << step for step, bit in enumerate(order))
    return where


def scatter_split(x, order_left, position):
    axis = 1 + order_left.index(position)
    high = own_bit(position) == 1
    lower = lax.index_in_dim(x, 0, axis, keepdims=False)
    upper = lax.index_in_dim(x, 1, axis, keepdims=False)
    order_left.remove(position)
    return jnp.where(high, upper, lower), jnp.where(high, lower, upper)


def attention_kernel(q_ref, k_ref, v_ref, g_ref, mask_ref, o_ref, dq_ref, dkv_ref):
    head_size = q_ref.shape[1] // 2
    score_scale = 1.0 / math.sqrt(head_size)
    q = q_ref[...]
    k = k_ref[...]
    v = v_ref[...]
    g = g_ref[...]
    keep = mask_ref[...] > 0
    lane_head = lax.broadcasted_iota(jnp.int32, q.shape, 1) // head_size
    lane_head_keys = lax.broadcasted_iota(jnp.int32, k.shape, 1) // head_size
    rows = (((1,), (1,)), ((), ()))
    cols = (((0,), (0,)), ((), ()))
    out = jnp.zeros(q.shape, jnp.float32)
    dq = jnp.zeros(q.shape, jnp.float32)
    dk = jnp.zeros(k.shape, jnp.float32)
    dv = jnp.zeros(k.shape, jnp.float32)
    for head in range(2):
        mine = lane_head == head
        mine_keys = lane_head_keys == head
        q_head = jnp.where(mine, q, jnp.zeros_like(q))
        g_head = jnp.where(mine, g, jnp.zeros_like(g))
        scores = lax.dot_general(q_head, k, rows, preferred_element_type=jnp.float32) * score_scale
        scores = jnp.where(keep, scores, -1e30)
        row_max = jnp.max(scores, axis=1, keepdims=True)
        exps = jnp.exp(scores - row_max)
        probs = exps / jnp.sum(exps, axis=1, keepdims=True)
        rounded = probs.astype(jnp.bfloat16)
        attended = jnp.dot(rounded, v, preferred_element_type=jnp.float32)
        attended = attended.astype(jnp.bfloat16).astype(jnp.float32)
        out = jnp.where(mine, attended, out)
        delta = jnp.sum(
            jnp.where(mine, g.astype(jnp.float32) * attended, 0.0), axis=1, keepdims=True
        )
        dots = lax.dot_general(g_head, v, rows, preferred_element_type=jnp.float32)
        slopes = (probs * (dots - delta) * score_scale).astype(jnp.bfloat16)
        dq = jnp.where(mine, jnp.dot(slopes, k, preferred_element_type=jnp.float32), dq)
        dk = jnp.where(
            mine_keys, lax.dot_general(slopes, q, cols, preferred_element_type=jnp.float32), dk
        )
        dv = jnp.where(
            mine_keys, lax.dot_general(rounded, g, cols, preferred_element_type=jnp.float32), dv
        )
    o_ref[...] = out.astype(o_ref.dtype)
    dq_ref[...] = dq.astype(dq_ref.dtype)
    dkv_ref[0] = dk
    dkv_ref[1] = dv


def attention(queries, all_kv, grad_attended, keep):
    tokens, model_width = queries.shape
    key_count = all_kv.shape[0]
    lanes = 2 * (model_width // HEADS)
    steps = model_width // lanes
    token_block = pl.BlockSpec((tokens, lanes), lambda i: (0, i))
    key_block = pl.BlockSpec((key_count, lanes), lambda i: (0, i))
    value_block = pl.BlockSpec((key_count, lanes), lambda i: (0, i + steps))
    mask_block = pl.BlockSpec((tokens, key_count), lambda i: (0, 0))
    grads_block = pl.BlockSpec((2, key_count, lanes), lambda i: (0, 0, i))
    flops = 2 * 2 * 6 * tokens * key_count * model_width
    moved = 2 * (3 * tokens * model_width + 2 * key_count * model_width) + 4 * (
        tokens * key_count + 2 * key_count * model_width
    )
    return pl.pallas_call(
        attention_kernel,
        grid=(steps,),
        in_specs=[token_block, key_block, value_block, token_block, mask_block],
        out_specs=[token_block, token_block, grads_block],
        out_shape=[
            jax.ShapeDtypeStruct((tokens, model_width), jnp.bfloat16),
            jax.ShapeDtypeStruct((tokens, model_width), jnp.bfloat16),
            jax.ShapeDtypeStruct((2, key_count, model_width), jnp.float32),
        ],
        cost_estimate=pl.CostEstimate(
            flops=flops, transcendentals=HEADS * tokens * key_count, bytes_accessed=moved
        ),
    )(queries, all_kv, all_kv, grad_attended, keep)


def shards(features, w_query, w_key, w_value, w_out, reg_pos, grad_out):
    tile_rows, tile_cols, model_width = features.shape
    row_count = lax.axis_size("rows")
    col_count = lax.axis_size("cols")
    row_index = lax.axis_index("rows")
    col_index = lax.axis_index("cols")
    band_rows = tile_rows * row_count
    band_cols = tile_cols * col_count
    first_row = row_index * tile_rows
    first_col = col_index * tile_cols
    tokens = tile_rows * tile_cols
    device_count = row_count * col_count
    col_bits = bits(col_count)
    all_bits = col_bits + bits(row_count)
    ext_rows = tile_rows + 2 * RAD
    width = 2 * model_width

    flat_tokens = features.reshape(-1, model_width)
    queries = jnp.dot(flat_tokens, w_query, preferred_element_type=jnp.float32).astype(jnp.bfloat16)
    keys_local = jnp.dot(flat_tokens, w_key, preferred_element_type=jnp.float32).astype(
        jnp.bfloat16
    )
    values_local = jnp.dot(flat_tokens, w_value, preferred_element_type=jnp.float32).astype(
        jnp.bfloat16
    )
    key_value = jnp.concatenate([keys_local, values_local], axis=1)
    tile_kv = key_value.reshape(tile_rows, tile_cols, width)

    own_index = row_index * col_count + col_index
    own_place = lax.dynamic_index_in_dim(reg_pos, own_index, 0, keepdims=False)
    own_local = (own_place // band_cols - first_row) * tile_cols + (own_place % band_cols - first_col)
    gathered = lax.dynamic_slice_in_dim(key_value, own_local, 1, 0)
    order = [col_bits, 0] + list(range(1, col_bits)) + list(range(col_bits + 1, all_bits))

    from_above, from_below, got = exchange(
        tile_kv[:RAD].reshape(-1, width),
        tile_kv[tile_rows - RAD :].reshape(-1, width),
        "rows",
        gathered,
    )
    gathered = gather_step(gathered, got, order[0])
    extended = jnp.concatenate(
        [
            from_above.reshape(RAD, tile_cols, width),
            tile_kv,
            from_below.reshape(RAD, tile_cols, width),
        ],
        axis=0,
    )
    from_left, from_right, got = exchange(
        extended[:, :RAD].reshape(-1, width),
        extended[:, tile_cols - RAD :].reshape(-1, width),
        "cols",
        gathered,
    )
    gathered = gather_step(gathered, got, order[1])
    for position in order[2:]:
        gathered = gather_step(gathered, partner(gathered, position), position)
    global_kv = jnp.take(gathered, jnp.asarray(gather_order(order, device_count)), axis=0)

    own_keys = ext_rows * tile_cols
    strip_keys = ext_rows * RAD
    frame_keys = own_keys + 2 * strip_keys
    used = frame_keys + device_count
    key_count = -(-used // 128) * 128
    all_kv = jnp.concatenate(
        [
            extended.reshape(own_keys, width),
            from_left,
            from_right,
            global_kv,
            jnp.zeros((key_count - used, width), key_value.dtype),
        ],
        axis=0,
    )

    a, b = np.meshgrid(np.arange(ext_rows), np.arange(tile_cols), indexing="ij")
    s, t = np.meshgrid(np.arange(ext_rows), np.arange(RAD), indexing="ij")
    key_rows = np.zeros(key_count, np.int32)
    key_cols = np.zeros(key_count, np.int32)
    key_rows[:frame_keys] = np.concatenate([a.reshape(-1), s.reshape(-1), s.reshape(-1)])
    key_cols[:frame_keys] = np.concatenate(
        [b.reshape(-1) + RAD, t.reshape(-1), t.reshape(-1) + RAD + tile_cols]
    )
    kind = np.full(key_count, 2, np.int32)
    kind[:frame_keys] = 0
    kind[frame_keys:used] = 1

    query_rows = first_row + jnp.repeat(jnp.arange(tile_rows, dtype=jnp.int32), tile_cols)
    query_cols = first_col + jnp.tile(jnp.arange(tile_cols, dtype=jnp.int32), tile_rows)
    start_rows = jnp.clip(query_rows - RAD, 0, band_rows - KW)[:, None]
    start_cols = jnp.clip(query_cols - RAD, 0, band_cols - KW)[:, None]
    cell_rows = (first_row - RAD + jnp.asarray(key_rows))[None, :]
    cell_cols = (first_col - RAD + jnp.asarray(key_cols))[None, :]
    inside = (
        (cell_rows >= start_rows)
        & (cell_rows < start_rows + KW)
        & (cell_cols >= start_cols)
        & (cell_cols < start_cols + KW)
    )
    key_kind = jnp.asarray(kind)[None, :]
    keep = ((inside & (key_kind == 0)) | (key_kind == 1)).astype(jnp.float32)

    grad_attended = jnp.dot(
        grad_out.reshape(-1, model_width), w_out.T, preferred_element_type=jnp.float32
    ).astype(jnp.bfloat16)
    attended, query_grads, kv_grads_all = attention(queries, all_kv, grad_attended, keep)
    layer_out = (
        jnp.dot(attended, w_out, preferred_element_type=jnp.float32)
        .astype(jnp.bfloat16)
        .reshape(features.shape)
    )

    scatter = kv_grads_all[:, frame_keys:used].reshape((2,) + (2,) * all_bits + (model_width,))
    left = list(range(all_bits - 1, -1, -1))
    back_order = [0, col_bits] + list(range(1, col_bits)) + list(range(col_bits + 1, all_bits))

    keep_part, send_part = scatter_split(scatter, left, back_order[0])
    strip_shape = (2, ext_rows, RAD, model_width)
    from_left, from_right, got = exchange(
        kv_grads_all[:, own_keys : own_keys + strip_keys],
        kv_grads_all[:, own_keys + strip_keys : frame_keys],
        "cols",
        send_part.reshape(2, -1, model_width),
        rider_dim=1,
    )
    scatter = keep_part + got.reshape(keep_part.shape)
    extended_grads = kv_grads_all[:, :own_keys].reshape(2, ext_rows, tile_cols, model_width)
    extended_grads = extended_grads + jnp.pad(
        from_left.reshape(strip_shape), ((0, 0), (0, 0), (0, tile_cols - RAD), (0, 0))
    )
    extended_grads = extended_grads + jnp.pad(
        from_right.reshape(strip_shape), ((0, 0), (0, 0), (tile_cols - RAD, 0), (0, 0))
    )
    keep_part, send_part = scatter_split(scatter, left, back_order[1])
    band_shape = (2, RAD, tile_cols, model_width)
    from_above, from_below, got = exchange(
        extended_grads[:, :RAD].reshape(2, -1, model_width),
        extended_grads[:, RAD + tile_rows :].reshape(2, -1, model_width),
        "rows",
        send_part.reshape(2, -1, model_width),
        rider_dim=1,
    )
    scatter = keep_part + got.reshape(keep_part.shape)
    centre = extended_grads[:, RAD : RAD + tile_rows]
    centre = centre + jnp.pad(
        from_above.reshape(band_shape), ((0, 0), (0, tile_rows - RAD), (0, 0), (0, 0))
    )
    centre = centre + jnp.pad(
        from_below.reshape(band_shape), ((0, 0), (tile_rows - RAD, 0), (0, 0), (0, 0))
    )
    for position in back_order[2:]:
        keep_part, send_part = scatter_split(scatter, left, position)
        scatter = keep_part + partner(send_part, position)
    own_grads = scatter.reshape(2, 1, model_width)

    middle = centre.reshape(2, tokens, model_width)
    own_row = lax.dynamic_slice_in_dim(middle, own_local, 1, 1) + own_grads
    kv_grads = lax.dynamic_update_slice_in_dim(middle, own_row, own_local, 1).astype(jnp.bfloat16)

    grad_in = (
        jnp.dot(query_grads, w_query.T, preferred_element_type=jnp.float32)
        + jnp.dot(kv_grads[0], w_key.T, preferred_element_type=jnp.float32)
        + jnp.dot(kv_grads[1], w_value.T, preferred_element_type=jnp.float32)
    )
    grad_in = grad_in.astype(jnp.bfloat16).reshape(features.shape)
    return (layer_out, grad_in)


def solution(mesh):
    placed = (P("rows", "cols", None), P(), P(), P(), P(), P(), P("rows", "cols", None))
    return jax.shard_map(
        shards,
        mesh=mesh,
        in_specs=placed,
        out_specs=(P("rows", "cols", None), P("rows", "cols", None)),
        check_vma=False,
    )
```

```python
import math

import jax
import jax.numpy as jnp
import numpy as np
from jax import lax
from jax.experimental import pallas as pl
from jax.sharding import PartitionSpec as P

HEADS = 16
KW = 13
RAD = 6


def bits(n):
    return n.bit_length() - 1


def device_bit(position):
    col_bits = bits(lax.axis_size("cols"))
    if position < col_bits:
        return "cols", position
    return "rows", position - col_bits


def own_bit(position):
    axis, bit = device_bit(position)
    return (lax.axis_index(axis) >> bit) % 2


def partner(x, position):
    axis, bit = device_bit(position)
    size = lax.axis_size(axis)
    return lax.ppermute(x, axis, [(i, i ^ (1 << bit)) for i in range(size)])


def exchange(to_lower, to_higher, axis, rider=None, rider_dim=0):
    size = lax.axis_size(axis)
    even = lax.axis_index(axis) % 2 == 0
    first = jnp.where(even, to_higher, to_lower)
    length = first.shape[rider_dim]
    if rider is not None:
        first = jnp.concatenate([first, rider], axis=rider_dim)
    got_first = lax.ppermute(first, axis, [(i, i ^ 1) for i in range(size)])
    links = [(i, i + 1) for i in range(1, size - 1, 2)] + [(i, i - 1) for i in range(2, size, 2)]
    got_second = lax.ppermute(jnp.where(even, to_lower, to_higher), axis, links)
    rider_got = None
    if rider is not None:
        rider_got = lax.slice_in_dim(got_first, length, None, axis=rider_dim)
        got_first = lax.slice_in_dim(got_first, 0, length, axis=rider_dim)
    from_lower = jnp.where(even, got_second, got_first)
    from_higher = jnp.where(even, got_first, got_second)
    return from_lower, from_higher, rider_got


def gather_step(x, other, position):
    low = own_bit(position) == 0
    return jnp.where(low, jnp.concatenate([x, other]), jnp.concatenate([other, x]))


def gather_order(order, count):
    where = np.zeros(count, np.int32)
    for l in range(count):
        where[l] = sum(((l >> bit) & 1) << step for step, bit in enumerate(order))
    return where


def scatter_split(x, order_left, position):
    axis = 1 + order_left.index(position)
    high = own_bit(position) == 1
    lower = lax.index_in_dim(x, 0, axis, keepdims=False)
    upper = lax.index_in_dim(x, 1, axis, keepdims=False)
    order_left.remove(position)
    return jnp.where(high, upper, lower), jnp.where(high, lower, upper)


def attention_kernel(q_ref, k_ref, v_ref, g_ref, mask_ref, o_ref, dq_ref, dkv_ref):
    head_size = q_ref.shape[1] // 2
    score_scale = 1.0 / math.sqrt(head_size)
    q = q_ref[...]
    k = k_ref[...]
    v = v_ref[...]
    g = g_ref[...]
    keep = mask_ref[...] > 0
    lane_head = lax.broadcasted_iota(jnp.int32, q.shape, 1) // head_size
    lane_head_keys = lax.broadcasted_iota(jnp.int32, k.shape, 1) // head_size
    rows = (((1,), (1,)), ((), ()))
    cols = (((0,), (0,)), ((), ()))
    out = jnp.zeros(q.shape, jnp.float32)
    dq = jnp.zeros(q.shape, jnp.float32)
    dk = jnp.zeros(k.shape, jnp.float32)
    dv = jnp.zeros(k.shape, jnp.float32)
    for head in range(2):
        mine = lane_head == head
        mine_keys = lane_head_keys == head
        q_head = jnp.where(mine, q, jnp.zeros_like(q))
        g_head = jnp.where(mine, g, jnp.zeros_like(g))
        scores = lax.dot_general(q_head, k, rows, preferred_element_type=jnp.float32) * score_scale
        scores = jnp.where(keep, scores, -1e30)
        row_max = jnp.max(scores, axis=1, keepdims=True)
        exps = jnp.exp(scores - row_max)
        probs = exps / jnp.sum(exps, axis=1, keepdims=True)
        rounded = probs.astype(jnp.bfloat16)
        attended = jnp.dot(rounded, v, preferred_element_type=jnp.float32)
        attended = attended.astype(jnp.bfloat16).astype(jnp.float32)
        out = jnp.where(mine, attended, out)
        delta = jnp.sum(
            jnp.where(mine, g.astype(jnp.float32) * attended, 0.0), axis=1, keepdims=True
        )
        dots = lax.dot_general(g_head, v, rows, preferred_element_type=jnp.float32)
        slopes = (probs * (dots - delta) * score_scale).astype(jnp.bfloat16)
        dq = jnp.where(mine, jnp.dot(slopes, k, preferred_element_type=jnp.float32), dq)
        dk = jnp.where(
            mine_keys, lax.dot_general(slopes, q, cols, preferred_element_type=jnp.float32), dk
        )
        dv = jnp.where(
            mine_keys, lax.dot_general(rounded, g, cols, preferred_element_type=jnp.float32), dv
        )
    o_ref[...] = out.astype(o_ref.dtype)
    dq_ref[...] = dq.astype(dq_ref.dtype)
    dkv_ref[0] = dk
    dkv_ref[1] = dv


def attention(queries, keys, values, grad_attended, keep):
    tokens, model_width = queries.shape
    key_count = keys.shape[0]
    lanes = 2 * (model_width // HEADS)
    steps = model_width // lanes
    token_block = pl.BlockSpec((tokens, lanes), lambda i: (0, i))
    key_block = pl.BlockSpec((key_count, lanes), lambda i: (0, i))
    mask_block = pl.BlockSpec((tokens, key_count), lambda i: (0, 0))
    grads_block = pl.BlockSpec((2, key_count, lanes), lambda i: (0, 0, i))
    flops = 2 * 2 * 6 * tokens * key_count * model_width
    moved = 2 * (3 * tokens * model_width + 2 * key_count * model_width) + 4 * (
        tokens * key_count + 2 * key_count * model_width
    )
    return pl.pallas_call(
        attention_kernel,
        grid=(steps,),
        in_specs=[token_block, key_block, key_block, token_block, mask_block],
        out_specs=[token_block, token_block, grads_block],
        out_shape=[
            jax.ShapeDtypeStruct((tokens, model_width), jnp.bfloat16),
            jax.ShapeDtypeStruct((tokens, model_width), jnp.bfloat16),
            jax.ShapeDtypeStruct((2, key_count, model_width), jnp.float32),
        ],
        cost_estimate=pl.CostEstimate(
            flops=flops, transcendentals=HEADS * tokens * key_count, bytes_accessed=moved
        ),
    )(queries, keys, values, grad_attended, keep)


def split_wide(x):
    high = x.astype(jnp.bfloat16)
    low = (x - high.astype(jnp.float32)).astype(jnp.bfloat16)
    return jnp.concatenate([high, low], axis=0)


def join_wide(pair):
    half = pair.shape[0] // 2
    return pair[:half].astype(jnp.float32) + pair[half:].astype(jnp.float32)


def shards(features, w_query, w_key, w_value, w_out, reg_pos, grad_out):
    tile_rows, tile_cols, model_width = features.shape
    row_count = lax.axis_size("rows")
    col_count = lax.axis_size("cols")
    row_index = lax.axis_index("rows")
    col_index = lax.axis_index("cols")
    band_rows = tile_rows * row_count
    band_cols = tile_cols * col_count
    first_row = row_index * tile_rows
    first_col = col_index * tile_cols
    tokens = tile_rows * tile_cols
    device_count = row_count * col_count
    col_bits = bits(col_count)
    all_bits = col_bits + bits(row_count)
    ext_rows = tile_rows + 2 * RAD

    flat_tokens = features.reshape(-1, model_width)

    own_index = row_index * col_count + col_index
    own_place = lax.dynamic_index_in_dim(reg_pos, own_index, 0, keepdims=False)
    own_local = (own_place // band_cols - first_row) * tile_cols + (own_place % band_cols - first_col)
    gathered = lax.dynamic_slice_in_dim(flat_tokens, own_local, 1, 0)
    order = [col_bits, 0] + list(range(1, col_bits)) + list(range(col_bits + 1, all_bits))

    from_above, from_below, got = exchange(
        features[:RAD].reshape(-1, model_width),
        features[tile_rows - RAD :].reshape(-1, model_width),
        "rows",
        gathered,
    )
    gathered = gather_step(gathered, got, order[0])
    extended = jnp.concatenate(
        [
            from_above.reshape(RAD, tile_cols, model_width),
            features,
            from_below.reshape(RAD, tile_cols, model_width),
        ],
        axis=0,
    )
    from_left, from_right, got = exchange(
        extended[:, :RAD].reshape(-1, model_width),
        extended[:, tile_cols - RAD :].reshape(-1, model_width),
        "cols",
        gathered,
    )
    gathered = gather_step(gathered, got, order[1])

    queries = jnp.dot(flat_tokens, w_query, preferred_element_type=jnp.float32).astype(jnp.bfloat16)
    grad_attended = jnp.dot(
        grad_out.reshape(-1, model_width), w_out.T, preferred_element_type=jnp.float32
    ).astype(jnp.bfloat16)

    for position in order[2:]:
        gathered = gather_step(gathered, partner(gathered, position), position)
    global_features = jnp.take(gathered, jnp.asarray(gather_order(order, device_count)), axis=0)

    own_keys = ext_rows * tile_cols
    strip_keys = ext_rows * RAD
    frame_keys = own_keys + 2 * strip_keys
    used = frame_keys + device_count
    key_count = -(-used // 128) * 128
    key_features = jnp.concatenate(
        [
            extended.reshape(own_keys, model_width),
            from_left,
            from_right,
            global_features,
            jnp.zeros((key_count - used, model_width), features.dtype),
        ],
        axis=0,
    )
    keys = jnp.dot(key_features, w_key, preferred_element_type=jnp.float32).astype(jnp.bfloat16)
    values = jnp.dot(key_features, w_value, preferred_element_type=jnp.float32).astype(
        jnp.bfloat16
    )

    a, b = np.meshgrid(np.arange(ext_rows), np.arange(tile_cols), indexing="ij")
    s, t = np.meshgrid(np.arange(ext_rows), np.arange(RAD), indexing="ij")
    key_rows = np.zeros(key_count, np.int32)
    key_cols = np.zeros(key_count, np.int32)
    key_rows[:frame_keys] = np.concatenate([a.reshape(-1), s.reshape(-1), s.reshape(-1)])
    key_cols[:frame_keys] = np.concatenate(
        [b.reshape(-1) + RAD, t.reshape(-1), t.reshape(-1) + RAD + tile_cols]
    )
    kind = np.full(key_count, 2, np.int32)
    kind[:frame_keys] = 0
    kind[frame_keys:used] = 1

    query_rows = first_row + jnp.repeat(jnp.arange(tile_rows, dtype=jnp.int32), tile_cols)
    query_cols = first_col + jnp.tile(jnp.arange(tile_cols, dtype=jnp.int32), tile_rows)
    start_rows = jnp.clip(query_rows - RAD, 0, band_rows - KW)[:, None]
    start_cols = jnp.clip(query_cols - RAD, 0, band_cols - KW)[:, None]
    cell_rows = (first_row - RAD + jnp.asarray(key_rows))[None, :]
    cell_cols = (first_col - RAD + jnp.asarray(key_cols))[None, :]
    inside = (
        (cell_rows >= start_rows)
        & (cell_rows < start_rows + KW)
        & (cell_cols >= start_cols)
        & (cell_cols < start_cols + KW)
    )
    key_kind = jnp.asarray(kind)[None, :]
    keep = ((inside & (key_kind == 0)) | (key_kind == 1)).astype(jnp.float32)

    attended, query_grads, kv_grads_all = attention(queries, keys, values, grad_attended, keep)
    layer_out = (
        jnp.dot(attended, w_out, preferred_element_type=jnp.float32)
        .astype(jnp.bfloat16)
        .reshape(features.shape)
    )

    rounded_grads = kv_grads_all.astype(jnp.bfloat16)
    given = jnp.dot(rounded_grads[0], w_key.T, preferred_element_type=jnp.float32) + jnp.dot(
        rounded_grads[1], w_value.T, preferred_element_type=jnp.float32
    )

    scatter = kv_grads_all[:, frame_keys:used].reshape((2,) + (2,) * all_bits + (model_width,))
    left = list(range(all_bits - 1, -1, -1))
    back_order = [0, col_bits] + list(range(1, col_bits)) + list(range(col_bits + 1, all_bits))

    keep_part, send_part = scatter_split(scatter, left, back_order[0])
    strip_shape = (ext_rows, RAD, model_width)
    from_left, from_right, got = exchange(
        given[own_keys : own_keys + strip_keys].astype(jnp.bfloat16),
        given[own_keys + strip_keys : frame_keys].astype(jnp.bfloat16),
        "cols",
        split_wide(send_part.reshape(-1, model_width)),
    )
    scatter = keep_part + join_wide(got).reshape(keep_part.shape)
    received = jnp.pad(
        from_left.astype(jnp.float32).reshape(strip_shape), ((0, 0), (0, tile_cols - RAD), (0, 0))
    ) + jnp.pad(
        from_right.astype(jnp.float32).reshape(strip_shape), ((0, 0), (tile_cols - RAD, 0), (0, 0))
    )
    extended_given = given[:own_keys].reshape(ext_rows, tile_cols, model_width) + received
    keep_part, send_part = scatter_split(scatter, left, back_order[1])
    band_shape = (RAD, tile_cols, model_width)
    from_above, from_below, got = exchange(
        extended_given[:RAD].reshape(-1, model_width).astype(jnp.bfloat16),
        extended_given[RAD + tile_rows :].reshape(-1, model_width).astype(jnp.bfloat16),
        "rows",
        split_wide(send_part.reshape(-1, model_width)),
    )
    scatter = keep_part + join_wide(got).reshape(keep_part.shape)
    received = received[RAD : RAD + tile_rows]
    received = received + jnp.pad(
        from_above.astype(jnp.float32).reshape(band_shape), ((0, tile_rows - RAD), (0, 0), (0, 0))
    )
    received = received + jnp.pad(
        from_below.astype(jnp.float32).reshape(band_shape), ((tile_rows - RAD, 0), (0, 0), (0, 0))
    )
    for position in back_order[2:]:
        keep_part, send_part = scatter_split(scatter, left, position)
        scatter = keep_part + partner(send_part, position)
    own_grads = scatter.reshape(2, 1, model_width)

    own_given = given[RAD * tile_cols : (RAD + tile_rows) * tile_cols]
    own_row = (
        lax.dynamic_slice_in_dim(kv_grads_all, RAD * tile_cols + own_local, 1, 1) + own_grads
    ).astype(jnp.bfloat16)
    own_row_given = jnp.dot(own_row[0], w_key.T, preferred_element_type=jnp.float32) + jnp.dot(
        own_row[1], w_value.T, preferred_element_type=jnp.float32
    )
    own_given = lax.dynamic_update_slice_in_dim(own_given, own_row_given, own_local, 0)

    grad_in = (
        jnp.dot(query_grads, w_query.T, preferred_element_type=jnp.float32)
        + own_given
        + received.reshape(tokens, model_width)
    )
    grad_in = grad_in.astype(jnp.bfloat16).reshape(features.shape)
    return (layer_out, grad_in)


def solution(mesh):
    placed = (P("rows", "cols", None), P(), P(), P(), P(), P(), P("rows", "cols", None))
    return jax.shard_map(
        shards,
        mesh=mesh,
        in_specs=placed,
        out_specs=(P("rows", "cols", None), P("rows", "cols", None)),
        check_vma=False,
    )
```

```python
import functools
import math

import jax
import jax.numpy as jnp
import numpy as np
from jax import lax
from jax.experimental import pallas as pl
from jax.sharding import PartitionSpec as P

HEADS = 16
KW = 13
RAD = 6


def bits(n):
    return n.bit_length() - 1


def device_bit(position):
    col_bits = bits(lax.axis_size("cols"))
    if position < col_bits:
        return "cols", position
    return "rows", position - col_bits


def own_bit(position):
    axis, bit = device_bit(position)
    return (lax.axis_index(axis) >> bit) % 2


def partner(x, position):
    axis, bit = device_bit(position)
    size = lax.axis_size(axis)
    return lax.ppermute(x, axis, [(i, i ^ (1 << bit)) for i in range(size)])


def exchange(to_lower, to_higher, axis, rider=None, rider_dim=0):
    size = lax.axis_size(axis)
    even = lax.axis_index(axis) % 2 == 0
    first = jnp.where(even, to_higher, to_lower)
    length = first.shape[rider_dim]
    if rider is not None:
        first = jnp.concatenate([first, rider], axis=rider_dim)
    got_first = lax.ppermute(first, axis, [(i, i ^ 1) for i in range(size)])
    links = [(i, i + 1) for i in range(1, size - 1, 2)] + [(i, i - 1) for i in range(2, size, 2)]
    got_second = lax.ppermute(jnp.where(even, to_lower, to_higher), axis, links)
    rider_got = None
    if rider is not None:
        rider_got = lax.slice_in_dim(got_first, length, None, axis=rider_dim)
        got_first = lax.slice_in_dim(got_first, 0, length, axis=rider_dim)
    from_lower = jnp.where(even, got_second, got_first)
    from_higher = jnp.where(even, got_first, got_second)
    return from_lower, from_higher, rider_got


def gather_step(x, other, position):
    low = own_bit(position) == 0
    return jnp.where(low, jnp.concatenate([x, other]), jnp.concatenate([other, x]))


def gather_order(order, count):
    where = np.zeros(count, np.int32)
    for l in range(count):
        where[l] = sum(((l >> bit) & 1) << step for step, bit in enumerate(order))
    return where


def scatter_split(x, order_left, position):
    axis = 1 + order_left.index(position)
    high = own_bit(position) == 1
    lower = lax.index_in_dim(x, 0, axis, keepdims=False)
    upper = lax.index_in_dim(x, 1, axis, keepdims=False)
    order_left.remove(position)
    return jnp.where(high, upper, lower), jnp.where(high, lower, upper)


def attention_kernel(own, first, last, q_ref, k_ref, v_ref, g_ref, mask_ref, o_ref, dq_ref, dkv_ref, wide_ref):
    head_size = q_ref.shape[1] // 2
    score_scale = 1.0 / math.sqrt(head_size)
    q = q_ref[...]
    k = k_ref[...]
    v = v_ref[...]
    g = g_ref[...]
    keep = mask_ref[...] > 0
    lane_head = lax.broadcasted_iota(jnp.int32, q.shape, 1) // head_size
    lane_head_keys = lax.broadcasted_iota(jnp.int32, k.shape, 1) // head_size
    rows = (((1,), (1,)), ((), ()))
    cols = (((0,), (0,)), ((), ()))
    out = jnp.zeros(q.shape, jnp.float32)
    dq = jnp.zeros(q.shape, jnp.float32)
    dk = jnp.zeros(k.shape, jnp.float32)
    dv = jnp.zeros(k.shape, jnp.float32)
    for head in range(2):
        mine = lane_head == head
        mine_keys = lane_head_keys == head
        q_head = jnp.where(mine, q, jnp.zeros_like(q))
        g_head = jnp.where(mine, g, jnp.zeros_like(g))
        scores = lax.dot_general(q_head, k, rows, preferred_element_type=jnp.float32) * score_scale
        scores = jnp.where(keep, scores, -1e30)
        row_max = jnp.max(scores, axis=1, keepdims=True)
        exps = jnp.exp(scores - row_max)
        probs = exps / jnp.sum(exps, axis=1, keepdims=True)
        rounded = probs.astype(jnp.bfloat16)
        attended = jnp.dot(rounded, v, preferred_element_type=jnp.float32)
        attended = attended.astype(jnp.bfloat16).astype(jnp.float32)
        out = jnp.where(mine, attended, out)
        delta = jnp.sum(
            jnp.where(mine, g.astype(jnp.float32) * attended, 0.0), axis=1, keepdims=True
        )
        dots = lax.dot_general(g_head, v, rows, preferred_element_type=jnp.float32)
        slopes = (probs * (dots - delta) * score_scale).astype(jnp.bfloat16)
        dq = jnp.where(mine, jnp.dot(slopes, k, preferred_element_type=jnp.float32), dq)
        dk = jnp.where(
            mine_keys, lax.dot_general(slopes, q, cols, preferred_element_type=jnp.float32), dk
        )
        dv = jnp.where(
            mine_keys, lax.dot_general(rounded, g, cols, preferred_element_type=jnp.float32), dv
        )
    o_ref[...] = out.astype(o_ref.dtype)
    dq_ref[...] = dq.astype(dq_ref.dtype)
    dkv_ref[0] = dk.astype(dkv_ref.dtype)
    dkv_ref[1] = dv.astype(dkv_ref.dtype)
    wide_ref[0, :own] = dk[:own]
    wide_ref[1, :own] = dv[:own]
    wide_ref[0, own:] = dk[first:last]
    wide_ref[1, own:] = dv[first:last]


def attention(queries, keys, values, grad_attended, keep, first, last):
    tokens, model_width = queries.shape
    key_count = keys.shape[0]
    lanes = 2 * (model_width // HEADS)
    steps = model_width // lanes
    token_block = pl.BlockSpec((tokens, lanes), lambda i: (0, i))
    key_block = pl.BlockSpec((key_count, lanes), lambda i: (0, i))
    mask_block = pl.BlockSpec((tokens, key_count), lambda i: (0, 0))
    grads_block = pl.BlockSpec((2, key_count, lanes), lambda i: (0, 0, i))
    wide_rows = tokens + last - first
    wide_block = pl.BlockSpec((2, wide_rows, lanes), lambda i: (0, 0, i))
    flops = 2 * 2 * 6 * tokens * key_count * model_width
    moved = 2 * (3 * tokens * model_width + 2 * key_count * model_width) + 4 * (
        tokens * key_count + 2 * key_count * model_width
    )
    return pl.pallas_call(
        functools.partial(attention_kernel, tokens, first, last),
        grid=(steps,),
        in_specs=[token_block, key_block, key_block, token_block, mask_block],
        out_specs=[token_block, token_block, grads_block, wide_block],
        out_shape=[
            jax.ShapeDtypeStruct((tokens, model_width), jnp.bfloat16),
            jax.ShapeDtypeStruct((tokens, model_width), jnp.bfloat16),
            jax.ShapeDtypeStruct((2, key_count, model_width), jnp.bfloat16),
            jax.ShapeDtypeStruct((2, wide_rows, model_width), jnp.float32),
        ],
        cost_estimate=pl.CostEstimate(
            flops=flops, transcendentals=HEADS * tokens * key_count, bytes_accessed=moved
        ),
    )(queries, keys, values, grad_attended, keep)


def split_wide(x):
    high = x.astype(jnp.bfloat16)
    low = (x - high.astype(jnp.float32)).astype(jnp.bfloat16)
    return jnp.concatenate([high, low], axis=0)


def join_wide(pair):
    half = pair.shape[0] // 2
    return pair[:half].astype(jnp.float32) + pair[half:].astype(jnp.float32)


def shards(features, w_query, w_key, w_value, w_out, reg_pos, grad_out):
    tile_rows, tile_cols, model_width = features.shape
    row_count = lax.axis_size("rows")
    col_count = lax.axis_size("cols")
    row_index = lax.axis_index("rows")
    col_index = lax.axis_index("cols")
    band_rows = tile_rows * row_count
    band_cols = tile_cols * col_count
    first_row = row_index * tile_rows
    first_col = col_index * tile_cols
    tokens = tile_rows * tile_cols
    device_count = row_count * col_count
    col_bits = bits(col_count)
    all_bits = col_bits + bits(row_count)
    ext_rows = tile_rows + 2 * RAD
    band_keys = RAD * tile_cols
    strip_keys = ext_rows * RAD
    frame_keys = tokens + 2 * band_keys + 2 * strip_keys
    used = frame_keys + device_count
    key_count = -(-used // 128) * 128

    flat_tokens = features.reshape(-1, model_width)

    own_index = row_index * col_count + col_index
    own_place = lax.dynamic_index_in_dim(reg_pos, own_index, 0, keepdims=False)
    own_local = (own_place // band_cols - first_row) * tile_cols + (own_place % band_cols - first_col)
    gathered = lax.dynamic_slice_in_dim(flat_tokens, own_local, 1, 0)
    order = [col_bits, 0] + list(range(1, col_bits)) + list(range(col_bits + 1, all_bits))

    from_above, from_below, got = exchange(
        features[:RAD].reshape(-1, model_width),
        features[tile_rows - RAD :].reshape(-1, model_width),
        "rows",
        gathered,
    )
    gathered = gather_step(gathered, got, order[0])
    extended = jnp.concatenate(
        [
            from_above.reshape(RAD, tile_cols, model_width),
            features,
            from_below.reshape(RAD, tile_cols, model_width),
        ],
        axis=0,
    )
    from_left, from_right, got = exchange(
        extended[:, :RAD].reshape(-1, model_width),
        extended[:, tile_cols - RAD :].reshape(-1, model_width),
        "cols",
        gathered,
    )
    gathered = gather_step(gathered, got, order[1])

    queries = jnp.dot(flat_tokens, w_query, preferred_element_type=jnp.float32).astype(jnp.bfloat16)
    grad_attended = jnp.dot(
        grad_out.reshape(-1, model_width), w_out.T, preferred_element_type=jnp.float32
    ).astype(jnp.bfloat16)

    key_features = jnp.concatenate(
        [
            flat_tokens,
            from_above,
            from_below,
            from_left,
            from_right,
            jnp.zeros((key_count - frame_keys, model_width), features.dtype),
        ],
        axis=0,
    )
    keys = jnp.dot(key_features, w_key, preferred_element_type=jnp.float32).astype(jnp.bfloat16)
    values = jnp.dot(key_features, w_value, preferred_element_type=jnp.float32).astype(
        jnp.bfloat16
    )

    for position in order[2:]:
        gathered = gather_step(gathered, partner(gathered, position), position)
    global_features = jnp.take(gathered, jnp.asarray(gather_order(order, device_count)), axis=0)
    global_keys = jnp.dot(global_features, w_key, preferred_element_type=jnp.float32)
    global_values = jnp.dot(global_features, w_value, preferred_element_type=jnp.float32)
    keys = lax.dynamic_update_slice_in_dim(keys, global_keys.astype(jnp.bfloat16), frame_keys, 0)
    values = lax.dynamic_update_slice_in_dim(
        values, global_values.astype(jnp.bfloat16), frame_keys, 0
    )

    def grid(height, width, row0, col0):
        a, b = np.meshgrid(np.arange(height) + row0, np.arange(width) + col0, indexing="ij")
        return a.reshape(-1), b.reshape(-1)

    parts = [
        grid(tile_rows, tile_cols, RAD, RAD),
        grid(RAD, tile_cols, 0, RAD),
        grid(RAD, tile_cols, RAD + tile_rows, RAD),
        grid(ext_rows, RAD, 0, 0),
        grid(ext_rows, RAD, 0, RAD + tile_cols),
    ]
    key_rows = np.zeros(key_count, np.int32)
    key_cols = np.zeros(key_count, np.int32)
    key_rows[:frame_keys] = np.concatenate([p[0] for p in parts])
    key_cols[:frame_keys] = np.concatenate([p[1] for p in parts])
    kind = np.full(key_count, 2, np.int32)
    kind[:frame_keys] = 0
    kind[frame_keys:used] = 1

    query_rows = first_row + jnp.repeat(jnp.arange(tile_rows, dtype=jnp.int32), tile_cols)
    query_cols = first_col + jnp.tile(jnp.arange(tile_cols, dtype=jnp.int32), tile_rows)
    start_rows = jnp.clip(query_rows - RAD, 0, band_rows - KW)[:, None]
    start_cols = jnp.clip(query_cols - RAD, 0, band_cols - KW)[:, None]
    cell_rows = (first_row - RAD + jnp.asarray(key_rows))[None, :]
    cell_cols = (first_col - RAD + jnp.asarray(key_cols))[None, :]
    inside = (
        (cell_rows >= start_rows)
        & (cell_rows < start_rows + KW)
        & (cell_cols >= start_cols)
        & (cell_cols < start_cols + KW)
    )
    key_kind = jnp.asarray(kind)[None, :]
    keep = ((inside & (key_kind == 0)) | (key_kind == 1)).astype(jnp.float32)

    attended, query_grads, rounded_grads, wide_grads = attention(
        queries, keys, values, grad_attended, keep, frame_keys, used
    )
    layer_out = (
        jnp.dot(attended, w_out, preferred_element_type=jnp.float32)
        .astype(jnp.bfloat16)
        .reshape(features.shape)
    )

    def given(lo, hi):
        return jnp.dot(rounded_grads[0, lo:hi], w_key.T, preferred_element_type=jnp.float32) + jnp.dot(
            rounded_grads[1, lo:hi], w_value.T, preferred_element_type=jnp.float32
        )

    scatter = wide_grads[:, tokens:].reshape(
        (2,) + (2,) * all_bits + (model_width,)
    )
    left = list(range(all_bits - 1, -1, -1))
    back_order = [0, col_bits] + list(range(1, col_bits)) + list(range(col_bits + 1, all_bits))

    strips_from = tokens + 2 * band_keys
    keep_part, send_part = scatter_split(scatter, left, back_order[0])
    strip_shape = (ext_rows, RAD, model_width)
    from_left, from_right, got = exchange(
        given(strips_from, strips_from + strip_keys).astype(jnp.bfloat16),
        given(strips_from + strip_keys, frame_keys).astype(jnp.bfloat16),
        "cols",
        split_wide(send_part.reshape(-1, model_width)),
    )
    scatter = keep_part + join_wide(got).reshape(keep_part.shape)
    received = jnp.pad(
        from_left.astype(jnp.float32).reshape(strip_shape), ((0, 0), (0, tile_cols - RAD), (0, 0))
    ) + jnp.pad(
        from_right.astype(jnp.float32).reshape(strip_shape), ((0, 0), (tile_cols - RAD, 0), (0, 0))
    )
    band_shape = (RAD, tile_cols, model_width)
    keep_part, send_part = scatter_split(scatter, left, back_order[1])
    from_above, from_below, got = exchange(
        (given(tokens, tokens + band_keys).reshape(band_shape) + received[:RAD])
        .reshape(-1, model_width)
        .astype(jnp.bfloat16),
        (given(tokens + band_keys, strips_from).reshape(band_shape) + received[RAD + tile_rows :])
        .reshape(-1, model_width)
        .astype(jnp.bfloat16),
        "rows",
        split_wide(send_part.reshape(-1, model_width)),
    )
    scatter = keep_part + join_wide(got).reshape(keep_part.shape)
    received = received[RAD : RAD + tile_rows]
    received = received + jnp.pad(
        from_above.astype(jnp.float32).reshape(band_shape), ((0, tile_rows - RAD), (0, 0), (0, 0))
    )
    received = received + jnp.pad(
        from_below.astype(jnp.float32).reshape(band_shape), ((tile_rows - RAD, 0), (0, 0), (0, 0))
    )
    for position in back_order[2:]:
        keep_part, send_part = scatter_split(scatter, left, position)
        scatter = keep_part + partner(send_part, position)
    own_grads = scatter.reshape(2, 1, model_width)

    own_given = given(0, tokens)
    own_row = (lax.dynamic_slice_in_dim(wide_grads, own_local, 1, 1) + own_grads).astype(
        jnp.bfloat16
    )
    own_row_given = jnp.dot(own_row[0], w_key.T, preferred_element_type=jnp.float32) + jnp.dot(
        own_row[1], w_value.T, preferred_element_type=jnp.float32
    )
    own_given = lax.dynamic_update_slice_in_dim(own_given, own_row_given, own_local, 0)

    grad_in = (
        jnp.dot(query_grads, w_query.T, preferred_element_type=jnp.float32)
        + own_given
        + received.reshape(tokens, model_width)
    )
    grad_in = grad_in.astype(jnp.bfloat16).reshape(features.shape)
    return (layer_out, grad_in)


def solution(mesh):
    placed = (P("rows", "cols", None), P(), P(), P(), P(), P(), P("rows", "cols", None))
    return jax.shard_map(
        shards,
        mesh=mesh,
        in_specs=placed,
        out_specs=(P("rows", "cols", None), P("rows", "cols", None)),
        check_vma=False,
    )
```

```python
import functools
import math

import jax
import jax.numpy as jnp
import numpy as np
from jax import lax
from jax.experimental import pallas as pl
from jax.sharding import PartitionSpec as P

HEADS = 16
KW = 13
RAD = 6


def bits(n):
    return n.bit_length() - 1


def device_bit(position):
    col_bits = bits(lax.axis_size("cols"))
    if position < col_bits:
        return "cols", position
    return "rows", position - col_bits


def own_bit(position):
    axis, bit = device_bit(position)
    return (lax.axis_index(axis) >> bit) % 2


def partner(x, position):
    axis, bit = device_bit(position)
    size = lax.axis_size(axis)
    return lax.ppermute(x, axis, [(i, i ^ (1 << bit)) for i in range(size)])


def exchange(to_lower, to_higher, axis, rider=None, rider_dim=0):
    size = lax.axis_size(axis)
    even = lax.axis_index(axis) % 2 == 0
    first = jnp.where(even, to_higher, to_lower)
    length = first.shape[rider_dim]
    if rider is not None:
        first = jnp.concatenate([first, rider], axis=rider_dim)
    got_first = lax.ppermute(first, axis, [(i, i ^ 1) for i in range(size)])
    links = [(i, i + 1) for i in range(1, size - 1, 2)] + [(i, i - 1) for i in range(2, size, 2)]
    got_second = lax.ppermute(jnp.where(even, to_lower, to_higher), axis, links)
    rider_got = None
    if rider is not None:
        rider_got = lax.slice_in_dim(got_first, length, None, axis=rider_dim)
        got_first = lax.slice_in_dim(got_first, 0, length, axis=rider_dim)
    from_lower = jnp.where(even, got_second, got_first)
    from_higher = jnp.where(even, got_first, got_second)
    return from_lower, from_higher, rider_got


def gather_step(x, other, position):
    low = own_bit(position) == 0
    return jnp.where(low, jnp.concatenate([x, other]), jnp.concatenate([other, x]))


def gather_order(order, count):
    where = np.zeros(count, np.int32)
    for l in range(count):
        where[l] = sum(((l >> bit) & 1) << step for step, bit in enumerate(order))
    return where


def scatter_split(x, order_left, position):
    axis = 1 + order_left.index(position)
    high = own_bit(position) == 1
    lower = lax.index_in_dim(x, 0, axis, keepdims=False)
    upper = lax.index_in_dim(x, 1, axis, keepdims=False)
    order_left.remove(position)
    return jnp.where(high, upper, lower), jnp.where(high, lower, upper)


def attention_kernel(
    own, first, last, q_ref, kf_ref, kg_ref, vf_ref, vg_ref, g_ref, mask_ref, o_ref, dq_ref, dkv_ref, wide_ref
):
    head_size = q_ref.shape[1] // 2
    score_scale = 1.0 / math.sqrt(head_size)
    q = q_ref[...]
    k = jnp.concatenate([kf_ref[...], kg_ref[...]], axis=0)
    v = jnp.concatenate([vf_ref[...], vg_ref[...]], axis=0)
    g = g_ref[...]
    keep = mask_ref[...] > 0
    lane_head = lax.broadcasted_iota(jnp.int32, q.shape, 1) // head_size
    lane_head_keys = lax.broadcasted_iota(jnp.int32, k.shape, 1) // head_size
    rows = (((1,), (1,)), ((), ()))
    cols = (((0,), (0,)), ((), ()))
    out = jnp.zeros(q.shape, jnp.float32)
    dq = jnp.zeros(q.shape, jnp.float32)
    dk = jnp.zeros(k.shape, jnp.float32)
    dv = jnp.zeros(k.shape, jnp.float32)
    for head in range(2):
        mine = lane_head == head
        mine_keys = lane_head_keys == head
        q_head = jnp.where(mine, q, jnp.zeros_like(q))
        g_head = jnp.where(mine, g, jnp.zeros_like(g))
        scores = lax.dot_general(q_head, k, rows, preferred_element_type=jnp.float32) * score_scale
        scores = jnp.where(keep, scores, -1e30)
        row_max = jnp.max(scores, axis=1, keepdims=True)
        exps = jnp.exp(scores - row_max)
        probs = exps * (1.0 / jnp.sum(exps, axis=1, keepdims=True))
        rounded = probs.astype(jnp.bfloat16)
        attended = jnp.dot(rounded, v, preferred_element_type=jnp.float32)
        attended = attended.astype(jnp.bfloat16).astype(jnp.float32)
        out = jnp.where(mine, attended, out)
        delta = jnp.sum(
            jnp.where(mine, g.astype(jnp.float32) * attended, 0.0), axis=1, keepdims=True
        )
        dots = lax.dot_general(g_head, v, rows, preferred_element_type=jnp.float32)
        slopes = (probs * (dots - delta) * score_scale).astype(jnp.bfloat16)
        dq = jnp.where(mine, jnp.dot(slopes, k, preferred_element_type=jnp.float32), dq)
        dk = jnp.where(
            mine_keys, lax.dot_general(slopes, q, cols, preferred_element_type=jnp.float32), dk
        )
        dv = jnp.where(
            mine_keys, lax.dot_general(rounded, g, cols, preferred_element_type=jnp.float32), dv
        )
    o_ref[...] = out.astype(o_ref.dtype)
    dq_ref[...] = dq.astype(dq_ref.dtype)
    dkv_ref[0] = dk.astype(dkv_ref.dtype)
    dkv_ref[1] = dv.astype(dkv_ref.dtype)
    wide_ref[0, :own] = dk[:own]
    wide_ref[1, :own] = dv[:own]
    wide_ref[0, own:] = dk[first:last]
    wide_ref[1, own:] = dv[first:last]


def attention(queries, keys, values, global_keys, global_values, grad_attended, keep):
    tokens, model_width = queries.shape
    first = keys.shape[0]
    last = first + global_keys.shape[0]
    key_count = last
    lanes = 2 * (model_width // HEADS)
    steps = model_width // lanes
    token_block = pl.BlockSpec((tokens, lanes), lambda i: (0, i))
    key_block = pl.BlockSpec((key_count, lanes), lambda i: (0, i))
    frame_block = pl.BlockSpec((first, lanes), lambda i: (0, i))
    global_block = pl.BlockSpec((last - first, lanes), lambda i: (0, i))
    mask_block = pl.BlockSpec((tokens, key_count), lambda i: (0, 0))
    grads_block = pl.BlockSpec((2, key_count, lanes), lambda i: (0, 0, i))
    wide_rows = tokens + last - first
    wide_block = pl.BlockSpec((2, wide_rows, lanes), lambda i: (0, 0, i))
    flops = 2 * 2 * 6 * tokens * key_count * model_width
    moved = 2 * (3 * tokens * model_width + 2 * key_count * model_width) + 4 * (
        tokens * key_count + 2 * key_count * model_width
    )
    return pl.pallas_call(
        functools.partial(attention_kernel, tokens, first, last),
        grid=(steps,),
        in_specs=[
            token_block,
            frame_block,
            global_block,
            frame_block,
            global_block,
            token_block,
            mask_block,
        ],
        out_specs=[token_block, token_block, grads_block, wide_block],
        out_shape=[
            jax.ShapeDtypeStruct((tokens, model_width), jnp.bfloat16),
            jax.ShapeDtypeStruct((tokens, model_width), jnp.bfloat16),
            jax.ShapeDtypeStruct((2, key_count, model_width), jnp.bfloat16),
            jax.ShapeDtypeStruct((2, wide_rows, model_width), jnp.float32),
        ],
        cost_estimate=pl.CostEstimate(
            flops=flops, transcendentals=HEADS * tokens * key_count, bytes_accessed=moved
        ),
    )(queries, keys, global_keys, values, global_values, grad_attended, keep)


def split_wide(x):
    high = x.astype(jnp.bfloat16)
    low = (x - high.astype(jnp.float32)).astype(jnp.bfloat16)
    return jnp.concatenate([high, low], axis=0)


def join_wide(pair):
    half = pair.shape[0] // 2
    return pair[:half].astype(jnp.float32) + pair[half:].astype(jnp.float32)


def shards(features, w_query, w_key, w_value, w_out, reg_pos, grad_out):
    tile_rows, tile_cols, model_width = features.shape
    row_count = lax.axis_size("rows")
    col_count = lax.axis_size("cols")
    row_index = lax.axis_index("rows")
    col_index = lax.axis_index("cols")
    band_rows = tile_rows * row_count
    band_cols = tile_cols * col_count
    first_row = row_index * tile_rows
    first_col = col_index * tile_cols
    tokens = tile_rows * tile_cols
    device_count = row_count * col_count
    col_bits = bits(col_count)
    all_bits = col_bits + bits(row_count)
    ext_rows = tile_rows + 2 * RAD
    band_keys = RAD * tile_cols
    strip_keys = ext_rows * RAD
    frame_keys = tokens + 2 * band_keys + 2 * strip_keys
    used = frame_keys + device_count
    key_count = -(-used // 128) * 128

    flat_tokens = features.reshape(-1, model_width)

    own_index = row_index * col_count + col_index
    own_place = lax.dynamic_index_in_dim(reg_pos, own_index, 0, keepdims=False)
    own_local = (own_place // band_cols - first_row) * tile_cols + (own_place % band_cols - first_col)
    gathered = lax.dynamic_slice_in_dim(flat_tokens, own_local, 1, 0)
    order = [col_bits, 0] + list(range(1, col_bits)) + list(range(col_bits + 1, all_bits))

    from_above, from_below, got = exchange(
        features[:RAD].reshape(-1, model_width),
        features[tile_rows - RAD :].reshape(-1, model_width),
        "rows",
        gathered,
    )
    gathered = gather_step(gathered, got, order[0])
    extended = jnp.concatenate(
        [
            from_above.reshape(RAD, tile_cols, model_width),
            features,
            from_below.reshape(RAD, tile_cols, model_width),
        ],
        axis=0,
    )
    from_left, from_right, got = exchange(
        extended[:, :RAD].reshape(-1, model_width),
        extended[:, tile_cols - RAD :].reshape(-1, model_width),
        "cols",
        gathered,
    )
    gathered = gather_step(gathered, got, order[1])

    queries = jnp.dot(flat_tokens, w_query, preferred_element_type=jnp.float32).astype(jnp.bfloat16)
    grad_attended = jnp.dot(
        grad_out.reshape(-1, model_width), w_out.T, preferred_element_type=jnp.float32
    ).astype(jnp.bfloat16)

    key_features = jnp.concatenate(
        [
            flat_tokens,
            from_above,
            from_below,
            from_left,
            from_right,
            jnp.zeros((key_count - used, model_width), features.dtype),
        ],
        axis=0,
    )
    keys = jnp.dot(key_features, w_key, preferred_element_type=jnp.float32).astype(jnp.bfloat16)
    values = jnp.dot(key_features, w_value, preferred_element_type=jnp.float32).astype(
        jnp.bfloat16
    )

    for position in order[2:]:
        gathered = gather_step(gathered, partner(gathered, position), position)
    global_features = jnp.take(gathered, jnp.asarray(gather_order(order, device_count)), axis=0)
    global_keys = jnp.dot(global_features, w_key, preferred_element_type=jnp.float32).astype(
        jnp.bfloat16
    )
    global_values = jnp.dot(
        global_features, w_value, preferred_element_type=jnp.float32
    ).astype(jnp.bfloat16)

    def grid(height, width, row0, col0):
        a, b = np.meshgrid(np.arange(height) + row0, np.arange(width) + col0, indexing="ij")
        return a.reshape(-1), b.reshape(-1)

    parts = [
        grid(tile_rows, tile_cols, RAD, RAD),
        grid(RAD, tile_cols, 0, RAD),
        grid(RAD, tile_cols, RAD + tile_rows, RAD),
        grid(ext_rows, RAD, 0, 0),
        grid(ext_rows, RAD, 0, RAD + tile_cols),
    ]
    key_rows = np.zeros(key_count, np.int32)
    key_cols = np.zeros(key_count, np.int32)
    key_rows[:frame_keys] = np.concatenate([p[0] for p in parts])
    key_cols[:frame_keys] = np.concatenate([p[1] for p in parts])
    kind = np.full(key_count, 2, np.int32)
    kind[:frame_keys] = 0
    kind[key_count - device_count :] = 1

    query_rows = first_row + jnp.repeat(jnp.arange(tile_rows, dtype=jnp.int32), tile_cols)
    query_cols = first_col + jnp.tile(jnp.arange(tile_cols, dtype=jnp.int32), tile_rows)
    start_rows = jnp.clip(query_rows - RAD, 0, band_rows - KW)[:, None]
    start_cols = jnp.clip(query_cols - RAD, 0, band_cols - KW)[:, None]
    cell_rows = (first_row - RAD + jnp.asarray(key_rows))[None, :]
    cell_cols = (first_col - RAD + jnp.asarray(key_cols))[None, :]
    inside = (
        (cell_rows >= start_rows)
        & (cell_rows < start_rows + KW)
        & (cell_cols >= start_cols)
        & (cell_cols < start_cols + KW)
    )
    key_kind = jnp.asarray(kind)[None, :]
    keep = ((inside & (key_kind == 0)) | (key_kind == 1)).astype(jnp.float32)

    attended, query_grads, rounded_grads, wide_grads = attention(
        queries, keys, values, global_keys, global_values, grad_attended, keep
    )
    layer_out = (
        jnp.dot(attended, w_out, preferred_element_type=jnp.float32)
        .astype(jnp.bfloat16)
        .reshape(features.shape)
    )

    given_all = jnp.dot(
        rounded_grads[0, :frame_keys], w_key.T, preferred_element_type=jnp.float32
    ) + jnp.dot(rounded_grads[1, :frame_keys], w_value.T, preferred_element_type=jnp.float32)

    def given(lo, hi):
        return given_all[lo:hi]

    scatter = wide_grads[:, tokens:].reshape(
        (2,) + (2,) * all_bits + (model_width,)
    )
    left = list(range(all_bits - 1, -1, -1))
    back_order = [0, col_bits] + list(range(1, col_bits)) + list(range(col_bits + 1, all_bits))

    strips_from = tokens + 2 * band_keys
    keep_part, send_part = scatter_split(scatter, left, back_order[0])
    strip_shape = (ext_rows, RAD, model_width)
    from_left, from_right, got = exchange(
        given(strips_from, strips_from + strip_keys).astype(jnp.bfloat16),
        given(strips_from + strip_keys, frame_keys).astype(jnp.bfloat16),
        "cols",
        split_wide(send_part.reshape(-1, model_width)),
    )
    scatter = keep_part + join_wide(got).reshape(keep_part.shape)
    received = jnp.pad(
        from_left.astype(jnp.float32).reshape(strip_shape), ((0, 0), (0, tile_cols - RAD), (0, 0))
    ) + jnp.pad(
        from_right.astype(jnp.float32).reshape(strip_shape), ((0, 0), (tile_cols - RAD, 0), (0, 0))
    )
    band_shape = (RAD, tile_cols, model_width)
    keep_part, send_part = scatter_split(scatter, left, back_order[1])
    from_above, from_below, got = exchange(
        (given(tokens, tokens + band_keys).reshape(band_shape) + received[:RAD])
        .reshape(-1, model_width)
        .astype(jnp.bfloat16),
        (given(tokens + band_keys, strips_from).reshape(band_shape) + received[RAD + tile_rows :])
        .reshape(-1, model_width)
        .astype(jnp.bfloat16),
        "rows",
        split_wide(send_part.reshape(-1, model_width)),
    )
    scatter = keep_part + join_wide(got).reshape(keep_part.shape)
    received = received[RAD : RAD + tile_rows]
    received = received + jnp.pad(
        from_above.astype(jnp.float32).reshape(band_shape), ((0, tile_rows - RAD), (0, 0), (0, 0))
    )
    received = received + jnp.pad(
        from_below.astype(jnp.float32).reshape(band_shape), ((tile_rows - RAD, 0), (0, 0), (0, 0))
    )
    for position in back_order[2:]:
        keep_part, send_part = scatter_split(scatter, left, position)
        scatter = keep_part + partner(send_part, position)
    own_grads = scatter.reshape(2, 1, model_width)

    own_given = given(0, tokens)
    own_row = (lax.dynamic_slice_in_dim(wide_grads, own_local, 1, 1) + own_grads).astype(
        jnp.bfloat16
    )
    own_row_given = jnp.dot(own_row[0], w_key.T, preferred_element_type=jnp.float32) + jnp.dot(
        own_row[1], w_value.T, preferred_element_type=jnp.float32
    )
    own_given = lax.dynamic_update_slice_in_dim(own_given, own_row_given, own_local, 0)

    grad_in = (
        jnp.dot(query_grads, w_query.T, preferred_element_type=jnp.float32)
        + own_given
        + received.reshape(tokens, model_width)
    )
    grad_in = grad_in.astype(jnp.bfloat16).reshape(features.shape)
    return (layer_out, grad_in)


def solution(mesh):
    placed = (P("rows", "cols", None), P(), P(), P(), P(), P(), P("rows", "cols", None))
    return jax.shard_map(
        shards,
        mesh=mesh,
        in_specs=placed,
        out_specs=(P("rows", "cols", None), P("rows", "cols", None)),
        check_vma=False,
    )
```

```python
import functools
import math

import jax
import jax.numpy as jnp
import numpy as np
from jax import lax
from jax.experimental import pallas as pl
from jax.sharding import PartitionSpec as P

HEADS = 16
KW = 13
RAD = 6


def bits(n):
    return n.bit_length() - 1


def device_bit(position):
    col_bits = bits(lax.axis_size("cols"))
    if position < col_bits:
        return "cols", position
    return "rows", position - col_bits


def own_bit(position):
    axis, bit = device_bit(position)
    return (lax.axis_index(axis) >> bit) % 2


def partner(x, position):
    axis, bit = device_bit(position)
    size = lax.axis_size(axis)
    return lax.ppermute(x, axis, [(i, i ^ (1 << bit)) for i in range(size)])


def exchange(to_lower, to_higher, axis, rider=None, rider_dim=0):
    size = lax.axis_size(axis)
    even = lax.axis_index(axis) % 2 == 0
    first = jnp.where(even, to_higher, to_lower)
    length = first.shape[rider_dim]
    if rider is not None:
        first = jnp.concatenate([first, rider], axis=rider_dim)
    got_first = lax.ppermute(first, axis, [(i, i ^ 1) for i in range(size)])
    links = [(i, i + 1) for i in range(1, size - 1, 2)] + [(i, i - 1) for i in range(2, size, 2)]
    got_second = lax.ppermute(jnp.where(even, to_lower, to_higher), axis, links)
    rider_got = None
    if rider is not None:
        rider_got = lax.slice_in_dim(got_first, length, None, axis=rider_dim)
        got_first = lax.slice_in_dim(got_first, 0, length, axis=rider_dim)
    from_lower = jnp.where(even, got_second, got_first)
    from_higher = jnp.where(even, got_first, got_second)
    return from_lower, from_higher, rider_got


def gather_step(x, other, position):
    low = own_bit(position) == 0
    return jnp.where(low, jnp.concatenate([x, other]), jnp.concatenate([other, x]))


def gather_order(order, count):
    where = np.zeros(count, np.int32)
    for l in range(count):
        where[l] = sum(((l >> bit) & 1) << step for step, bit in enumerate(order))
    return where


def scatter_split(x, order_left, position):
    axis = 1 + order_left.index(position)
    high = own_bit(position) == 1
    lower = lax.index_in_dim(x, 0, axis, keepdims=False)
    upper = lax.index_in_dim(x, 1, axis, keepdims=False)
    order_left.remove(position)
    return jnp.where(high, upper, lower), jnp.where(high, lower, upper)


def attention_kernel(
    own, first, last, q_ref, ko_ref, kh_ref, kg_ref, vo_ref, vh_ref, vg_ref, g_ref, mask_ref,
    o_ref, dq_ref, dkv_ref, wide_ref,
):
    head_size = q_ref.shape[1] // 2
    score_scale = 1.0 / math.sqrt(head_size)
    q = q_ref[...]
    k = jnp.concatenate([ko_ref[...], kh_ref[...], kg_ref[...]], axis=0)
    v = jnp.concatenate([vo_ref[...], vh_ref[...], vg_ref[...]], axis=0)
    g = g_ref[...]
    keep = mask_ref[...] > 0
    lane_head = lax.broadcasted_iota(jnp.int32, q.shape, 1) // head_size
    lane_head_keys = lax.broadcasted_iota(jnp.int32, k.shape, 1) // head_size
    rows = (((1,), (1,)), ((), ()))
    cols = (((0,), (0,)), ((), ()))
    out = jnp.zeros(q.shape, jnp.float32)
    dq = jnp.zeros(q.shape, jnp.float32)
    dk = jnp.zeros(k.shape, jnp.float32)
    dv = jnp.zeros(k.shape, jnp.float32)
    for head in range(2):
        mine = lane_head == head
        mine_keys = lane_head_keys == head
        q_head = jnp.where(mine, q, jnp.zeros_like(q))
        g_head = jnp.where(mine, g, jnp.zeros_like(g))
        scores = lax.dot_general(q_head, k, rows, preferred_element_type=jnp.float32) * score_scale
        scores = jnp.where(keep, scores, -1e30)
        row_max = jnp.max(scores, axis=1, keepdims=True)
        exps = jnp.exp(scores - row_max)
        probs = exps * (1.0 / jnp.sum(exps, axis=1, keepdims=True))
        rounded = probs.astype(jnp.bfloat16)
        attended = jnp.dot(rounded, v, preferred_element_type=jnp.float32)
        attended = attended.astype(jnp.bfloat16).astype(jnp.float32)
        out = jnp.where(mine, attended, out)
        delta = jnp.sum(
            jnp.where(mine, g.astype(jnp.float32) * attended, 0.0), axis=1, keepdims=True
        )
        dots = lax.dot_general(g_head, v, rows, preferred_element_type=jnp.float32)
        slopes = (probs * (dots - delta) * score_scale).astype(jnp.bfloat16)
        dq = jnp.where(mine, jnp.dot(slopes, k, preferred_element_type=jnp.float32), dq)
        dk = jnp.where(
            mine_keys, lax.dot_general(slopes, q, cols, preferred_element_type=jnp.float32), dk
        )
        dv = jnp.where(
            mine_keys, lax.dot_general(rounded, g, cols, preferred_element_type=jnp.float32), dv
        )
    o_ref[...] = out.astype(o_ref.dtype)
    dq_ref[...] = dq.astype(dq_ref.dtype)
    dkv_ref[0] = dk.astype(dkv_ref.dtype)
    dkv_ref[1] = dv.astype(dkv_ref.dtype)
    wide_ref[0, :own] = dk[:own]
    wide_ref[1, :own] = dv[:own]
    wide_ref[0, own:] = dk[first:last]
    wide_ref[1, own:] = dv[first:last]


def attention(queries, keys, values, global_keys, global_values, grad_attended, keep):
    tokens, model_width = queries.shape
    first = keys[0].shape[0] + keys[1].shape[0]
    last = first + global_keys.shape[0]
    key_count = last
    lanes = 2 * (model_width // HEADS)
    steps = model_width // lanes
    token_block = pl.BlockSpec((tokens, lanes), lambda i: (0, i))
    key_block = pl.BlockSpec((key_count, lanes), lambda i: (0, i))
    own_block = pl.BlockSpec((keys[0].shape[0], lanes), lambda i: (0, i))
    halo_block = pl.BlockSpec((keys[1].shape[0], lanes), lambda i: (0, i))
    global_block = pl.BlockSpec((last - first, lanes), lambda i: (0, i))
    mask_block = pl.BlockSpec((tokens, key_count), lambda i: (0, 0))
    grads_block = pl.BlockSpec((2, key_count, lanes), lambda i: (0, 0, i))
    wide_rows = tokens + last - first
    wide_block = pl.BlockSpec((2, wide_rows, lanes), lambda i: (0, 0, i))
    flops = 2 * 2 * 6 * tokens * key_count * model_width
    moved = 2 * (3 * tokens * model_width + 2 * key_count * model_width) + 4 * (
        tokens * key_count + 2 * key_count * model_width
    )
    return pl.pallas_call(
        functools.partial(attention_kernel, tokens, first, last),
        grid=(steps,),
        in_specs=[
            token_block,
            own_block,
            halo_block,
            global_block,
            own_block,
            halo_block,
            global_block,
            token_block,
            mask_block,
        ],
        out_specs=[token_block, token_block, grads_block, wide_block],
        out_shape=[
            jax.ShapeDtypeStruct((tokens, model_width), jnp.bfloat16),
            jax.ShapeDtypeStruct((tokens, model_width), jnp.bfloat16),
            jax.ShapeDtypeStruct((2, key_count, model_width), jnp.bfloat16),
            jax.ShapeDtypeStruct((2, wide_rows, model_width), jnp.float32),
        ],
        cost_estimate=pl.CostEstimate(
            flops=flops, transcendentals=HEADS * tokens * key_count, bytes_accessed=moved
        ),
    )(queries, *keys, global_keys, *values, global_values, grad_attended, keep)


def split_wide(x):
    high = x.astype(jnp.bfloat16)
    low = (x - high.astype(jnp.float32)).astype(jnp.bfloat16)
    return jnp.concatenate([high, low], axis=0)


def join_wide(pair):
    half = pair.shape[0] // 2
    return pair[:half].astype(jnp.float32) + pair[half:].astype(jnp.float32)


def shards(features, w_query, w_key, w_value, w_out, reg_pos, grad_out):
    tile_rows, tile_cols, model_width = features.shape
    row_count = lax.axis_size("rows")
    col_count = lax.axis_size("cols")
    row_index = lax.axis_index("rows")
    col_index = lax.axis_index("cols")
    band_rows = tile_rows * row_count
    band_cols = tile_cols * col_count
    first_row = row_index * tile_rows
    first_col = col_index * tile_cols
    tokens = tile_rows * tile_cols
    device_count = row_count * col_count
    col_bits = bits(col_count)
    all_bits = col_bits + bits(row_count)
    ext_rows = tile_rows + 2 * RAD
    band_keys = RAD * tile_cols
    strip_keys = ext_rows * RAD
    frame_keys = tokens + 2 * band_keys + 2 * strip_keys
    used = frame_keys + device_count
    key_count = -(-used // 128) * 128

    flat_tokens = features.reshape(-1, model_width)
    own_keys = jnp.dot(flat_tokens, w_key, preferred_element_type=jnp.float32).astype(jnp.bfloat16)
    own_values = jnp.dot(flat_tokens, w_value, preferred_element_type=jnp.float32).astype(
        jnp.bfloat16
    )

    own_index = row_index * col_count + col_index
    own_place = lax.dynamic_index_in_dim(reg_pos, own_index, 0, keepdims=False)
    own_local = (own_place // band_cols - first_row) * tile_cols + (own_place % band_cols - first_col)
    gathered = jnp.concatenate(
        [
            lax.dynamic_slice_in_dim(own_keys, own_local, 1, 0),
            lax.dynamic_slice_in_dim(own_values, own_local, 1, 0),
        ],
        axis=1,
    )
    order = [col_bits, 0] + list(range(1, col_bits)) + list(range(col_bits + 1, all_bits))

    from_above, from_below, got = exchange(
        features[:RAD].reshape(-1, model_width),
        features[tile_rows - RAD :].reshape(-1, model_width),
        "rows",
        gathered.reshape(-1, model_width),
    )
    gathered = gather_step(gathered, got.reshape(gathered.shape), order[0])
    extended = jnp.concatenate(
        [
            from_above.reshape(RAD, tile_cols, model_width),
            features,
            from_below.reshape(RAD, tile_cols, model_width),
        ],
        axis=0,
    )
    from_left, from_right, got = exchange(
        extended[:, :RAD].reshape(-1, model_width),
        extended[:, tile_cols - RAD :].reshape(-1, model_width),
        "cols",
        gathered.reshape(-1, model_width),
    )
    gathered = gather_step(gathered, got.reshape(gathered.shape), order[1])

    queries = jnp.dot(flat_tokens, w_query, preferred_element_type=jnp.float32).astype(jnp.bfloat16)
    grad_attended = jnp.dot(
        grad_out.reshape(-1, model_width), w_out.T, preferred_element_type=jnp.float32
    ).astype(jnp.bfloat16)

    halo_features = jnp.concatenate(
        [
            from_above,
            from_below,
            from_left,
            from_right,
            jnp.zeros((key_count - used, model_width), features.dtype),
        ],
        axis=0,
    )
    halo_keys = jnp.dot(halo_features, w_key, preferred_element_type=jnp.float32).astype(
        jnp.bfloat16
    )
    halo_values = jnp.dot(halo_features, w_value, preferred_element_type=jnp.float32).astype(
        jnp.bfloat16
    )

    for position in order[2:]:
        gathered = gather_step(gathered, partner(gathered, position), position)
    global_kv = jnp.take(gathered, jnp.asarray(gather_order(order, device_count)), axis=0)
    global_keys = global_kv[:, :model_width]
    global_values = global_kv[:, model_width:]

    def grid(height, width, row0, col0):
        a, b = np.meshgrid(np.arange(height) + row0, np.arange(width) + col0, indexing="ij")
        return a.reshape(-1), b.reshape(-1)

    parts = [
        grid(tile_rows, tile_cols, RAD, RAD),
        grid(RAD, tile_cols, 0, RAD),
        grid(RAD, tile_cols, RAD + tile_rows, RAD),
        grid(ext_rows, RAD, 0, 0),
        grid(ext_rows, RAD, 0, RAD + tile_cols),
    ]
    key_rows = np.zeros(key_count, np.int32)
    key_cols = np.zeros(key_count, np.int32)
    key_rows[:frame_keys] = np.concatenate([p[0] for p in parts])
    key_cols[:frame_keys] = np.concatenate([p[1] for p in parts])
    kind = np.full(key_count, 2, np.int32)
    kind[:frame_keys] = 0
    kind[key_count - device_count :] = 1

    query_rows = first_row + jnp.repeat(jnp.arange(tile_rows, dtype=jnp.int32), tile_cols)
    query_cols = first_col + jnp.tile(jnp.arange(tile_cols, dtype=jnp.int32), tile_rows)
    start_rows = jnp.clip(query_rows - RAD, 0, band_rows - KW)[:, None]
    start_cols = jnp.clip(query_cols - RAD, 0, band_cols - KW)[:, None]
    cell_rows = (first_row - RAD + jnp.asarray(key_rows))[None, :]
    cell_cols = (first_col - RAD + jnp.asarray(key_cols))[None, :]
    inside = (
        (cell_rows >= start_rows)
        & (cell_rows < start_rows + KW)
        & (cell_cols >= start_cols)
        & (cell_cols < start_cols + KW)
    )
    key_kind = jnp.asarray(kind)[None, :]
    keep = ((inside & (key_kind == 0)) | (key_kind == 1)).astype(jnp.float32)

    attended, query_grads, rounded_grads, wide_grads = attention(
        queries,
        (own_keys, halo_keys),
        (own_values, halo_values),
        global_keys,
        global_values,
        grad_attended,
        keep,
    )
    layer_out = (
        jnp.dot(attended, w_out, preferred_element_type=jnp.float32)
        .astype(jnp.bfloat16)
        .reshape(features.shape)
    )

    given_all = jnp.dot(
        rounded_grads[0, :frame_keys], w_key.T, preferred_element_type=jnp.float32
    ) + jnp.dot(rounded_grads[1, :frame_keys], w_value.T, preferred_element_type=jnp.float32)

    def given(lo, hi):
        return given_all[lo:hi]

    scatter = wide_grads[:, tokens:].reshape(
        (2,) + (2,) * all_bits + (model_width,)
    )
    left = list(range(all_bits - 1, -1, -1))
    back_order = [0, col_bits] + list(range(1, col_bits)) + list(range(col_bits + 1, all_bits))

    strips_from = tokens + 2 * band_keys
    keep_part, send_part = scatter_split(scatter, left, back_order[0])
    from_left, from_right, got = exchange(
        given(strips_from, strips_from + strip_keys).astype(jnp.bfloat16),
        given(strips_from + strip_keys, frame_keys).astype(jnp.bfloat16),
        "cols",
        split_wide(send_part.reshape(-1, model_width)),
    )
    scatter = keep_part + join_wide(got).reshape(keep_part.shape)
    corner = RAD * RAD
    lower_rows = (RAD + tile_rows) * RAD

    def cols_placed(piece, height, at_right):
        piece = piece.astype(jnp.float32).reshape(height, RAD, model_width)
        pad = (tile_cols - RAD, 0) if at_right else (0, tile_cols - RAD)
        return jnp.pad(piece, ((0, 0), pad, (0, 0)))

    band_shape = (RAD, tile_cols, model_width)
    upper = (
        given(tokens, tokens + band_keys).reshape(band_shape)
        + cols_placed(from_left[:corner], RAD, False)
        + cols_placed(from_right[:corner], RAD, True)
    )
    lower = (
        given(tokens + band_keys, strips_from).reshape(band_shape)
        + cols_placed(from_left[lower_rows:], RAD, False)
        + cols_placed(from_right[lower_rows:], RAD, True)
    )
    keep_part, send_part = scatter_split(scatter, left, back_order[1])
    from_above, from_below, got = exchange(
        upper.reshape(-1, model_width).astype(jnp.bfloat16),
        lower.reshape(-1, model_width).astype(jnp.bfloat16),
        "rows",
        split_wide(send_part.reshape(-1, model_width)),
    )
    scatter = keep_part + join_wide(got).reshape(keep_part.shape)
    received = cols_placed(from_left[corner:lower_rows], tile_rows, False) + cols_placed(
        from_right[corner:lower_rows], tile_rows, True
    )
    received = received + jnp.pad(
        from_above.astype(jnp.float32).reshape(band_shape), ((0, tile_rows - RAD), (0, 0), (0, 0))
    )
    received = received + jnp.pad(
        from_below.astype(jnp.float32).reshape(band_shape), ((tile_rows - RAD, 0), (0, 0), (0, 0))
    )
    for position in back_order[2:]:
        keep_part, send_part = scatter_split(scatter, left, position)
        scatter = keep_part + partner(send_part, position)
    own_grads = scatter.reshape(2, 1, model_width)

    own_given = given(0, tokens)
    own_row = (lax.dynamic_slice_in_dim(wide_grads, own_local, 1, 1) + own_grads).astype(
        jnp.bfloat16
    )
    own_row_given = jnp.dot(own_row[0], w_key.T, preferred_element_type=jnp.float32) + jnp.dot(
        own_row[1], w_value.T, preferred_element_type=jnp.float32
    )
    own_given = lax.dynamic_update_slice_in_dim(own_given, own_row_given, own_local, 0)

    grad_in = (
        jnp.dot(query_grads, w_query.T, preferred_element_type=jnp.float32)
        + own_given
        + received.reshape(tokens, model_width)
    )
    grad_in = grad_in.astype(jnp.bfloat16).reshape(features.shape)
    return (layer_out, grad_in)


def solution(mesh):
    placed = (P("rows", "cols", None), P(), P(), P(), P(), P(), P("rows", "cols", None))
    return jax.shard_map(
        shards,
        mesh=mesh,
        in_specs=placed,
        out_specs=(P("rows", "cols", None), P("rows", "cols", None)),
        check_vma=False,
    )
```

```python
import functools
import math

import jax
import jax.numpy as jnp
import numpy as np
from jax import lax
from jax.experimental import pallas as pl
from jax.sharding import PartitionSpec as P

HEADS = 16
KW = 13
RAD = 6


def bits(n):
    return n.bit_length() - 1


def device_bit(position):
    col_bits = bits(lax.axis_size("cols"))
    if position < col_bits:
        return "cols", position
    return "rows", position - col_bits


def own_bit(position):
    axis, bit = device_bit(position)
    return (lax.axis_index(axis) >> bit) % 2


def partner(x, position):
    axis, bit = device_bit(position)
    size = lax.axis_size(axis)
    return lax.ppermute(x, axis, [(i, i ^ (1 << bit)) for i in range(size)])


def exchange(to_lower, to_higher, axis, rider=None, rider_dim=0):
    size = lax.axis_size(axis)
    even = lax.axis_index(axis) % 2 == 0
    first = jnp.where(even, to_higher, to_lower)
    length = first.shape[rider_dim]
    if rider is not None:
        first = jnp.concatenate([first, rider], axis=rider_dim)
    got_first = lax.ppermute(first, axis, [(i, i ^ 1) for i in range(size)])
    links = [(i, i + 1) for i in range(1, size - 1, 2)] + [(i, i - 1) for i in range(2, size, 2)]
    got_second = lax.ppermute(jnp.where(even, to_lower, to_higher), axis, links)
    rider_got = None
    if rider is not None:
        rider_got = lax.slice_in_dim(got_first, length, None, axis=rider_dim)
        got_first = lax.slice_in_dim(got_first, 0, length, axis=rider_dim)
    from_lower = jnp.where(even, got_second, got_first)
    from_higher = jnp.where(even, got_first, got_second)
    return from_lower, from_higher, rider_got


def gather_step(x, other, position):
    low = own_bit(position) == 0
    return jnp.where(low, jnp.concatenate([x, other]), jnp.concatenate([other, x]))


def gather_order(order, count):
    where = np.zeros(count, np.int32)
    for l in range(count):
        where[l] = sum(((l >> bit) & 1) << step for step, bit in enumerate(order))
    return where


def scatter_split(x, order_left, position):
    axis = 1 + order_left.index(position)
    high = own_bit(position) == 1
    lower = lax.index_in_dim(x, 0, axis, keepdims=False)
    upper = lax.index_in_dim(x, 1, axis, keepdims=False)
    order_left.remove(position)
    return jnp.where(high, upper, lower), jnp.where(high, lower, upper)


def attention_kernel(
    own, first, last, q_ref, ko_ref, kh_ref, kg_ref, vo_ref, vh_ref, vg_ref, g_ref, mask_ref,
    o_ref, dq_ref, dkv_ref, wide_ref,
):
    head_size = q_ref.shape[1] // 2
    score_scale = 1.0 / math.sqrt(head_size)
    q = q_ref[...]
    k = jnp.concatenate([ko_ref[...], kh_ref[...], kg_ref[...]], axis=0)
    v = jnp.concatenate([vo_ref[...], vh_ref[...], vg_ref[...]], axis=0)
    g = g_ref[...]
    keep = mask_ref[...] > 0
    lane_head = lax.broadcasted_iota(jnp.int32, q.shape, 1) // head_size
    lane_head_keys = lax.broadcasted_iota(jnp.int32, k.shape, 1) // head_size
    rows = (((1,), (1,)), ((), ()))
    cols = (((0,), (0,)), ((), ()))
    out = jnp.zeros(q.shape, jnp.float32)
    dq = jnp.zeros(q.shape, jnp.float32)
    dk = jnp.zeros(k.shape, jnp.float32)
    dv = jnp.zeros(k.shape, jnp.float32)
    for head in range(2):
        mine = lane_head == head
        mine_keys = lane_head_keys == head
        q_head = jnp.where(mine, q, jnp.zeros_like(q))
        g_head = jnp.where(mine, g, jnp.zeros_like(g))
        scores = lax.dot_general(q_head, k, rows, preferred_element_type=jnp.float32) * score_scale
        scores = jnp.where(keep, scores, -1e30)
        row_max = jnp.max(scores, axis=1, keepdims=True)
        exps = jnp.exp(scores - row_max)
        probs = exps * (1.0 / jnp.sum(exps, axis=1, keepdims=True))
        rounded = probs.astype(jnp.bfloat16)
        attended = jnp.dot(rounded, v, preferred_element_type=jnp.float32)
        attended = attended.astype(jnp.bfloat16).astype(jnp.float32)
        out = jnp.where(mine, attended, out)
        delta = jnp.sum(
            jnp.where(mine, g.astype(jnp.float32) * attended, 0.0), axis=1, keepdims=True
        )
        dots = lax.dot_general(g_head, v, rows, preferred_element_type=jnp.float32)
        slopes = (probs * (dots - delta) * score_scale).astype(jnp.bfloat16)
        dq = jnp.where(mine, jnp.dot(slopes, k, preferred_element_type=jnp.float32), dq)
        dk = jnp.where(
            mine_keys, lax.dot_general(slopes, q, cols, preferred_element_type=jnp.float32), dk
        )
        dv = jnp.where(
            mine_keys, lax.dot_general(rounded, g, cols, preferred_element_type=jnp.float32), dv
        )
    o_ref[...] = out.astype(o_ref.dtype)
    dq_ref[...] = dq.astype(dq_ref.dtype)
    dkv_ref[0] = dk.astype(dkv_ref.dtype)
    dkv_ref[1] = dv.astype(dkv_ref.dtype)
    wide_ref[0, :own] = dk[:own]
    wide_ref[1, :own] = dv[:own]
    wide_ref[0, own:] = dk[first:last]
    wide_ref[1, own:] = dv[first:last]


def attention(queries, keys, values, global_keys, global_values, grad_attended, keep):
    tokens, model_width = queries.shape
    first = keys[0].shape[0] + keys[1].shape[0]
    last = first + global_keys.shape[0]
    key_count = last
    lanes = 2 * (model_width // HEADS)
    steps = model_width // lanes
    token_block = pl.BlockSpec((tokens, lanes), lambda i: (0, i))
    key_block = pl.BlockSpec((key_count, lanes), lambda i: (0, i))
    own_block = pl.BlockSpec((keys[0].shape[0], lanes), lambda i: (0, i))
    halo_block = pl.BlockSpec((keys[1].shape[0], lanes), lambda i: (0, i))
    global_block = pl.BlockSpec((last - first, lanes), lambda i: (0, i))
    mask_block = pl.BlockSpec((tokens, key_count), lambda i: (0, 0))
    grads_block = pl.BlockSpec((2, key_count, lanes), lambda i: (0, 0, i))
    wide_rows = tokens + last - first
    wide_block = pl.BlockSpec((2, wide_rows, lanes), lambda i: (0, 0, i))
    flops = 2 * 2 * 6 * tokens * key_count * model_width
    moved = 2 * (3 * tokens * model_width + 2 * key_count * model_width) + 4 * (
        tokens * key_count + 2 * key_count * model_width
    )
    return pl.pallas_call(
        functools.partial(attention_kernel, tokens, first, last),
        grid=(steps,),
        in_specs=[
            token_block,
            own_block,
            halo_block,
            global_block,
            own_block,
            halo_block,
            global_block,
            token_block,
            mask_block,
        ],
        out_specs=[token_block, token_block, grads_block, wide_block],
        out_shape=[
            jax.ShapeDtypeStruct((tokens, model_width), jnp.bfloat16),
            jax.ShapeDtypeStruct((tokens, model_width), jnp.bfloat16),
            jax.ShapeDtypeStruct((2, key_count, model_width), jnp.bfloat16),
            jax.ShapeDtypeStruct((2, wide_rows, model_width), jnp.float32),
        ],
        cost_estimate=pl.CostEstimate(
            flops=flops, transcendentals=HEADS * tokens * key_count, bytes_accessed=moved
        ),
    )(queries, *keys, global_keys, *values, global_values, grad_attended, keep)


def split_wide(x):
    high = x.astype(jnp.bfloat16)
    low = (x - high.astype(jnp.float32)).astype(jnp.bfloat16)
    return jnp.concatenate([high, low], axis=0)


def join_wide(pair):
    half = pair.shape[0] // 2
    return pair[:half].astype(jnp.float32) + pair[half:].astype(jnp.float32)


def shards(features, w_query, w_key, w_value, w_out, reg_pos, grad_out):
    tile_rows, tile_cols, model_width = features.shape
    row_count = lax.axis_size("rows")
    col_count = lax.axis_size("cols")
    row_index = lax.axis_index("rows")
    col_index = lax.axis_index("cols")
    band_rows = tile_rows * row_count
    band_cols = tile_cols * col_count
    first_row = row_index * tile_rows
    first_col = col_index * tile_cols
    tokens = tile_rows * tile_cols
    device_count = row_count * col_count
    col_bits = bits(col_count)
    all_bits = col_bits + bits(row_count)
    ext_rows = tile_rows + 2 * RAD
    band_keys = RAD * tile_cols
    strip_keys = ext_rows * RAD
    frame_keys = tokens + 2 * band_keys + 2 * strip_keys
    used = frame_keys + device_count
    key_count = -(-used // 128) * 128

    flat_tokens = features.reshape(-1, model_width)
    own_keys = jnp.dot(flat_tokens, w_key, preferred_element_type=jnp.float32).astype(jnp.bfloat16)
    own_values = jnp.dot(flat_tokens, w_value, preferred_element_type=jnp.float32).astype(
        jnp.bfloat16
    )

    own_index = row_index * col_count + col_index
    own_place = lax.dynamic_index_in_dim(reg_pos, own_index, 0, keepdims=False)
    own_local = (own_place // band_cols - first_row) * tile_cols + (own_place % band_cols - first_col)
    gathered = jnp.concatenate(
        [
            lax.dynamic_slice_in_dim(own_keys, own_local, 1, 0),
            lax.dynamic_slice_in_dim(own_values, own_local, 1, 0),
        ],
        axis=1,
    )
    order = [col_bits, 0] + list(range(1, col_bits)) + list(range(col_bits + 1, all_bits))

    from_above, from_below, got = exchange(
        features[:RAD].reshape(-1, model_width),
        features[tile_rows - RAD :].reshape(-1, model_width),
        "rows",
        gathered.reshape(-1, model_width),
    )
    gathered = gather_step(gathered, got.reshape(gathered.shape), order[0])
    extended = jnp.concatenate(
        [
            from_above.reshape(RAD, tile_cols, model_width),
            features,
            from_below.reshape(RAD, tile_cols, model_width),
        ],
        axis=0,
    )
    from_left, from_right, got = exchange(
        extended[:, :RAD].reshape(-1, model_width),
        extended[:, tile_cols - RAD :].reshape(-1, model_width),
        "cols",
        gathered.reshape(-1, model_width),
    )
    gathered = gather_step(gathered, got.reshape(gathered.shape), order[1])

    queries = jnp.dot(flat_tokens, w_query, preferred_element_type=jnp.float32).astype(jnp.bfloat16)
    grad_attended = jnp.dot(
        grad_out.reshape(-1, model_width), w_out.T, preferred_element_type=jnp.float32
    ).astype(jnp.bfloat16)

    halo_features = jnp.concatenate(
        [
            from_above,
            from_below,
            from_left,
            from_right,
            jnp.zeros((key_count - used, model_width), features.dtype),
        ],
        axis=0,
    )
    halo_keys = jnp.dot(halo_features, w_key, preferred_element_type=jnp.float32).astype(
        jnp.bfloat16
    )
    halo_values = jnp.dot(halo_features, w_value, preferred_element_type=jnp.float32).astype(
        jnp.bfloat16
    )

    for position in order[2:]:
        gathered = gather_step(gathered, partner(gathered, position), position)
    global_kv = jnp.take(gathered, jnp.asarray(gather_order(order, device_count)), axis=0)
    global_keys = global_kv[:, :model_width]
    global_values = global_kv[:, model_width:]

    def grid(height, width, row0, col0):
        a, b = np.meshgrid(np.arange(height) + row0, np.arange(width) + col0, indexing="ij")
        return a.reshape(-1), b.reshape(-1)

    parts = [
        grid(tile_rows, tile_cols, RAD, RAD),
        grid(RAD, tile_cols, 0, RAD),
        grid(RAD, tile_cols, RAD + tile_rows, RAD),
        grid(ext_rows, RAD, 0, 0),
        grid(ext_rows, RAD, 0, RAD + tile_cols),
    ]
    key_rows = np.zeros(key_count, np.int32)
    key_cols = np.zeros(key_count, np.int32)
    key_rows[:frame_keys] = np.concatenate([p[0] for p in parts])
    key_cols[:frame_keys] = np.concatenate([p[1] for p in parts])
    kind = np.full(key_count, 2, np.int32)
    kind[:frame_keys] = 0
    kind[key_count - device_count :] = 1

    query_rows = first_row + jnp.repeat(jnp.arange(tile_rows, dtype=jnp.int32), tile_cols)
    query_cols = first_col + jnp.tile(jnp.arange(tile_cols, dtype=jnp.int32), tile_rows)
    start_rows = jnp.clip(query_rows - RAD, 0, band_rows - KW)[:, None]
    start_cols = jnp.clip(query_cols - RAD, 0, band_cols - KW)[:, None]
    cell_rows = (first_row - RAD + jnp.asarray(key_rows))[None, :]
    cell_cols = (first_col - RAD + jnp.asarray(key_cols))[None, :]
    inside = (
        (cell_rows >= start_rows)
        & (cell_rows < start_rows + KW)
        & (cell_cols >= start_cols)
        & (cell_cols < start_cols + KW)
    )
    key_kind = jnp.asarray(kind)[None, :]
    keep = ((inside & (key_kind == 0)) | (key_kind == 1)).astype(jnp.float32)

    attended, query_grads, rounded_grads, wide_grads = attention(
        queries,
        (own_keys, halo_keys),
        (own_values, halo_values),
        global_keys,
        global_values,
        grad_attended,
        keep,
    )
    layer_out = (
        jnp.dot(attended, w_out, preferred_element_type=jnp.float32)
        .astype(jnp.bfloat16)
        .reshape(features.shape)
    )

    given_all = jnp.dot(
        rounded_grads[0, :frame_keys], w_key.T, preferred_element_type=jnp.float32
    ) + jnp.dot(rounded_grads[1, :frame_keys], w_value.T, preferred_element_type=jnp.float32)

    def given(lo, hi):
        return given_all[lo:hi]

    scatter = wide_grads[:, tokens:].reshape(
        (2,) + (2,) * all_bits + (model_width,)
    )
    left = list(range(all_bits - 1, -1, -1))
    back_order = [0, col_bits] + list(range(1, col_bits)) + list(range(col_bits + 1, all_bits))

    strips_from = tokens + 2 * band_keys
    keep_part, send_part = scatter_split(scatter, left, back_order[0])
    strip_shape = (ext_rows, RAD, model_width)
    from_left, from_right, got = exchange(
        given(strips_from, strips_from + strip_keys).astype(jnp.bfloat16),
        given(strips_from + strip_keys, frame_keys).astype(jnp.bfloat16),
        "cols",
        split_wide(send_part.reshape(-1, model_width)),
    )
    scatter = keep_part + join_wide(got).reshape(keep_part.shape)
    received = jnp.pad(
        from_left.astype(jnp.float32).reshape(strip_shape), ((0, 0), (0, tile_cols - RAD), (0, 0))
    ) + jnp.pad(
        from_right.astype(jnp.float32).reshape(strip_shape), ((0, 0), (tile_cols - RAD, 0), (0, 0))
    )
    band_shape = (RAD, tile_cols, model_width)
    keep_part, send_part = scatter_split(scatter, left, back_order[1])
    from_above, from_below, got = exchange(
        (given(tokens, tokens + band_keys).reshape(band_shape) + received[:RAD])
        .reshape(-1, model_width)
        .astype(jnp.bfloat16),
        (given(tokens + band_keys, strips_from).reshape(band_shape) + received[RAD + tile_rows :])
        .reshape(-1, model_width)
        .astype(jnp.bfloat16),
        "rows",
        split_wide(send_part.reshape(-1, model_width)),
    )
    scatter = keep_part + join_wide(got).reshape(keep_part.shape)
    received = received[RAD : RAD + tile_rows]
    received = received + jnp.pad(
        from_above.astype(jnp.float32).reshape(band_shape), ((0, tile_rows - RAD), (0, 0), (0, 0))
    )
    received = received + jnp.pad(
        from_below.astype(jnp.float32).reshape(band_shape), ((tile_rows - RAD, 0), (0, 0), (0, 0))
    )
    for position in back_order[2:]:
        keep_part, send_part = scatter_split(scatter, left, position)
        scatter = keep_part + partner(send_part, position)
    own_grads = scatter.reshape(2, 1, model_width)

    own_given = given(0, tokens)
    own_row = (lax.dynamic_slice_in_dim(wide_grads, own_local, 1, 1) + own_grads).astype(
        jnp.bfloat16
    )
    own_row_given = jnp.dot(own_row[0], w_key.T, preferred_element_type=jnp.float32) + jnp.dot(
        own_row[1], w_value.T, preferred_element_type=jnp.float32
    )
    own_given = lax.dynamic_update_slice_in_dim(own_given, own_row_given, own_local, 0)

    grad_in = (
        jnp.dot(query_grads, w_query.T, preferred_element_type=jnp.float32)
        + own_given
        + received.reshape(tokens, model_width)
    )
    grad_in = grad_in.astype(jnp.bfloat16).reshape(features.shape)
    return (layer_out, grad_in)


def solution(mesh):
    placed = (P("rows", "cols", None), P(), P(), P(), P(), P(), P("rows", "cols", None))
    return jax.shard_map(
        shards,
        mesh=mesh,
        in_specs=placed,
        out_specs=(P("rows", "cols", None), P("rows", "cols", None)),
        check_vma=False,
    )
```

```python
import functools
import math

import jax
import jax.numpy as jnp
import numpy as np
from jax import lax
from jax.experimental import pallas as pl
from jax.sharding import PartitionSpec as P

HEADS = 16
KW = 13
RAD = 6


def bits(n):
    return n.bit_length() - 1


def device_bit(position):
    col_bits = bits(lax.axis_size("cols"))
    if position < col_bits:
        return "cols", position
    return "rows", position - col_bits


def own_bit(position):
    axis, bit = device_bit(position)
    return (lax.axis_index(axis) >> bit) % 2


def partner(x, position):
    axis, bit = device_bit(position)
    size = lax.axis_size(axis)
    return lax.ppermute(x, axis, [(i, i ^ (1 << bit)) for i in range(size)])


def exchange(to_lower, to_higher, axis, rider=None, rider_dim=0):
    size = lax.axis_size(axis)
    even = lax.axis_index(axis) % 2 == 0
    first = jnp.where(even, to_higher, to_lower)
    length = first.shape[rider_dim]
    if rider is not None:
        first = jnp.concatenate([first, rider], axis=rider_dim)
    got_first = lax.ppermute(first, axis, [(i, i ^ 1) for i in range(size)])
    links = [(i, i + 1) for i in range(1, size - 1, 2)] + [(i, i - 1) for i in range(2, size, 2)]
    got_second = lax.ppermute(jnp.where(even, to_lower, to_higher), axis, links)
    rider_got = None
    if rider is not None:
        rider_got = lax.slice_in_dim(got_first, length, None, axis=rider_dim)
        got_first = lax.slice_in_dim(got_first, 0, length, axis=rider_dim)
    from_lower = jnp.where(even, got_second, got_first)
    from_higher = jnp.where(even, got_first, got_second)
    return from_lower, from_higher, rider_got


def gather_step(x, other, position):
    low = own_bit(position) == 0
    return jnp.where(low, jnp.concatenate([x, other]), jnp.concatenate([other, x]))


def gather_order(order, count):
    where = np.zeros(count, np.int32)
    for l in range(count):
        where[l] = sum(((l >> bit) & 1) << step for step, bit in enumerate(order))
    return where


def scatter_split(x, order_left, position):
    axis = 1 + order_left.index(position)
    high = own_bit(position) == 1
    lower = lax.index_in_dim(x, 0, axis, keepdims=False)
    upper = lax.index_in_dim(x, 1, axis, keepdims=False)
    order_left.remove(position)
    return jnp.where(high, upper, lower), jnp.where(high, lower, upper)


def attention_kernel(
    own, first, last, q_ref, ko_ref, kh_ref, kg_ref, vo_ref, vh_ref, vg_ref, g_ref, mask_ref,
    o_ref, dq_ref, dkv_ref, wide_ref,
):
    head_size = q_ref.shape[1] // 2
    score_scale = 1.0 / math.sqrt(head_size)
    q = (q_ref[...] * score_scale).astype(q_ref.dtype)
    k = jnp.concatenate([ko_ref[...], kh_ref[...], kg_ref[...]], axis=0)
    v = jnp.concatenate([vo_ref[...], vh_ref[...], vg_ref[...]], axis=0)
    g = g_ref[...]
    keep = mask_ref[...] > 0
    lane_head = lax.broadcasted_iota(jnp.int32, q.shape, 1) // head_size
    rows = (((1,), (1,)), ((), ()))
    cols = (((0,), (0,)), ((), ()))
    out = jnp.zeros(q.shape, jnp.float32)
    dq = jnp.zeros(q.shape, jnp.float32)
    dk = None
    dv = None
    for head in range(2):
        mine = lane_head == head
        q_head = jnp.where(mine, q, jnp.zeros_like(q))
        g_head = jnp.where(mine, g, jnp.zeros_like(g))
        scores = lax.dot_general(q_head, k, rows, preferred_element_type=jnp.float32)
        scores = jnp.where(keep, scores, -1e30)
        row_max = jnp.max(scores, axis=1, keepdims=True)
        exps = jnp.exp(scores - row_max)
        probs = exps * (1.0 / jnp.sum(exps, axis=1, keepdims=True))
        rounded = probs.astype(jnp.bfloat16)
        attended = jnp.dot(rounded, v, preferred_element_type=jnp.float32)
        attended = attended.astype(jnp.bfloat16).astype(jnp.float32)
        out = jnp.where(mine, attended, out)
        delta = jnp.sum(
            jnp.where(mine, g.astype(jnp.float32) * attended, 0.0), axis=1, keepdims=True
        )
        dots = lax.dot_general(g_head, v, rows, preferred_element_type=jnp.float32)
        slopes = (probs * (dots - delta)).astype(jnp.bfloat16)
        dq = jnp.where(
            mine, jnp.dot(slopes, k, preferred_element_type=jnp.float32) * score_scale, dq
        )
        dk_head = lax.dot_general(slopes, q_head, cols, preferred_element_type=jnp.float32)
        dv_head = lax.dot_general(rounded, g_head, cols, preferred_element_type=jnp.float32)
        dk = dk_head if dk is None else dk + dk_head
        dv = dv_head if dv is None else dv + dv_head
    o_ref[...] = out.astype(o_ref.dtype)
    dq_ref[...] = dq.astype(dq_ref.dtype)
    dkv_ref[0] = dk.astype(dkv_ref.dtype)
    dkv_ref[1] = dv.astype(dkv_ref.dtype)
    wide_ref[0, :own] = dk[:own]
    wide_ref[1, :own] = dv[:own]
    wide_ref[0, own:] = dk[first:last]
    wide_ref[1, own:] = dv[first:last]


def attention(queries, keys, values, global_keys, global_values, grad_attended, keep):
    tokens, model_width = queries.shape
    first = keys[0].shape[0] + keys[1].shape[0]
    last = first + global_keys.shape[0]
    key_count = last
    lanes = 2 * (model_width // HEADS)
    steps = model_width // lanes
    token_block = pl.BlockSpec((tokens, lanes), lambda i: (0, i))
    key_block = pl.BlockSpec((key_count, lanes), lambda i: (0, i))
    own_block = pl.BlockSpec((keys[0].shape[0], lanes), lambda i: (0, i))
    halo_block = pl.BlockSpec((keys[1].shape[0], lanes), lambda i: (0, i))
    global_block = pl.BlockSpec((last - first, lanes), lambda i: (0, i))
    mask_block = pl.BlockSpec((tokens, key_count), lambda i: (0, 0))
    grads_block = pl.BlockSpec((2, key_count, lanes), lambda i: (0, 0, i))
    wide_rows = tokens + last - first
    wide_block = pl.BlockSpec((2, wide_rows, lanes), lambda i: (0, 0, i))
    flops = 2 * 2 * 6 * tokens * key_count * model_width
    moved = 2 * (3 * tokens * model_width + 2 * key_count * model_width) + 4 * (
        tokens * key_count + 2 * key_count * model_width
    )
    return pl.pallas_call(
        functools.partial(attention_kernel, tokens, first, last),
        grid=(steps,),
        in_specs=[
            token_block,
            own_block,
            halo_block,
            global_block,
            own_block,
            halo_block,
            global_block,
            token_block,
            mask_block,
        ],
        out_specs=[token_block, token_block, grads_block, wide_block],
        out_shape=[
            jax.ShapeDtypeStruct((tokens, model_width), jnp.bfloat16),
            jax.ShapeDtypeStruct((tokens, model_width), jnp.bfloat16),
            jax.ShapeDtypeStruct((2, key_count, model_width), jnp.bfloat16),
            jax.ShapeDtypeStruct((2, wide_rows, model_width), jnp.float32),
        ],
        cost_estimate=pl.CostEstimate(
            flops=flops, transcendentals=HEADS * tokens * key_count, bytes_accessed=moved
        ),
    )(queries, *keys, global_keys, *values, global_values, grad_attended, keep)


def split_wide(x):
    high = x.astype(jnp.bfloat16)
    low = (x - high.astype(jnp.float32)).astype(jnp.bfloat16)
    return jnp.concatenate([high, low], axis=0)


def join_wide(pair):
    half = pair.shape[0] // 2
    return pair[:half].astype(jnp.float32) + pair[half:].astype(jnp.float32)


def shards(features, w_query, w_key, w_value, w_out, reg_pos, grad_out):
    tile_rows, tile_cols, model_width = features.shape
    row_count = lax.axis_size("rows")
    col_count = lax.axis_size("cols")
    row_index = lax.axis_index("rows")
    col_index = lax.axis_index("cols")
    band_rows = tile_rows * row_count
    band_cols = tile_cols * col_count
    first_row = row_index * tile_rows
    first_col = col_index * tile_cols
    tokens = tile_rows * tile_cols
    device_count = row_count * col_count
    col_bits = bits(col_count)
    all_bits = col_bits + bits(row_count)
    ext_rows = tile_rows + 2 * RAD
    band_keys = RAD * tile_cols
    strip_keys = ext_rows * RAD
    frame_keys = tokens + 2 * band_keys + 2 * strip_keys
    used = frame_keys + device_count
    key_count = -(-used // 128) * 128

    flat_tokens = features.reshape(-1, model_width)
    own_keys = jnp.dot(flat_tokens, w_key, preferred_element_type=jnp.float32).astype(jnp.bfloat16)
    own_values = jnp.dot(flat_tokens, w_value, preferred_element_type=jnp.float32).astype(
        jnp.bfloat16
    )

    own_index = row_index * col_count + col_index
    own_place = lax.dynamic_index_in_dim(reg_pos, own_index, 0, keepdims=False)
    own_local = (own_place // band_cols - first_row) * tile_cols + (own_place % band_cols - first_col)
    gathered = jnp.concatenate(
        [
            lax.dynamic_slice_in_dim(own_keys, own_local, 1, 0),
            lax.dynamic_slice_in_dim(own_values, own_local, 1, 0),
        ],
        axis=1,
    )
    order = [col_bits, 0] + list(range(1, col_bits)) + list(range(col_bits + 1, all_bits))

    from_above, from_below, got = exchange(
        features[:RAD].reshape(-1, model_width),
        features[tile_rows - RAD :].reshape(-1, model_width),
        "rows",
        gathered.reshape(-1, model_width),
    )
    gathered = gather_step(gathered, got.reshape(gathered.shape), order[0])
    extended = jnp.concatenate(
        [
            from_above.reshape(RAD, tile_cols, model_width),
            features,
            from_below.reshape(RAD, tile_cols, model_width),
        ],
        axis=0,
    )
    from_left, from_right, got = exchange(
        extended[:, :RAD].reshape(-1, model_width),
        extended[:, tile_cols - RAD :].reshape(-1, model_width),
        "cols",
        gathered.reshape(-1, model_width),
    )
    gathered = gather_step(gathered, got.reshape(gathered.shape), order[1])

    queries = jnp.dot(flat_tokens, w_query, preferred_element_type=jnp.float32).astype(jnp.bfloat16)
    grad_attended = jnp.dot(
        grad_out.reshape(-1, model_width), w_out.T, preferred_element_type=jnp.float32
    ).astype(jnp.bfloat16)

    halo_features = jnp.concatenate(
        [
            from_above,
            from_below,
            from_left,
            from_right,
            jnp.zeros((key_count - used, model_width), features.dtype),
        ],
        axis=0,
    )
    halo_keys = jnp.dot(halo_features, w_key, preferred_element_type=jnp.float32).astype(
        jnp.bfloat16
    )
    halo_values = jnp.dot(halo_features, w_value, preferred_element_type=jnp.float32).astype(
        jnp.bfloat16
    )

    for position in order[2:]:
        gathered = gather_step(gathered, partner(gathered, position), position)
    global_kv = jnp.take(gathered, jnp.asarray(gather_order(order, device_count)), axis=0)
    global_keys = global_kv[:, :model_width]
    global_values = global_kv[:, model_width:]

    def grid(height, width, row0, col0):
        a, b = np.meshgrid(np.arange(height) + row0, np.arange(width) + col0, indexing="ij")
        return a.reshape(-1), b.reshape(-1)

    parts = [
        grid(tile_rows, tile_cols, RAD, RAD),
        grid(RAD, tile_cols, 0, RAD),
        grid(RAD, tile_cols, RAD + tile_rows, RAD),
        grid(ext_rows, RAD, 0, 0),
        grid(ext_rows, RAD, 0, RAD + tile_cols),
    ]
    key_rows = np.zeros(key_count, np.int32)
    key_cols = np.zeros(key_count, np.int32)
    key_rows[:frame_keys] = np.concatenate([p[0] for p in parts])
    key_cols[:frame_keys] = np.concatenate([p[1] for p in parts])
    kind = np.full(key_count, 2, np.int32)
    kind[:frame_keys] = 0
    kind[key_count - device_count :] = 1

    query_rows = first_row + jnp.repeat(jnp.arange(tile_rows, dtype=jnp.int32), tile_cols)
    query_cols = first_col + jnp.tile(jnp.arange(tile_cols, dtype=jnp.int32), tile_rows)
    start_rows = jnp.clip(query_rows - RAD, 0, band_rows - KW)[:, None]
    start_cols = jnp.clip(query_cols - RAD, 0, band_cols - KW)[:, None]
    cell_rows = (first_row - RAD + jnp.asarray(key_rows))[None, :]
    cell_cols = (first_col - RAD + jnp.asarray(key_cols))[None, :]
    inside = (
        (cell_rows >= start_rows)
        & (cell_rows < start_rows + KW)
        & (cell_cols >= start_cols)
        & (cell_cols < start_cols + KW)
    )
    key_kind = jnp.asarray(kind)[None, :]
    keep = ((inside & (key_kind == 0)) | (key_kind == 1)).astype(jnp.float32)

    attended, query_grads, rounded_grads, wide_grads = attention(
        queries,
        (own_keys, halo_keys),
        (own_values, halo_values),
        global_keys,
        global_values,
        grad_attended,
        keep,
    )
    layer_out = (
        jnp.dot(attended, w_out, preferred_element_type=jnp.float32)
        .astype(jnp.bfloat16)
        .reshape(features.shape)
    )

    given_all = jnp.dot(
        rounded_grads[0, :frame_keys], w_key.T, preferred_element_type=jnp.float32
    ) + jnp.dot(rounded_grads[1, :frame_keys], w_value.T, preferred_element_type=jnp.float32)

    def given(lo, hi):
        return given_all[lo:hi]

    scatter = wide_grads[:, tokens:].reshape(
        (2,) + (2,) * all_bits + (model_width,)
    )
    left = list(range(all_bits - 1, -1, -1))
    back_order = [0, col_bits] + list(range(1, col_bits)) + list(range(col_bits + 1, all_bits))

    strips_from = tokens + 2 * band_keys
    keep_part, send_part = scatter_split(scatter, left, back_order[0])
    strip_shape = (ext_rows, RAD, model_width)
    from_left, from_right, got = exchange(
        given(strips_from, strips_from + strip_keys).astype(jnp.bfloat16),
        given(strips_from + strip_keys, frame_keys).astype(jnp.bfloat16),
        "cols",
        split_wide(send_part.reshape(-1, model_width)),
    )
    scatter = keep_part + join_wide(got).reshape(keep_part.shape)
    received = jnp.pad(
        from_left.astype(jnp.float32).reshape(strip_shape), ((0, 0), (0, tile_cols - RAD), (0, 0))
    ) + jnp.pad(
        from_right.astype(jnp.float32).reshape(strip_shape), ((0, 0), (tile_cols - RAD, 0), (0, 0))
    )
    band_shape = (RAD, tile_cols, model_width)
    keep_part, send_part = scatter_split(scatter, left, back_order[1])
    from_above, from_below, got = exchange(
        (given(tokens, tokens + band_keys).reshape(band_shape) + received[:RAD])
        .reshape(-1, model_width)
        .astype(jnp.bfloat16),
        (given(tokens + band_keys, strips_from).reshape(band_shape) + received[RAD + tile_rows :])
        .reshape(-1, model_width)
        .astype(jnp.bfloat16),
        "rows",
        split_wide(send_part.reshape(-1, model_width)),
    )
    scatter = keep_part + join_wide(got).reshape(keep_part.shape)
    received = received[RAD : RAD + tile_rows]
    received = received + jnp.pad(
        from_above.astype(jnp.float32).reshape(band_shape), ((0, tile_rows - RAD), (0, 0), (0, 0))
    )
    received = received + jnp.pad(
        from_below.astype(jnp.float32).reshape(band_shape), ((tile_rows - RAD, 0), (0, 0), (0, 0))
    )
    for position in back_order[2:]:
        keep_part, send_part = scatter_split(scatter, left, position)
        scatter = keep_part + partner(send_part, position)
    own_grads = scatter.reshape(2, 1, model_width)

    own_given = given(0, tokens)
    own_row = (lax.dynamic_slice_in_dim(wide_grads, own_local, 1, 1) + own_grads).astype(
        jnp.bfloat16
    )
    own_row_given = jnp.dot(own_row[0], w_key.T, preferred_element_type=jnp.float32) + jnp.dot(
        own_row[1], w_value.T, preferred_element_type=jnp.float32
    )
    own_given = lax.dynamic_update_slice_in_dim(own_given, own_row_given, own_local, 0)

    grad_in = (
        jnp.dot(query_grads, w_query.T, preferred_element_type=jnp.float32)
        + own_given
        + received.reshape(tokens, model_width)
    )
    grad_in = grad_in.astype(jnp.bfloat16).reshape(features.shape)
    return (layer_out, grad_in)


def solution(mesh):
    placed = (P("rows", "cols", None), P(), P(), P(), P(), P(), P("rows", "cols", None))
    return jax.shard_map(
        shards,
        mesh=mesh,
        in_specs=placed,
        out_specs=(P("rows", "cols", None), P("rows", "cols", None)),
        check_vma=False,
    )
```

```python
import functools
import math

import jax
import jax.numpy as jnp
import numpy as np
from jax import lax
from jax.experimental import pallas as pl
from jax.sharding import PartitionSpec as P

HEADS = 16
KW = 13
RAD = 6


def bits(n):
    return n.bit_length() - 1


def device_bit(position):
    col_bits = bits(lax.axis_size("cols"))
    if position < col_bits:
        return "cols", position
    return "rows", position - col_bits


def own_bit(position):
    axis, bit = device_bit(position)
    return (lax.axis_index(axis) >> bit) % 2


def partner(x, position):
    axis, bit = device_bit(position)
    size = lax.axis_size(axis)
    return lax.ppermute(x, axis, [(i, i ^ (1 << bit)) for i in range(size)])


def exchange(to_lower, to_higher, axis, rider=None, rider_dim=0):
    size = lax.axis_size(axis)
    even = lax.axis_index(axis) % 2 == 0
    length = to_higher.shape[rider_dim]
    if rider is not None:
        to_higher = jnp.concatenate([to_higher, rider], axis=rider_dim)
        to_lower = jnp.concatenate([to_lower, rider], axis=rider_dim)
    from_lower = lax.ppermute(to_higher, axis, [(i, i + 1) for i in range(size - 1)])
    from_higher = lax.ppermute(to_lower, axis, [(i + 1, i) for i in range(size - 1)])
    rider_got = None
    if rider is not None:
        rider_got = jnp.where(
            even,
            lax.slice_in_dim(from_higher, length, None, axis=rider_dim),
            lax.slice_in_dim(from_lower, length, None, axis=rider_dim),
        )
        from_lower = lax.slice_in_dim(from_lower, 0, length, axis=rider_dim)
        from_higher = lax.slice_in_dim(from_higher, 0, length, axis=rider_dim)
    return from_lower, from_higher, rider_got


def gather_step(x, other, position):
    low = own_bit(position) == 0
    return jnp.where(low, jnp.concatenate([x, other]), jnp.concatenate([other, x]))


def gather_order(order, count):
    where = np.zeros(count, np.int32)
    for l in range(count):
        where[l] = sum(((l >> bit) & 1) << step for step, bit in enumerate(order))
    return where


def scatter_split(x, order_left, position):
    axis = 1 + order_left.index(position)
    high = own_bit(position) == 1
    lower = lax.index_in_dim(x, 0, axis, keepdims=False)
    upper = lax.index_in_dim(x, 1, axis, keepdims=False)
    order_left.remove(position)
    return jnp.where(high, upper, lower), jnp.where(high, lower, upper)


def attention_kernel(
    own, first, last, q_ref, ko_ref, kh_ref, kg_ref, vo_ref, vh_ref, vg_ref, g_ref, mask_ref,
    o_ref, dq_ref, dkv_ref, wide_ref,
):
    head_size = q_ref.shape[1] // 2
    score_scale = 1.0 / math.sqrt(head_size)
    q = (q_ref[...] * score_scale).astype(q_ref.dtype)
    k = jnp.concatenate([ko_ref[...], kh_ref[...], kg_ref[...]], axis=0)
    v = jnp.concatenate([vo_ref[...], vh_ref[...], vg_ref[...]], axis=0)
    g = g_ref[...]
    keep = mask_ref[...] > 0
    lane_head = lax.broadcasted_iota(jnp.int32, q.shape, 1) // head_size
    rows = (((1,), (1,)), ((), ()))
    cols = (((0,), (0,)), ((), ()))
    out = jnp.zeros(q.shape, jnp.float32)
    dq = jnp.zeros(q.shape, jnp.float32)
    dk = None
    dv = None
    for head in range(2):
        mine = lane_head == head
        q_head = jnp.where(mine, q, jnp.zeros_like(q))
        g_head = jnp.where(mine, g, jnp.zeros_like(g))
        scores = lax.dot_general(q_head, k, rows, preferred_element_type=jnp.float32)
        scores = jnp.where(keep, scores, -1e30)
        row_max = jnp.max(scores, axis=1, keepdims=True)
        exps = jnp.exp(scores - row_max)
        probs = exps * (1.0 / jnp.sum(exps, axis=1, keepdims=True))
        rounded = probs.astype(jnp.bfloat16)
        attended = jnp.dot(rounded, v, preferred_element_type=jnp.float32)
        attended = attended.astype(jnp.bfloat16).astype(jnp.float32)
        out = jnp.where(mine, attended, out)
        delta = jnp.sum(
            jnp.where(mine, g.astype(jnp.float32) * attended, 0.0), axis=1, keepdims=True
        )
        dots = lax.dot_general(g_head, v, rows, preferred_element_type=jnp.float32)
        slopes = (probs * (dots - delta)).astype(jnp.bfloat16)
        dq = jnp.where(
            mine, jnp.dot(slopes, k, preferred_element_type=jnp.float32) * score_scale, dq
        )
        dk_head = lax.dot_general(slopes, q_head, cols, preferred_element_type=jnp.float32)
        dv_head = lax.dot_general(rounded, g_head, cols, preferred_element_type=jnp.float32)
        dk = dk_head if dk is None else dk + dk_head
        dv = dv_head if dv is None else dv + dv_head
    o_ref[...] = out.astype(o_ref.dtype)
    dq_ref[...] = dq.astype(dq_ref.dtype)
    dkv_ref[0] = dk.astype(dkv_ref.dtype)
    dkv_ref[1] = dv.astype(dkv_ref.dtype)
    wide_ref[0, :own] = dk[:own]
    wide_ref[1, :own] = dv[:own]
    wide_ref[0, own:] = dk[first:last]
    wide_ref[1, own:] = dv[first:last]


def attention(queries, keys, values, global_keys, global_values, grad_attended, keep):
    tokens, model_width = queries.shape
    first = keys[0].shape[0] + keys[1].shape[0]
    last = first + global_keys.shape[0]
    key_count = last
    lanes = 2 * (model_width // HEADS)
    steps = model_width // lanes
    token_block = pl.BlockSpec((tokens, lanes), lambda i: (0, i))
    key_block = pl.BlockSpec((key_count, lanes), lambda i: (0, i))
    own_block = pl.BlockSpec((keys[0].shape[0], lanes), lambda i: (0, i))
    halo_block = pl.BlockSpec((keys[1].shape[0], lanes), lambda i: (0, i))
    global_block = pl.BlockSpec((last - first, lanes), lambda i: (0, i))
    mask_block = pl.BlockSpec((tokens, key_count), lambda i: (0, 0))
    grads_block = pl.BlockSpec((2, key_count, lanes), lambda i: (0, 0, i))
    wide_rows = tokens + last - first
    wide_block = pl.BlockSpec((2, wide_rows, lanes), lambda i: (0, 0, i))
    flops = 2 * 2 * 6 * tokens * key_count * model_width
    moved = 2 * (3 * tokens * model_width + 2 * key_count * model_width) + 4 * (
        tokens * key_count + 2 * key_count * model_width
    )
    return pl.pallas_call(
        functools.partial(attention_kernel, tokens, first, last),
        grid=(steps,),
        in_specs=[
            token_block,
            own_block,
            halo_block,
            global_block,
            own_block,
            halo_block,
            global_block,
            token_block,
            mask_block,
        ],
        out_specs=[token_block, token_block, grads_block, wide_block],
        out_shape=[
            jax.ShapeDtypeStruct((tokens, model_width), jnp.bfloat16),
            jax.ShapeDtypeStruct((tokens, model_width), jnp.bfloat16),
            jax.ShapeDtypeStruct((2, key_count, model_width), jnp.bfloat16),
            jax.ShapeDtypeStruct((2, wide_rows, model_width), jnp.float32),
        ],
        cost_estimate=pl.CostEstimate(
            flops=flops, transcendentals=HEADS * tokens * key_count, bytes_accessed=moved
        ),
    )(queries, *keys, global_keys, *values, global_values, grad_attended, keep)


def split_wide(x):
    high = x.astype(jnp.bfloat16)
    low = (x - high.astype(jnp.float32)).astype(jnp.bfloat16)
    return jnp.concatenate([high, low], axis=0)


def join_wide(pair):
    half = pair.shape[0] // 2
    return pair[:half].astype(jnp.float32) + pair[half:].astype(jnp.float32)


def shards(features, w_query, w_key, w_value, w_out, reg_pos, grad_out):
    tile_rows, tile_cols, model_width = features.shape
    row_count = lax.axis_size("rows")
    col_count = lax.axis_size("cols")
    row_index = lax.axis_index("rows")
    col_index = lax.axis_index("cols")
    band_rows = tile_rows * row_count
    band_cols = tile_cols * col_count
    first_row = row_index * tile_rows
    first_col = col_index * tile_cols
    tokens = tile_rows * tile_cols
    device_count = row_count * col_count
    col_bits = bits(col_count)
    all_bits = col_bits + bits(row_count)
    ext_rows = tile_rows + 2 * RAD
    band_keys = RAD * tile_cols
    strip_keys = ext_rows * RAD
    frame_keys = tokens + 2 * band_keys + 2 * strip_keys
    used = frame_keys + device_count
    key_count = -(-used // 128) * 128

    flat_tokens = features.reshape(-1, model_width)
    own_keys = jnp.dot(flat_tokens, w_key, preferred_element_type=jnp.float32).astype(jnp.bfloat16)
    own_values = jnp.dot(flat_tokens, w_value, preferred_element_type=jnp.float32).astype(
        jnp.bfloat16
    )

    own_index = row_index * col_count + col_index
    own_place = lax.dynamic_index_in_dim(reg_pos, own_index, 0, keepdims=False)
    own_local = (own_place // band_cols - first_row) * tile_cols + (own_place % band_cols - first_col)
    gathered = jnp.concatenate(
        [
            lax.dynamic_slice_in_dim(own_keys, own_local, 1, 0),
            lax.dynamic_slice_in_dim(own_values, own_local, 1, 0),
        ],
        axis=1,
    )
    order = [col_bits, 0] + list(range(1, col_bits)) + list(range(col_bits + 1, all_bits))

    from_above, from_below, got = exchange(
        features[:RAD].reshape(-1, model_width),
        features[tile_rows - RAD :].reshape(-1, model_width),
        "rows",
        gathered.reshape(-1, model_width),
    )
    gathered = gather_step(gathered, got.reshape(gathered.shape), order[0])
    extended = jnp.concatenate(
        [
            from_above.reshape(RAD, tile_cols, model_width),
            features,
            from_below.reshape(RAD, tile_cols, model_width),
        ],
        axis=0,
    )
    from_left, from_right, got = exchange(
        extended[:, :RAD].reshape(-1, model_width),
        extended[:, tile_cols - RAD :].reshape(-1, model_width),
        "cols",
        gathered.reshape(-1, model_width),
    )
    gathered = gather_step(gathered, got.reshape(gathered.shape), order[1])

    queries = jnp.dot(flat_tokens, w_query, preferred_element_type=jnp.float32).astype(jnp.bfloat16)
    grad_attended = jnp.dot(
        grad_out.reshape(-1, model_width), w_out.T, preferred_element_type=jnp.float32
    ).astype(jnp.bfloat16)

    halo_features = jnp.concatenate(
        [
            from_above,
            from_below,
            from_left,
            from_right,
            jnp.zeros((key_count - used, model_width), features.dtype),
        ],
        axis=0,
    )
    halo_keys = jnp.dot(halo_features, w_key, preferred_element_type=jnp.float32).astype(
        jnp.bfloat16
    )
    halo_values = jnp.dot(halo_features, w_value, preferred_element_type=jnp.float32).astype(
        jnp.bfloat16
    )

    for position in order[2:]:
        gathered = gather_step(gathered, partner(gathered, position), position)
    global_kv = jnp.take(gathered, jnp.asarray(gather_order(order, device_count)), axis=0)
    global_keys = global_kv[:, :model_width]
    global_values = global_kv[:, model_width:]

    def grid(height, width, row0, col0):
        a, b = np.meshgrid(np.arange(height) + row0, np.arange(width) + col0, indexing="ij")
        return a.reshape(-1), b.reshape(-1)

    parts = [
        grid(tile_rows, tile_cols, RAD, RAD),
        grid(RAD, tile_cols, 0, RAD),
        grid(RAD, tile_cols, RAD + tile_rows, RAD),
        grid(ext_rows, RAD, 0, 0),
        grid(ext_rows, RAD, 0, RAD + tile_cols),
    ]
    key_rows = np.zeros(key_count, np.int32)
    key_cols = np.zeros(key_count, np.int32)
    key_rows[:frame_keys] = np.concatenate([p[0] for p in parts])
    key_cols[:frame_keys] = np.concatenate([p[1] for p in parts])
    kind = np.full(key_count, 2, np.int32)
    kind[:frame_keys] = 0
    kind[key_count - device_count :] = 1

    query_rows = first_row + jnp.repeat(jnp.arange(tile_rows, dtype=jnp.int32), tile_cols)
    query_cols = first_col + jnp.tile(jnp.arange(tile_cols, dtype=jnp.int32), tile_rows)
    start_rows = jnp.clip(query_rows - RAD, 0, band_rows - KW)[:, None]
    start_cols = jnp.clip(query_cols - RAD, 0, band_cols - KW)[:, None]
    cell_rows = (first_row - RAD + jnp.asarray(key_rows))[None, :]
    cell_cols = (first_col - RAD + jnp.asarray(key_cols))[None, :]
    inside = (
        (cell_rows >= start_rows)
        & (cell_rows < start_rows + KW)
        & (cell_cols >= start_cols)
        & (cell_cols < start_cols + KW)
    )
    key_kind = jnp.asarray(kind)[None, :]
    keep = ((inside & (key_kind == 0)) | (key_kind == 1)).astype(jnp.float32)

    attended, query_grads, rounded_grads, wide_grads = attention(
        queries,
        (own_keys, halo_keys),
        (own_values, halo_values),
        global_keys,
        global_values,
        grad_attended,
        keep,
    )
    layer_out = (
        jnp.dot(attended, w_out, preferred_element_type=jnp.float32)
        .astype(jnp.bfloat16)
        .reshape(features.shape)
    )

    given_all = jnp.dot(
        rounded_grads[0, :frame_keys], w_key.T, preferred_element_type=jnp.float32
    ) + jnp.dot(rounded_grads[1, :frame_keys], w_value.T, preferred_element_type=jnp.float32)

    def given(lo, hi):
        return given_all[lo:hi]

    scatter = wide_grads[:, tokens:].reshape(
        (2,) + (2,) * all_bits + (model_width,)
    )
    left = list(range(all_bits - 1, -1, -1))
    back_order = [0, col_bits] + list(range(1, col_bits)) + list(range(col_bits + 1, all_bits))

    strips_from = tokens + 2 * band_keys
    keep_part, send_part = scatter_split(scatter, left, back_order[0])
    strip_shape = (ext_rows, RAD, model_width)
    from_left, from_right, got = exchange(
        given(strips_from, strips_from + strip_keys).astype(jnp.bfloat16),
        given(strips_from + strip_keys, frame_keys).astype(jnp.bfloat16),
        "cols",
        split_wide(send_part.reshape(-1, model_width)),
    )
    scatter = keep_part + join_wide(got).reshape(keep_part.shape)
    received = jnp.pad(
        from_left.astype(jnp.float32).reshape(strip_shape), ((0, 0), (0, tile_cols - RAD), (0, 0))
    ) + jnp.pad(
        from_right.astype(jnp.float32).reshape(strip_shape), ((0, 0), (tile_cols - RAD, 0), (0, 0))
    )
    band_shape = (RAD, tile_cols, model_width)
    keep_part, send_part = scatter_split(scatter, left, back_order[1])
    from_above, from_below, got = exchange(
        (given(tokens, tokens + band_keys).reshape(band_shape) + received[:RAD])
        .reshape(-1, model_width)
        .astype(jnp.bfloat16),
        (given(tokens + band_keys, strips_from).reshape(band_shape) + received[RAD + tile_rows :])
        .reshape(-1, model_width)
        .astype(jnp.bfloat16),
        "rows",
        split_wide(send_part.reshape(-1, model_width)),
    )
    scatter = keep_part + join_wide(got).reshape(keep_part.shape)
    received = received[RAD : RAD + tile_rows]
    received = received + jnp.pad(
        from_above.astype(jnp.float32).reshape(band_shape), ((0, tile_rows - RAD), (0, 0), (0, 0))
    )
    received = received + jnp.pad(
        from_below.astype(jnp.float32).reshape(band_shape), ((tile_rows - RAD, 0), (0, 0), (0, 0))
    )
    for position in back_order[2:]:
        keep_part, send_part = scatter_split(scatter, left, position)
        scatter = keep_part + partner(send_part, position)
    own_grads = scatter.reshape(2, 1, model_width)

    own_given = given(0, tokens)
    own_row = (lax.dynamic_slice_in_dim(wide_grads, own_local, 1, 1) + own_grads).astype(
        jnp.bfloat16
    )
    own_row_given = jnp.dot(own_row[0], w_key.T, preferred_element_type=jnp.float32) + jnp.dot(
        own_row[1], w_value.T, preferred_element_type=jnp.float32
    )
    own_given = lax.dynamic_update_slice_in_dim(own_given, own_row_given, own_local, 0)

    grad_in = (
        jnp.dot(query_grads, w_query.T, preferred_element_type=jnp.float32)
        + own_given
        + received.reshape(tokens, model_width)
    )
    grad_in = grad_in.astype(jnp.bfloat16).reshape(features.shape)
    return (layer_out, grad_in)


def solution(mesh):
    placed = (P("rows", "cols", None), P(), P(), P(), P(), P(), P("rows", "cols", None))
    return jax.shard_map(
        shards,
        mesh=mesh,
        in_specs=placed,
        out_specs=(P("rows", "cols", None), P("rows", "cols", None)),
        check_vma=False,
    )
```

```python
import functools
import math

import jax
import jax.numpy as jnp
import numpy as np
from jax import lax
from jax.experimental import pallas as pl
from jax.sharding import PartitionSpec as P

HEADS = 16
KW = 13
RAD = 6


def bits(n):
    return n.bit_length() - 1


def device_bit(position):
    col_bits = bits(lax.axis_size("cols"))
    if position < col_bits:
        return "cols", position
    return "rows", position - col_bits


def own_bit(position):
    axis, bit = device_bit(position)
    return (lax.axis_index(axis) >> bit) % 2


def partner(x, position):
    axis, bit = device_bit(position)
    size = lax.axis_size(axis)
    return lax.ppermute(x, axis, [(i, i ^ (1 << bit)) for i in range(size)])


def exchange(to_lower, to_higher, axis, rider=None, rider_dim=0):
    size = lax.axis_size(axis)
    even = lax.axis_index(axis) % 2 == 0
    first = jnp.where(even, to_higher, to_lower)
    length = first.shape[rider_dim]
    if rider is not None:
        first = jnp.concatenate([first, rider], axis=rider_dim)
    got_first = lax.ppermute(first, axis, [(i, i ^ 1) for i in range(size)])
    links = [(i, i + 1) for i in range(1, size - 1, 2)] + [(i, i - 1) for i in range(2, size, 2)]
    got_second = lax.ppermute(jnp.where(even, to_lower, to_higher), axis, links)
    rider_got = None
    if rider is not None:
        rider_got = lax.slice_in_dim(got_first, length, None, axis=rider_dim)
        got_first = lax.slice_in_dim(got_first, 0, length, axis=rider_dim)
    from_lower = jnp.where(even, got_second, got_first)
    from_higher = jnp.where(even, got_first, got_second)
    return from_lower, from_higher, rider_got


def gather_step(x, other, position):
    low = own_bit(position) == 0
    return jnp.where(low, jnp.concatenate([x, other]), jnp.concatenate([other, x]))


def gather_order(order, count):
    where = np.zeros(count, np.int32)
    for l in range(count):
        where[l] = sum(((l >> bit) & 1) << step for step, bit in enumerate(order))
    return where


def scatter_split(x, order_left, position):
    axis = 1 + order_left.index(position)
    high = own_bit(position) == 1
    lower = lax.index_in_dim(x, 0, axis, keepdims=False)
    upper = lax.index_in_dim(x, 1, axis, keepdims=False)
    order_left.remove(position)
    return jnp.where(high, upper, lower), jnp.where(high, lower, upper)


def attention_kernel(
    own, first, last, q_ref, ko_ref, kh_ref, kg_ref, vo_ref, vh_ref, vg_ref, g_ref, mask_ref,
    o_ref, dq_ref, dkv_ref, wide_ref,
):
    head_size = q_ref.shape[1] // 2
    score_scale = 1.0 / math.sqrt(head_size)
    q = (q_ref[...] * score_scale).astype(q_ref.dtype)
    k = jnp.concatenate([ko_ref[...], kh_ref[...], kg_ref[...]], axis=0)
    v = jnp.concatenate([vo_ref[...], vh_ref[...], vg_ref[...]], axis=0)
    g = g_ref[...]
    keep = mask_ref[...] > 0
    lane_head = lax.broadcasted_iota(jnp.int32, q.shape, 1) // head_size
    rows = (((1,), (1,)), ((), ()))
    cols = (((0,), (0,)), ((), ()))
    out = jnp.zeros(q.shape, jnp.float32)
    dq = jnp.zeros(q.shape, jnp.float32)
    dk = None
    dv = None
    for head in range(2):
        mine = lane_head == head
        q_head = jnp.where(mine, q, jnp.zeros_like(q))
        g_head = jnp.where(mine, g, jnp.zeros_like(g))
        scores = lax.dot_general(q_head, k, rows, preferred_element_type=jnp.float32)
        scores = jnp.where(keep, scores, -1e30)
        row_max = jnp.max(scores, axis=1, keepdims=True)
        exps = jnp.exp(scores - row_max)
        probs = exps * (1.0 / jnp.sum(exps, axis=1, keepdims=True))
        rounded = probs.astype(jnp.bfloat16)
        attended = jnp.dot(rounded, v, preferred_element_type=jnp.float32)
        attended = attended.astype(jnp.bfloat16).astype(jnp.float32)
        out = jnp.where(mine, attended, out)
        delta = jnp.sum(
            jnp.where(mine, g.astype(jnp.float32) * attended, 0.0), axis=1, keepdims=True
        )
        dots = lax.dot_general(g_head, v, rows, preferred_element_type=jnp.float32)
        slopes = (probs * (dots - delta)).astype(jnp.bfloat16)
        dq = jnp.where(
            mine, jnp.dot(slopes, k, preferred_element_type=jnp.float32) * score_scale, dq
        )
        dk_head = lax.dot_general(slopes, q_head, cols, preferred_element_type=jnp.float32)
        dv_head = lax.dot_general(rounded, g_head, cols, preferred_element_type=jnp.float32)
        dk = dk_head if dk is None else dk + dk_head
        dv = dv_head if dv is None else dv + dv_head
    o_ref[...] = out.astype(o_ref.dtype)
    dq_ref[...] = dq.astype(dq_ref.dtype)
    dkv_ref[0] = dk.astype(dkv_ref.dtype)
    dkv_ref[1] = dv.astype(dkv_ref.dtype)
    wide_ref[0, :own] = dk[:own]
    wide_ref[1, :own] = dv[:own]
    wide_ref[0, own:] = dk[first:last]
    wide_ref[1, own:] = dv[first:last]


def attention(queries, keys, values, global_keys, global_values, grad_attended, keep):
    tokens, model_width = queries.shape
    first = keys[0].shape[0] + keys[1].shape[0]
    last = first + global_keys.shape[0]
    key_count = last
    lanes = 2 * (model_width // HEADS)
    steps = model_width // lanes
    token_block = pl.BlockSpec((tokens, lanes), lambda i: (0, i))
    key_block = pl.BlockSpec((key_count, lanes), lambda i: (0, i))
    own_block = pl.BlockSpec((keys[0].shape[0], lanes), lambda i: (0, i))
    halo_block = pl.BlockSpec((keys[1].shape[0], lanes), lambda i: (0, i))
    global_block = pl.BlockSpec((last - first, lanes), lambda i: (0, i))
    mask_block = pl.BlockSpec((tokens, key_count), lambda i: (0, 0))
    grads_block = pl.BlockSpec((2, key_count, lanes), lambda i: (0, 0, i))
    wide_rows = tokens + last - first
    wide_block = pl.BlockSpec((2, wide_rows, lanes), lambda i: (0, 0, i))
    flops = 2 * 2 * 6 * tokens * key_count * model_width
    moved = 2 * (3 * tokens * model_width + 2 * key_count * model_width) + 4 * (
        tokens * key_count + 2 * key_count * model_width
    )
    return pl.pallas_call(
        functools.partial(attention_kernel, tokens, first, last),
        grid=(steps,),
        in_specs=[
            token_block,
            own_block,
            halo_block,
            global_block,
            own_block,
            halo_block,
            global_block,
            token_block,
            mask_block,
        ],
        out_specs=[token_block, token_block, grads_block, wide_block],
        out_shape=[
            jax.ShapeDtypeStruct((tokens, model_width), jnp.bfloat16),
            jax.ShapeDtypeStruct((tokens, model_width), jnp.bfloat16),
            jax.ShapeDtypeStruct((2, key_count, model_width), jnp.bfloat16),
            jax.ShapeDtypeStruct((2, wide_rows, model_width), jnp.float32),
        ],
        cost_estimate=pl.CostEstimate(
            flops=flops, transcendentals=HEADS * tokens * key_count, bytes_accessed=moved
        ),
    )(queries, *keys, global_keys, *values, global_values, grad_attended, keep)


def split_wide(x):
    high = x.astype(jnp.bfloat16)
    low = (x - high.astype(jnp.float32)).astype(jnp.bfloat16)
    return jnp.concatenate([high, low], axis=0)


def join_wide(pair):
    half = pair.shape[0] // 2
    return pair[:half].astype(jnp.float32) + pair[half:].astype(jnp.float32)


def shards(features, w_query, w_key, w_value, w_out, reg_pos, grad_out):
    tile_rows, tile_cols, model_width = features.shape
    row_count = lax.axis_size("rows")
    col_count = lax.axis_size("cols")
    row_index = lax.axis_index("rows")
    col_index = lax.axis_index("cols")
    band_rows = tile_rows * row_count
    band_cols = tile_cols * col_count
    first_row = row_index * tile_rows
    first_col = col_index * tile_cols
    tokens = tile_rows * tile_cols
    device_count = row_count * col_count
    col_bits = bits(col_count)
    all_bits = col_bits + bits(row_count)
    ext_rows = tile_rows + 2 * RAD
    band_keys = RAD * tile_cols
    strip_keys = ext_rows * RAD
    frame_keys = tokens + 2 * band_keys + 2 * strip_keys
    used = frame_keys + device_count
    key_count = -(-used // 128) * 128

    flat_tokens = features.reshape(-1, model_width)
    own_keys = jnp.dot(flat_tokens, w_key, preferred_element_type=jnp.float32).astype(jnp.bfloat16)
    own_values = jnp.dot(flat_tokens, w_value, preferred_element_type=jnp.float32).astype(
        jnp.bfloat16
    )

    own_index = row_index * col_count + col_index
    own_place = lax.dynamic_index_in_dim(reg_pos, own_index, 0, keepdims=False)
    own_local = (own_place // band_cols - first_row) * tile_cols + (own_place % band_cols - first_col)
    gathered = jnp.concatenate(
        [
            lax.dynamic_slice_in_dim(own_keys, own_local, 1, 0),
            lax.dynamic_slice_in_dim(own_values, own_local, 1, 0),
        ],
        axis=1,
    )
    order = [col_bits, 0] + list(range(1, col_bits)) + list(range(col_bits + 1, all_bits))

    from_above, from_below, got = exchange(
        features[:RAD].reshape(-1, model_width),
        features[tile_rows - RAD :].reshape(-1, model_width),
        "rows",
        gathered.reshape(-1, model_width),
    )
    gathered = gather_step(gathered, got.reshape(gathered.shape), order[0])
    extended = jnp.concatenate(
        [
            from_above.reshape(RAD, tile_cols, model_width),
            features,
            from_below.reshape(RAD, tile_cols, model_width),
        ],
        axis=0,
    )
    from_left, from_right, got = exchange(
        extended[:, :RAD].reshape(-1, model_width),
        extended[:, tile_cols - RAD :].reshape(-1, model_width),
        "cols",
        gathered.reshape(-1, model_width),
    )
    gathered = gather_step(gathered, got.reshape(gathered.shape), order[1])

    queries = jnp.dot(flat_tokens, w_query, preferred_element_type=jnp.float32).astype(jnp.bfloat16)
    grad_attended = jnp.dot(
        grad_out.reshape(-1, model_width), w_out.T, preferred_element_type=jnp.float32
    ).astype(jnp.bfloat16)

    halo_features = jnp.concatenate(
        [
            from_above,
            from_below,
            from_left,
            from_right,
            jnp.zeros((key_count - used, model_width), features.dtype),
        ],
        axis=0,
    )
    halo_keys = jnp.dot(halo_features, w_key, preferred_element_type=jnp.float32).astype(
        jnp.bfloat16
    )
    halo_values = jnp.dot(halo_features, w_value, preferred_element_type=jnp.float32).astype(
        jnp.bfloat16
    )

    for position in order[2:]:
        gathered = gather_step(gathered, partner(gathered, position), position)
    global_kv = jnp.take(gathered, jnp.asarray(gather_order(order, device_count)), axis=0)
    global_keys = global_kv[:, :model_width]
    global_values = global_kv[:, model_width:]

    def grid(height, width, row0, col0):
        a, b = np.meshgrid(np.arange(height) + row0, np.arange(width) + col0, indexing="ij")
        return a.reshape(-1), b.reshape(-1)

    parts = [
        grid(tile_rows, tile_cols, RAD, RAD),
        grid(RAD, tile_cols, 0, RAD),
        grid(RAD, tile_cols, RAD + tile_rows, RAD),
        grid(ext_rows, RAD, 0, 0),
        grid(ext_rows, RAD, 0, RAD + tile_cols),
    ]
    key_rows = np.zeros(key_count, np.int32)
    key_cols = np.zeros(key_count, np.int32)
    key_rows[:frame_keys] = np.concatenate([p[0] for p in parts])
    key_cols[:frame_keys] = np.concatenate([p[1] for p in parts])
    kind = np.full(key_count, 2, np.int32)
    kind[:frame_keys] = 0
    kind[key_count - device_count :] = 1

    query_rows = first_row + jnp.repeat(jnp.arange(tile_rows, dtype=jnp.int32), tile_cols)
    query_cols = first_col + jnp.tile(jnp.arange(tile_cols, dtype=jnp.int32), tile_rows)
    start_rows = jnp.clip(query_rows - RAD, 0, band_rows - KW)[:, None]
    start_cols = jnp.clip(query_cols - RAD, 0, band_cols - KW)[:, None]
    cell_rows = (first_row - RAD + jnp.asarray(key_rows))[None, :]
    cell_cols = (first_col - RAD + jnp.asarray(key_cols))[None, :]
    inside = (
        (cell_rows >= start_rows)
        & (cell_rows < start_rows + KW)
        & (cell_cols >= start_cols)
        & (cell_cols < start_cols + KW)
    )
    key_kind = jnp.asarray(kind)[None, :]
    keep = ((inside & (key_kind == 0)) | (key_kind == 1)).astype(jnp.float32)

    attended, query_grads, rounded_grads, wide_grads = attention(
        queries,
        (own_keys, halo_keys),
        (own_values, halo_values),
        global_keys,
        global_values,
        grad_attended,
        keep,
    )
    layer_out = (
        jnp.dot(attended, w_out, preferred_element_type=jnp.float32)
        .astype(jnp.bfloat16)
        .reshape(features.shape)
    )

    strips_from = tokens + 2 * band_keys

    def contribution(lo, hi):
        return jnp.dot(
            rounded_grads[0, lo:hi], w_key.T, preferred_element_type=jnp.float32
        ) + jnp.dot(rounded_grads[1, lo:hi], w_value.T, preferred_element_type=jnp.float32)

    strip_given = contribution(strips_from, frame_keys)
    rest_given = contribution(0, strips_from)

    def given(lo, hi):
        if lo >= strips_from:
            return strip_given[lo - strips_from : hi - strips_from]
        return rest_given[lo:hi]

    scatter = wide_grads[:, tokens:].reshape(
        (2,) + (2,) * all_bits + (model_width,)
    )
    left = list(range(all_bits - 1, -1, -1))
    back_order = [0, col_bits] + list(range(1, col_bits)) + list(range(col_bits + 1, all_bits))

    keep_part, send_part = scatter_split(scatter, left, back_order[0])
    strip_shape = (ext_rows, RAD, model_width)
    from_left, from_right, got = exchange(
        given(strips_from, strips_from + strip_keys).astype(jnp.bfloat16),
        given(strips_from + strip_keys, frame_keys).astype(jnp.bfloat16),
        "cols",
        split_wide(send_part.reshape(-1, model_width)),
    )
    scatter = keep_part + join_wide(got).reshape(keep_part.shape)
    received = jnp.pad(
        from_left.astype(jnp.float32).reshape(strip_shape), ((0, 0), (0, tile_cols - RAD), (0, 0))
    ) + jnp.pad(
        from_right.astype(jnp.float32).reshape(strip_shape), ((0, 0), (tile_cols - RAD, 0), (0, 0))
    )
    band_shape = (RAD, tile_cols, model_width)
    keep_part, send_part = scatter_split(scatter, left, back_order[1])
    from_above, from_below, got = exchange(
        (given(tokens, tokens + band_keys).reshape(band_shape) + received[:RAD])
        .reshape(-1, model_width)
        .astype(jnp.bfloat16),
        (given(tokens + band_keys, strips_from).reshape(band_shape) + received[RAD + tile_rows :])
        .reshape(-1, model_width)
        .astype(jnp.bfloat16),
        "rows",
        split_wide(send_part.reshape(-1, model_width)),
    )
    scatter = keep_part + join_wide(got).reshape(keep_part.shape)
    received = received[RAD : RAD + tile_rows]
    received = received + jnp.pad(
        from_above.astype(jnp.float32).reshape(band_shape), ((0, tile_rows - RAD), (0, 0), (0, 0))
    )
    received = received + jnp.pad(
        from_below.astype(jnp.float32).reshape(band_shape), ((tile_rows - RAD, 0), (0, 0), (0, 0))
    )
    for position in back_order[2:]:
        keep_part, send_part = scatter_split(scatter, left, position)
        scatter = keep_part + partner(send_part, position)
    own_grads = scatter.reshape(2, 1, model_width)

    own_given = given(0, tokens)
    own_row = (lax.dynamic_slice_in_dim(wide_grads, own_local, 1, 1) + own_grads).astype(
        jnp.bfloat16
    )
    own_row_given = jnp.dot(own_row[0], w_key.T, preferred_element_type=jnp.float32) + jnp.dot(
        own_row[1], w_value.T, preferred_element_type=jnp.float32
    )
    own_given = lax.dynamic_update_slice_in_dim(own_given, own_row_given, own_local, 0)

    grad_in = (
        jnp.dot(query_grads, w_query.T, preferred_element_type=jnp.float32)
        + own_given
        + received.reshape(tokens, model_width)
    )
    grad_in = grad_in.astype(jnp.bfloat16).reshape(features.shape)
    return (layer_out, grad_in)


def solution(mesh):
    placed = (P("rows", "cols", None), P(), P(), P(), P(), P(), P("rows", "cols", None))
    return jax.shard_map(
        shards,
        mesh=mesh,
        in_specs=placed,
        out_specs=(P("rows", "cols", None), P("rows", "cols", None)),
        check_vma=False,
    )
```

```python
import functools
import math

import jax
import jax.numpy as jnp
import numpy as np
from jax import lax
from jax.experimental import pallas as pl
from jax.sharding import PartitionSpec as P

HEADS = 16
KW = 13
RAD = 6


def bits(n):
    return n.bit_length() - 1


def device_bit(position):
    col_bits = bits(lax.axis_size("cols"))
    if position < col_bits:
        return "cols", position
    return "rows", position - col_bits


def own_bit(position):
    axis, bit = device_bit(position)
    return (lax.axis_index(axis) >> bit) % 2


def partner(x, position):
    axis, bit = device_bit(position)
    size = lax.axis_size(axis)
    return lax.ppermute(x, axis, [(i, i ^ (1 << bit)) for i in range(size)])


def exchange(to_lower, to_higher, axis, rider=None, rider_dim=0):
    size = lax.axis_size(axis)
    even = lax.axis_index(axis) % 2 == 0
    first = jnp.where(even, to_higher, to_lower)
    length = first.shape[rider_dim]
    if rider is not None:
        first = jnp.concatenate([first, rider], axis=rider_dim)
    got_first = lax.ppermute(first, axis, [(i, i ^ 1) for i in range(size)])
    links = [(i, i + 1) for i in range(1, size - 1, 2)] + [(i, i - 1) for i in range(2, size, 2)]
    got_second = lax.ppermute(jnp.where(even, to_lower, to_higher), axis, links)
    rider_got = None
    if rider is not None:
        rider_got = lax.slice_in_dim(got_first, length, None, axis=rider_dim)
        got_first = lax.slice_in_dim(got_first, 0, length, axis=rider_dim)
    from_lower = jnp.where(even, got_second, got_first)
    from_higher = jnp.where(even, got_first, got_second)
    return from_lower, from_higher, rider_got


def gather_step(x, other, position):
    low = own_bit(position) == 0
    return jnp.where(low, jnp.concatenate([x, other]), jnp.concatenate([other, x]))


def gather_order(order, count):
    where = np.zeros(count, np.int32)
    for l in range(count):
        where[l] = sum(((l >> bit) & 1) << step for step, bit in enumerate(order))
    return where


def scatter_split(x, order_left, position):
    axis = 1 + order_left.index(position)
    high = own_bit(position) == 1
    lower = lax.index_in_dim(x, 0, axis, keepdims=False)
    upper = lax.index_in_dim(x, 1, axis, keepdims=False)
    order_left.remove(position)
    return jnp.where(high, upper, lower), jnp.where(high, lower, upper)


def attention_kernel(own, first, last, pieces, q_ref, *refs):
    key_refs = refs[:pieces]
    value_refs = refs[pieces : 2 * pieces]
    g_ref, mask_ref, o_ref, dq_ref, dkv_ref, wide_ref = refs[2 * pieces :]
    head_size = q_ref.shape[1] // 2
    score_scale = 1.0 / math.sqrt(head_size)
    q = (q_ref[...] * score_scale).astype(q_ref.dtype)
    k = jnp.concatenate([r[...] for r in key_refs], axis=0)
    v = jnp.concatenate([r[...] for r in value_refs], axis=0)
    g = g_ref[...]
    keep = mask_ref[...] > 0
    lane_head = lax.broadcasted_iota(jnp.int32, q.shape, 1) // head_size
    rows = (((1,), (1,)), ((), ()))
    cols = (((0,), (0,)), ((), ()))
    out = jnp.zeros(q.shape, jnp.float32)
    dq = jnp.zeros(q.shape, jnp.float32)
    dk = None
    dv = None
    for head in range(2):
        mine = lane_head == head
        q_head = jnp.where(mine, q, jnp.zeros_like(q))
        g_head = jnp.where(mine, g, jnp.zeros_like(g))
        scores = lax.dot_general(q_head, k, rows, preferred_element_type=jnp.float32)
        scores = jnp.where(keep, scores, -1e30)
        row_max = jnp.max(scores, axis=1, keepdims=True)
        exps = jnp.exp(scores - row_max)
        probs = exps * (1.0 / jnp.sum(exps, axis=1, keepdims=True))
        rounded = probs.astype(jnp.bfloat16)
        attended = jnp.dot(rounded, v, preferred_element_type=jnp.float32)
        attended = attended.astype(jnp.bfloat16).astype(jnp.float32)
        out = jnp.where(mine, attended, out)
        delta = jnp.sum(
            jnp.where(mine, g.astype(jnp.float32) * attended, 0.0), axis=1, keepdims=True
        )
        dots = lax.dot_general(g_head, v, rows, preferred_element_type=jnp.float32)
        slopes = (probs * (dots - delta)).astype(jnp.bfloat16)
        dq = jnp.where(
            mine, jnp.dot(slopes, k, preferred_element_type=jnp.float32) * score_scale, dq
        )
        dk_head = lax.dot_general(slopes, q_head, cols, preferred_element_type=jnp.float32)
        dv_head = lax.dot_general(rounded, g_head, cols, preferred_element_type=jnp.float32)
        dk = dk_head if dk is None else dk + dk_head
        dv = dv_head if dv is None else dv + dv_head
    o_ref[...] = out.astype(o_ref.dtype)
    dq_ref[...] = dq.astype(dq_ref.dtype)
    dkv_ref[0] = dk.astype(dkv_ref.dtype)
    dkv_ref[1] = dv.astype(dkv_ref.dtype)
    wide_ref[0, :own] = dk[:own]
    wide_ref[1, :own] = dv[:own]
    wide_ref[0, own:] = dk[first:last]
    wide_ref[1, own:] = dv[first:last]


def attention(queries, keys, values, global_keys, global_values, grad_attended, keep):
    tokens, model_width = queries.shape
    first = sum(piece.shape[0] for piece in keys)
    last = first + global_keys.shape[0]
    key_count = last
    lanes = 2 * (model_width // HEADS)
    steps = model_width // lanes
    token_block = pl.BlockSpec((tokens, lanes), lambda i: (0, i))
    key_block = pl.BlockSpec((key_count, lanes), lambda i: (0, i))
    piece_blocks = [pl.BlockSpec((piece.shape[0], lanes), lambda i: (0, i)) for piece in keys]
    global_block = pl.BlockSpec((last - first, lanes), lambda i: (0, i))
    mask_block = pl.BlockSpec((tokens, key_count), lambda i: (0, 0))
    grads_block = pl.BlockSpec((2, key_count, lanes), lambda i: (0, 0, i))
    wide_rows = tokens + last - first
    wide_block = pl.BlockSpec((2, wide_rows, lanes), lambda i: (0, 0, i))
    flops = 2 * 2 * 6 * tokens * key_count * model_width
    moved = 2 * (3 * tokens * model_width + 2 * key_count * model_width) + 4 * (
        tokens * key_count + 2 * key_count * model_width
    )
    return pl.pallas_call(
        functools.partial(attention_kernel, tokens, first, last, len(keys) + 1),
        grid=(steps,),
        in_specs=[token_block]
        + piece_blocks
        + [global_block]
        + piece_blocks
        + [global_block, token_block, mask_block],
        out_specs=[token_block, token_block, grads_block, wide_block],
        out_shape=[
            jax.ShapeDtypeStruct((tokens, model_width), jnp.bfloat16),
            jax.ShapeDtypeStruct((tokens, model_width), jnp.bfloat16),
            jax.ShapeDtypeStruct((2, key_count, model_width), jnp.bfloat16),
            jax.ShapeDtypeStruct((2, wide_rows, model_width), jnp.float32),
        ],
        cost_estimate=pl.CostEstimate(
            flops=flops, transcendentals=HEADS * tokens * key_count, bytes_accessed=moved
        ),
    )(queries, *keys, global_keys, *values, global_values, grad_attended, keep)


def split_wide(x):
    high = x.astype(jnp.bfloat16)
    low = (x - high.astype(jnp.float32)).astype(jnp.bfloat16)
    return jnp.concatenate([high, low], axis=0)


def join_wide(pair):
    half = pair.shape[0] // 2
    return pair[:half].astype(jnp.float32) + pair[half:].astype(jnp.float32)


def shards(features, w_query, w_key, w_value, w_out, reg_pos, grad_out):
    tile_rows, tile_cols, model_width = features.shape
    row_count = lax.axis_size("rows")
    col_count = lax.axis_size("cols")
    row_index = lax.axis_index("rows")
    col_index = lax.axis_index("cols")
    band_rows = tile_rows * row_count
    band_cols = tile_cols * col_count
    first_row = row_index * tile_rows
    first_col = col_index * tile_cols
    tokens = tile_rows * tile_cols
    device_count = row_count * col_count
    col_bits = bits(col_count)
    all_bits = col_bits + bits(row_count)
    ext_rows = tile_rows + 2 * RAD
    band_keys = RAD * tile_cols
    strip_keys = ext_rows * RAD
    frame_keys = tokens + 2 * band_keys + 2 * strip_keys
    used = frame_keys + device_count
    key_count = -(-used // 128) * 128

    flat_tokens = features.reshape(-1, model_width)
    own_keys = jnp.dot(flat_tokens, w_key, preferred_element_type=jnp.float32).astype(jnp.bfloat16)
    own_values = jnp.dot(flat_tokens, w_value, preferred_element_type=jnp.float32).astype(
        jnp.bfloat16
    )

    own_index = row_index * col_count + col_index
    own_place = lax.dynamic_index_in_dim(reg_pos, own_index, 0, keepdims=False)
    own_local = (own_place // band_cols - first_row) * tile_cols + (own_place % band_cols - first_col)
    gathered = jnp.concatenate(
        [
            lax.dynamic_slice_in_dim(own_keys, own_local, 1, 0),
            lax.dynamic_slice_in_dim(own_values, own_local, 1, 0),
        ],
        axis=1,
    )
    order = [col_bits, 0] + list(range(1, col_bits)) + list(range(col_bits + 1, all_bits))

    from_above, from_below, got = exchange(
        features[:RAD].reshape(-1, model_width),
        features[tile_rows - RAD :].reshape(-1, model_width),
        "rows",
        gathered.reshape(-1, model_width),
    )
    gathered = gather_step(gathered, got.reshape(gathered.shape), order[0])
    extended = jnp.concatenate(
        [
            from_above.reshape(RAD, tile_cols, model_width),
            features,
            from_below.reshape(RAD, tile_cols, model_width),
        ],
        axis=0,
    )
    from_left, from_right, got = exchange(
        extended[:, :RAD].reshape(-1, model_width),
        extended[:, tile_cols - RAD :].reshape(-1, model_width),
        "cols",
        gathered.reshape(-1, model_width),
    )
    gathered = gather_step(gathered, got.reshape(gathered.shape), order[1])

    queries = jnp.dot(flat_tokens, w_query, preferred_element_type=jnp.float32).astype(jnp.bfloat16)
    grad_attended = jnp.dot(
        grad_out.reshape(-1, model_width), w_out.T, preferred_element_type=jnp.float32
    ).astype(jnp.bfloat16)

    band_features = jnp.concatenate([from_above, from_below], axis=0)
    band_keys_kv = (
        jnp.dot(band_features, w_key, preferred_element_type=jnp.float32).astype(jnp.bfloat16),
        jnp.dot(band_features, w_value, preferred_element_type=jnp.float32).astype(jnp.bfloat16),
    )
    strip_features = jnp.concatenate(
        [from_left, from_right, jnp.zeros((key_count - used, model_width), features.dtype)],
        axis=0,
    )
    strip_keys_kv = (
        jnp.dot(strip_features, w_key, preferred_element_type=jnp.float32).astype(jnp.bfloat16),
        jnp.dot(strip_features, w_value, preferred_element_type=jnp.float32).astype(jnp.bfloat16),
    )

    for position in order[2:]:
        gathered = gather_step(gathered, partner(gathered, position), position)
    global_kv = jnp.take(gathered, jnp.asarray(gather_order(order, device_count)), axis=0)
    global_keys = global_kv[:, :model_width]
    global_values = global_kv[:, model_width:]

    def grid(height, width, row0, col0):
        a, b = np.meshgrid(np.arange(height) + row0, np.arange(width) + col0, indexing="ij")
        return a.reshape(-1), b.reshape(-1)

    parts = [
        grid(tile_rows, tile_cols, RAD, RAD),
        grid(RAD, tile_cols, 0, RAD),
        grid(RAD, tile_cols, RAD + tile_rows, RAD),
        grid(ext_rows, RAD, 0, 0),
        grid(ext_rows, RAD, 0, RAD + tile_cols),
    ]
    key_rows = np.zeros(key_count, np.int32)
    key_cols = np.zeros(key_count, np.int32)
    key_rows[:frame_keys] = np.concatenate([p[0] for p in parts])
    key_cols[:frame_keys] = np.concatenate([p[1] for p in parts])
    kind = np.full(key_count, 2, np.int32)
    kind[:frame_keys] = 0
    kind[key_count - device_count :] = 1

    query_rows = first_row + jnp.repeat(jnp.arange(tile_rows, dtype=jnp.int32), tile_cols)
    query_cols = first_col + jnp.tile(jnp.arange(tile_cols, dtype=jnp.int32), tile_rows)
    start_rows = jnp.clip(query_rows - RAD, 0, band_rows - KW)[:, None]
    start_cols = jnp.clip(query_cols - RAD, 0, band_cols - KW)[:, None]
    cell_rows = (first_row - RAD + jnp.asarray(key_rows))[None, :]
    cell_cols = (first_col - RAD + jnp.asarray(key_cols))[None, :]
    inside = (
        (cell_rows >= start_rows)
        & (cell_rows < start_rows + KW)
        & (cell_cols >= start_cols)
        & (cell_cols < start_cols + KW)
    )
    key_kind = jnp.asarray(kind)[None, :]
    keep = ((inside & (key_kind == 0)) | (key_kind == 1)).astype(jnp.float32)

    attended, query_grads, rounded_grads, wide_grads = attention(
        queries,
        (own_keys, band_keys_kv[0], strip_keys_kv[0]),
        (own_values, band_keys_kv[1], strip_keys_kv[1]),
        global_keys,
        global_values,
        grad_attended,
        keep,
    )
    layer_out = (
        jnp.dot(attended, w_out, preferred_element_type=jnp.float32)
        .astype(jnp.bfloat16)
        .reshape(features.shape)
    )

    strips_from = tokens + 2 * band_keys

    def contribution(lo, hi):
        return jnp.dot(
            rounded_grads[0, lo:hi], w_key.T, preferred_element_type=jnp.float32
        ) + jnp.dot(rounded_grads[1, lo:hi], w_value.T, preferred_element_type=jnp.float32)

    strip_given = contribution(strips_from, frame_keys)
    rest_given = contribution(0, strips_from)

    def given(lo, hi):
        if lo >= strips_from:
            return strip_given[lo - strips_from : hi - strips_from]
        return rest_given[lo:hi]

    scatter = wide_grads[:, tokens:].reshape(
        (2,) + (2,) * all_bits + (model_width,)
    )
    left = list(range(all_bits - 1, -1, -1))
    back_order = [0, col_bits] + list(range(1, col_bits)) + list(range(col_bits + 1, all_bits))

    keep_part, send_part = scatter_split(scatter, left, back_order[0])
    strip_shape = (ext_rows, RAD, model_width)
    from_left, from_right, got = exchange(
        given(strips_from, strips_from + strip_keys).astype(jnp.bfloat16),
        given(strips_from + strip_keys, frame_keys).astype(jnp.bfloat16),
        "cols",
        split_wide(send_part.reshape(-1, model_width)),
    )
    scatter = keep_part + join_wide(got).reshape(keep_part.shape)
    received = jnp.pad(
        from_left.astype(jnp.float32).reshape(strip_shape), ((0, 0), (0, tile_cols - RAD), (0, 0))
    ) + jnp.pad(
        from_right.astype(jnp.float32).reshape(strip_shape), ((0, 0), (tile_cols - RAD, 0), (0, 0))
    )
    band_shape = (RAD, tile_cols, model_width)
    keep_part, send_part = scatter_split(scatter, left, back_order[1])
    from_above, from_below, got = exchange(
        (given(tokens, tokens + band_keys).reshape(band_shape) + received[:RAD])
        .reshape(-1, model_width)
        .astype(jnp.bfloat16),
        (given(tokens + band_keys, strips_from).reshape(band_shape) + received[RAD + tile_rows :])
        .reshape(-1, model_width)
        .astype(jnp.bfloat16),
        "rows",
        split_wide(send_part.reshape(-1, model_width)),
    )
    scatter = keep_part + join_wide(got).reshape(keep_part.shape)
    received = received[RAD : RAD + tile_rows]
    received = received + jnp.pad(
        from_above.astype(jnp.float32).reshape(band_shape), ((0, tile_rows - RAD), (0, 0), (0, 0))
    )
    received = received + jnp.pad(
        from_below.astype(jnp.float32).reshape(band_shape), ((tile_rows - RAD, 0), (0, 0), (0, 0))
    )
    for position in back_order[2:]:
        keep_part, send_part = scatter_split(scatter, left, position)
        scatter = keep_part + partner(send_part, position)
    own_grads = scatter.reshape(2, 1, model_width)

    own_given = given(0, tokens)
    own_row = (lax.dynamic_slice_in_dim(wide_grads, own_local, 1, 1) + own_grads).astype(
        jnp.bfloat16
    )
    own_row_given = jnp.dot(own_row[0], w_key.T, preferred_element_type=jnp.float32) + jnp.dot(
        own_row[1], w_value.T, preferred_element_type=jnp.float32
    )
    own_given = lax.dynamic_update_slice_in_dim(own_given, own_row_given, own_local, 0)

    grad_in = (
        jnp.dot(query_grads, w_query.T, preferred_element_type=jnp.float32)
        + own_given
        + received.reshape(tokens, model_width)
    )
    grad_in = grad_in.astype(jnp.bfloat16).reshape(features.shape)
    return (layer_out, grad_in)


def solution(mesh):
    placed = (P("rows", "cols", None), P(), P(), P(), P(), P(), P("rows", "cols", None))
    return jax.shard_map(
        shards,
        mesh=mesh,
        in_specs=placed,
        out_specs=(P("rows", "cols", None), P("rows", "cols", None)),
        check_vma=False,
    )
```

```python
import functools
import math

import jax
import jax.numpy as jnp
import numpy as np
from jax import lax
from jax.experimental import pallas as pl
from jax.sharding import PartitionSpec as P

HEADS = 16
KW = 13
RAD = 6


def bits(n):
    return n.bit_length() - 1


def device_bit(position):
    col_bits = bits(lax.axis_size("cols"))
    if position < col_bits:
        return "cols", position
    return "rows", position - col_bits


def own_bit(position):
    axis, bit = device_bit(position)
    return (lax.axis_index(axis) >> bit) % 2


def partner(x, position):
    axis, bit = device_bit(position)
    size = lax.axis_size(axis)
    return lax.ppermute(x, axis, [(i, i ^ (1 << bit)) for i in range(size)])


def exchange(to_lower, to_higher, axis, rider=None, rider_dim=0):
    size = lax.axis_size(axis)
    even = lax.axis_index(axis) % 2 == 0
    first = jnp.where(even, to_higher, to_lower)
    length = first.shape[rider_dim]
    if rider is not None:
        first = jnp.concatenate([first, rider], axis=rider_dim)
    got_first = lax.ppermute(first, axis, [(i, i ^ 1) for i in range(size)])
    links = [(i, i + 1) for i in range(1, size - 1, 2)] + [(i, i - 1) for i in range(2, size, 2)]
    got_second = lax.ppermute(jnp.where(even, to_lower, to_higher), axis, links)
    rider_got = None
    if rider is not None:
        rider_got = lax.slice_in_dim(got_first, length, None, axis=rider_dim)
        got_first = lax.slice_in_dim(got_first, 0, length, axis=rider_dim)
    from_lower = jnp.where(even, got_second, got_first)
    from_higher = jnp.where(even, got_first, got_second)
    return from_lower, from_higher, rider_got


def gather_step(x, other, position):
    low = own_bit(position) == 0
    return jnp.where(low, jnp.concatenate([x, other]), jnp.concatenate([other, x]))


def gather_order(order, count):
    where = np.zeros(count, np.int32)
    for l in range(count):
        where[l] = sum(((l >> bit) & 1) << step for step, bit in enumerate(order))
    return where


def scatter_split(x, order_left, position):
    axis = 1 + order_left.index(position)
    high = own_bit(position) == 1
    lower = lax.index_in_dim(x, 0, axis, keepdims=False)
    upper = lax.index_in_dim(x, 1, axis, keepdims=False)
    order_left.remove(position)
    return jnp.where(high, upper, lower), jnp.where(high, lower, upper)


def attention_kernel(
    own, first, last, per_step, q_ref, ko_ref, kh_ref, kg_ref, vo_ref, vh_ref, vg_ref, g_ref, mask_ref,
    o_ref, dq_ref, dkv_ref, wide_ref,
):
    head_size = q_ref.shape[1] // per_step
    score_scale = 1.0 / math.sqrt(head_size)
    q = (q_ref[...] * score_scale).astype(q_ref.dtype)
    k = jnp.concatenate([ko_ref[...], kh_ref[...], kg_ref[...]], axis=0)
    v = jnp.concatenate([vo_ref[...], vh_ref[...], vg_ref[...]], axis=0)
    g = g_ref[...]
    keep = mask_ref[...] > 0
    lane_head = lax.broadcasted_iota(jnp.int32, q.shape, 1) // head_size
    rows = (((1,), (1,)), ((), ()))
    cols = (((0,), (0,)), ((), ()))
    out = jnp.zeros(q.shape, jnp.float32)
    dq = jnp.zeros(q.shape, jnp.float32)
    dk = None
    dv = None
    for head in range(per_step):
        mine = lane_head == head
        q_head = jnp.where(mine, q, jnp.zeros_like(q))
        g_head = jnp.where(mine, g, jnp.zeros_like(g))
        scores = lax.dot_general(q_head, k, rows, preferred_element_type=jnp.float32)
        scores = jnp.where(keep, scores, -1e30)
        row_max = jnp.max(scores, axis=1, keepdims=True)
        exps = jnp.exp(scores - row_max)
        probs = exps * (1.0 / jnp.sum(exps, axis=1, keepdims=True))
        rounded = probs.astype(jnp.bfloat16)
        attended = jnp.dot(rounded, v, preferred_element_type=jnp.float32)
        attended = attended.astype(jnp.bfloat16).astype(jnp.float32)
        out = jnp.where(mine, attended, out)
        delta = jnp.sum(
            jnp.where(mine, g.astype(jnp.float32) * attended, 0.0), axis=1, keepdims=True
        )
        dots = lax.dot_general(g_head, v, rows, preferred_element_type=jnp.float32)
        slopes = (probs * (dots - delta)).astype(jnp.bfloat16)
        dq = jnp.where(
            mine, jnp.dot(slopes, k, preferred_element_type=jnp.float32) * score_scale, dq
        )
        dk_head = lax.dot_general(slopes, q_head, cols, preferred_element_type=jnp.float32)
        dv_head = lax.dot_general(rounded, g_head, cols, preferred_element_type=jnp.float32)
        dk = dk_head if dk is None else dk + dk_head
        dv = dv_head if dv is None else dv + dv_head
    o_ref[...] = out.astype(o_ref.dtype)
    dq_ref[...] = dq.astype(dq_ref.dtype)
    dkv_ref[0] = dk.astype(dkv_ref.dtype)
    dkv_ref[1] = dv.astype(dkv_ref.dtype)
    wide_ref[0, :own] = dk[:own]
    wide_ref[1, :own] = dv[:own]
    wide_ref[0, own:] = dk[first:last]
    wide_ref[1, own:] = dv[first:last]


def attention(queries, keys, values, global_keys, global_values, grad_attended, keep):
    tokens, model_width = queries.shape
    first = keys[0].shape[0] + keys[1].shape[0]
    last = first + global_keys.shape[0]
    key_count = last
    per_step = 4
    lanes = per_step * (model_width // HEADS)
    steps = model_width // lanes
    token_block = pl.BlockSpec((tokens, lanes), lambda i: (0, i))
    key_block = pl.BlockSpec((key_count, lanes), lambda i: (0, i))
    own_block = pl.BlockSpec((keys[0].shape[0], lanes), lambda i: (0, i))
    halo_block = pl.BlockSpec((keys[1].shape[0], lanes), lambda i: (0, i))
    global_block = pl.BlockSpec((last - first, lanes), lambda i: (0, i))
    mask_block = pl.BlockSpec((tokens, key_count), lambda i: (0, 0))
    grads_block = pl.BlockSpec((2, key_count, lanes), lambda i: (0, 0, i))
    wide_rows = tokens + last - first
    wide_block = pl.BlockSpec((2, wide_rows, lanes), lambda i: (0, 0, i))
    flops = 2 * 2 * 6 * tokens * key_count * model_width
    moved = 2 * (3 * tokens * model_width + 2 * key_count * model_width) + 4 * (
        tokens * key_count + 2 * key_count * model_width
    )
    return pl.pallas_call(
        functools.partial(attention_kernel, tokens, first, last, per_step),
        grid=(steps,),
        in_specs=[
            token_block,
            own_block,
            halo_block,
            global_block,
            own_block,
            halo_block,
            global_block,
            token_block,
            mask_block,
        ],
        out_specs=[token_block, token_block, grads_block, wide_block],
        out_shape=[
            jax.ShapeDtypeStruct((tokens, model_width), jnp.bfloat16),
            jax.ShapeDtypeStruct((tokens, model_width), jnp.bfloat16),
            jax.ShapeDtypeStruct((2, key_count, model_width), jnp.bfloat16),
            jax.ShapeDtypeStruct((2, wide_rows, model_width), jnp.float32),
        ],
        cost_estimate=pl.CostEstimate(
            flops=flops, transcendentals=HEADS * tokens * key_count, bytes_accessed=moved
        ),
    )(queries, *keys, global_keys, *values, global_values, grad_attended, keep)


def split_wide(x):
    high = x.astype(jnp.bfloat16)
    low = (x - high.astype(jnp.float32)).astype(jnp.bfloat16)
    return jnp.concatenate([high, low], axis=0)


def join_wide(pair):
    half = pair.shape[0] // 2
    return pair[:half].astype(jnp.float32) + pair[half:].astype(jnp.float32)


def shards(features, w_query, w_key, w_value, w_out, reg_pos, grad_out):
    tile_rows, tile_cols, model_width = features.shape
    row_count = lax.axis_size("rows")
    col_count = lax.axis_size("cols")
    row_index = lax.axis_index("rows")
    col_index = lax.axis_index("cols")
    band_rows = tile_rows * row_count
    band_cols = tile_cols * col_count
    first_row = row_index * tile_rows
    first_col = col_index * tile_cols
    tokens = tile_rows * tile_cols
    device_count = row_count * col_count
    col_bits = bits(col_count)
    all_bits = col_bits + bits(row_count)
    ext_rows = tile_rows + 2 * RAD
    band_keys = RAD * tile_cols
    strip_keys = ext_rows * RAD
    frame_keys = tokens + 2 * band_keys + 2 * strip_keys
    used = frame_keys + device_count
    key_count = -(-used // 128) * 128

    flat_tokens = features.reshape(-1, model_width)
    own_keys = jnp.dot(flat_tokens, w_key, preferred_element_type=jnp.float32).astype(jnp.bfloat16)
    own_values = jnp.dot(flat_tokens, w_value, preferred_element_type=jnp.float32).astype(
        jnp.bfloat16
    )

    own_index = row_index * col_count + col_index
    own_place = lax.dynamic_index_in_dim(reg_pos, own_index, 0, keepdims=False)
    own_local = (own_place // band_cols - first_row) * tile_cols + (own_place % band_cols - first_col)
    gathered = jnp.concatenate(
        [
            lax.dynamic_slice_in_dim(own_keys, own_local, 1, 0),
            lax.dynamic_slice_in_dim(own_values, own_local, 1, 0),
        ],
        axis=1,
    )
    order = [col_bits, 0] + list(range(1, col_bits)) + list(range(col_bits + 1, all_bits))

    from_above, from_below, got = exchange(
        features[:RAD].reshape(-1, model_width),
        features[tile_rows - RAD :].reshape(-1, model_width),
        "rows",
        gathered.reshape(-1, model_width),
    )
    gathered = gather_step(gathered, got.reshape(gathered.shape), order[0])
    extended = jnp.concatenate(
        [
            from_above.reshape(RAD, tile_cols, model_width),
            features,
            from_below.reshape(RAD, tile_cols, model_width),
        ],
        axis=0,
    )
    from_left, from_right, got = exchange(
        extended[:, :RAD].reshape(-1, model_width),
        extended[:, tile_cols - RAD :].reshape(-1, model_width),
        "cols",
        gathered.reshape(-1, model_width),
    )
    gathered = gather_step(gathered, got.reshape(gathered.shape), order[1])

    queries = jnp.dot(flat_tokens, w_query, preferred_element_type=jnp.float32).astype(jnp.bfloat16)
    grad_attended = jnp.dot(
        grad_out.reshape(-1, model_width), w_out.T, preferred_element_type=jnp.float32
    ).astype(jnp.bfloat16)

    halo_features = jnp.concatenate(
        [
            from_above,
            from_below,
            from_left,
            from_right,
            jnp.zeros((key_count - used, model_width), features.dtype),
        ],
        axis=0,
    )
    halo_keys = jnp.dot(halo_features, w_key, preferred_element_type=jnp.float32).astype(
        jnp.bfloat16
    )
    halo_values = jnp.dot(halo_features, w_value, preferred_element_type=jnp.float32).astype(
        jnp.bfloat16
    )

    for position in order[2:]:
        gathered = gather_step(gathered, partner(gathered, position), position)
    global_kv = jnp.take(gathered, jnp.asarray(gather_order(order, device_count)), axis=0)
    global_keys = global_kv[:, :model_width]
    global_values = global_kv[:, model_width:]

    def grid(height, width, row0, col0):
        a, b = np.meshgrid(np.arange(height) + row0, np.arange(width) + col0, indexing="ij")
        return a.reshape(-1), b.reshape(-1)

    parts = [
        grid(tile_rows, tile_cols, RAD, RAD),
        grid(RAD, tile_cols, 0, RAD),
        grid(RAD, tile_cols, RAD + tile_rows, RAD),
        grid(ext_rows, RAD, 0, 0),
        grid(ext_rows, RAD, 0, RAD + tile_cols),
    ]
    key_rows = np.zeros(key_count, np.int32)
    key_cols = np.zeros(key_count, np.int32)
    key_rows[:frame_keys] = np.concatenate([p[0] for p in parts])
    key_cols[:frame_keys] = np.concatenate([p[1] for p in parts])
    kind = np.full(key_count, 2, np.int32)
    kind[:frame_keys] = 0
    kind[key_count - device_count :] = 1

    query_rows = first_row + jnp.repeat(jnp.arange(tile_rows, dtype=jnp.int32), tile_cols)
    query_cols = first_col + jnp.tile(jnp.arange(tile_cols, dtype=jnp.int32), tile_rows)
    start_rows = jnp.clip(query_rows - RAD, 0, band_rows - KW)[:, None]
    start_cols = jnp.clip(query_cols - RAD, 0, band_cols - KW)[:, None]
    cell_rows = (first_row - RAD + jnp.asarray(key_rows))[None, :]
    cell_cols = (first_col - RAD + jnp.asarray(key_cols))[None, :]
    inside = (
        (cell_rows >= start_rows)
        & (cell_rows < start_rows + KW)
        & (cell_cols >= start_cols)
        & (cell_cols < start_cols + KW)
    )
    key_kind = jnp.asarray(kind)[None, :]
    keep = ((inside & (key_kind == 0)) | (key_kind == 1)).astype(jnp.float32)

    attended, query_grads, rounded_grads, wide_grads = attention(
        queries,
        (own_keys, halo_keys),
        (own_values, halo_values),
        global_keys,
        global_values,
        grad_attended,
        keep,
    )
    layer_out = (
        jnp.dot(attended, w_out, preferred_element_type=jnp.float32)
        .astype(jnp.bfloat16)
        .reshape(features.shape)
    )

    strips_from = tokens + 2 * band_keys

    def contribution(lo, hi):
        return jnp.dot(
            rounded_grads[0, lo:hi], w_key.T, preferred_element_type=jnp.float32
        ) + jnp.dot(rounded_grads[1, lo:hi], w_value.T, preferred_element_type=jnp.float32)

    strip_given = contribution(strips_from, frame_keys)
    rest_given = contribution(0, strips_from)

    def given(lo, hi):
        if lo >= strips_from:
            return strip_given[lo - strips_from : hi - strips_from]
        return rest_given[lo:hi]

    scatter = wide_grads[:, tokens:].reshape(
        (2,) + (2,) * all_bits + (model_width,)
    )
    left = list(range(all_bits - 1, -1, -1))
    back_order = [0, col_bits] + list(range(1, col_bits)) + list(range(col_bits + 1, all_bits))

    keep_part, send_part = scatter_split(scatter, left, back_order[0])
    strip_shape = (ext_rows, RAD, model_width)
    from_left, from_right, got = exchange(
        given(strips_from, strips_from + strip_keys).astype(jnp.bfloat16),
        given(strips_from + strip_keys, frame_keys).astype(jnp.bfloat16),
        "cols",
        split_wide(send_part.reshape(-1, model_width)),
    )
    scatter = keep_part + join_wide(got).reshape(keep_part.shape)
    received = jnp.pad(
        from_left.astype(jnp.float32).reshape(strip_shape), ((0, 0), (0, tile_cols - RAD), (0, 0))
    ) + jnp.pad(
        from_right.astype(jnp.float32).reshape(strip_shape), ((0, 0), (tile_cols - RAD, 0), (0, 0))
    )
    band_shape = (RAD, tile_cols, model_width)
    keep_part, send_part = scatter_split(scatter, left, back_order[1])
    from_above, from_below, got = exchange(
        (given(tokens, tokens + band_keys).reshape(band_shape) + received[:RAD])
        .reshape(-1, model_width)
        .astype(jnp.bfloat16),
        (given(tokens + band_keys, strips_from).reshape(band_shape) + received[RAD + tile_rows :])
        .reshape(-1, model_width)
        .astype(jnp.bfloat16),
        "rows",
        split_wide(send_part.reshape(-1, model_width)),
    )
    scatter = keep_part + join_wide(got).reshape(keep_part.shape)
    received = received[RAD : RAD + tile_rows]
    received = received + jnp.pad(
        from_above.astype(jnp.float32).reshape(band_shape), ((0, tile_rows - RAD), (0, 0), (0, 0))
    )
    received = received + jnp.pad(
        from_below.astype(jnp.float32).reshape(band_shape), ((tile_rows - RAD, 0), (0, 0), (0, 0))
    )
    for position in back_order[2:]:
        keep_part, send_part = scatter_split(scatter, left, position)
        scatter = keep_part + partner(send_part, position)
    own_grads = scatter.reshape(2, 1, model_width)

    own_given = given(0, tokens)
    own_row = (lax.dynamic_slice_in_dim(wide_grads, own_local, 1, 1) + own_grads).astype(
        jnp.bfloat16
    )
    own_row_given = jnp.dot(own_row[0], w_key.T, preferred_element_type=jnp.float32) + jnp.dot(
        own_row[1], w_value.T, preferred_element_type=jnp.float32
    )
    own_given = lax.dynamic_update_slice_in_dim(own_given, own_row_given, own_local, 0)

    grad_in = (
        jnp.dot(query_grads, w_query.T, preferred_element_type=jnp.float32)
        + own_given
        + received.reshape(tokens, model_width)
    )
    grad_in = grad_in.astype(jnp.bfloat16).reshape(features.shape)
    return (layer_out, grad_in)


def solution(mesh):
    placed = (P("rows", "cols", None), P(), P(), P(), P(), P(), P("rows", "cols", None))
    return jax.shard_map(
        shards,
        mesh=mesh,
        in_specs=placed,
        out_specs=(P("rows", "cols", None), P("rows", "cols", None)),
        check_vma=False,
    )
```

```python
import functools
import math

import jax
import jax.numpy as jnp
import numpy as np
from jax import lax
from jax.experimental import pallas as pl
from jax.sharding import PartitionSpec as P

HEADS = 16
KW = 13
RAD = 6


def bits(n):
    return n.bit_length() - 1


def device_bit(position):
    col_bits = bits(lax.axis_size("cols"))
    if position < col_bits:
        return "cols", position
    return "rows", position - col_bits


def own_bit(position):
    axis, bit = device_bit(position)
    return (lax.axis_index(axis) >> bit) % 2


def partner(x, position):
    axis, bit = device_bit(position)
    size = lax.axis_size(axis)
    return lax.ppermute(x, axis, [(i, i ^ (1 << bit)) for i in range(size)])


def exchange(to_lower, to_higher, axis, rider=None, rider_dim=0):
    size = lax.axis_size(axis)
    even = lax.axis_index(axis) % 2 == 0
    first = jnp.where(even, to_higher, to_lower)
    length = first.shape[rider_dim]
    if rider is not None:
        first = jnp.concatenate([first, rider], axis=rider_dim)
    got_first = lax.ppermute(first, axis, [(i, i ^ 1) for i in range(size)])
    links = [(i, i + 1) for i in range(1, size - 1, 2)] + [(i, i - 1) for i in range(2, size, 2)]
    got_second = lax.ppermute(jnp.where(even, to_lower, to_higher), axis, links)
    rider_got = None
    if rider is not None:
        rider_got = lax.slice_in_dim(got_first, length, None, axis=rider_dim)
        got_first = lax.slice_in_dim(got_first, 0, length, axis=rider_dim)
    from_lower = jnp.where(even, got_second, got_first)
    from_higher = jnp.where(even, got_first, got_second)
    return from_lower, from_higher, rider_got


def gather_step(x, other, position):
    low = own_bit(position) == 0
    return jnp.where(low, jnp.concatenate([x, other]), jnp.concatenate([other, x]))


def gather_order(order, count):
    where = np.zeros(count, np.int32)
    for l in range(count):
        where[l] = sum(((l >> bit) & 1) << step for step, bit in enumerate(order))
    return where


def scatter_split(x, order_left, position):
    axis = 1 + order_left.index(position)
    high = own_bit(position) == 1
    lower = lax.index_in_dim(x, 0, axis, keepdims=False)
    upper = lax.index_in_dim(x, 1, axis, keepdims=False)
    order_left.remove(position)
    return jnp.where(high, upper, lower), jnp.where(high, lower, upper)


def attention_kernel(
    own, first, last, q_ref, ko_ref, kh_ref, kg_ref, vo_ref, vh_ref, vg_ref, g_ref, mask_ref,
    o_ref, dq_ref, dkv_ref, wide_ref,
):
    head_size = q_ref.shape[1] // 2
    score_scale = 1.0 / math.sqrt(head_size)
    q = (q_ref[...] * score_scale).astype(q_ref.dtype)
    k = jnp.concatenate([ko_ref[...], kh_ref[...], kg_ref[...]], axis=0)
    v = jnp.concatenate([vo_ref[...], vh_ref[...], vg_ref[...]], axis=0)
    g = g_ref[...]
    keep = mask_ref[...] > 0
    lane_head = lax.broadcasted_iota(jnp.int32, q.shape, 1) // head_size
    rows = (((1,), (1,)), ((), ()))
    cols = (((0,), (0,)), ((), ()))
    out = jnp.zeros(q.shape, jnp.float32)
    dq = jnp.zeros(q.shape, jnp.float32)
    dk = None
    dv = None
    for head in range(2):
        mine = lane_head == head
        q_head = jnp.where(mine, q, jnp.zeros_like(q))
        g_head = jnp.where(mine, g, jnp.zeros_like(g))
        lanes = slice(head * head_size, (head + 1) * head_size)
        scores = lax.dot_general(q[:, lanes], k[:, lanes], rows, preferred_element_type=jnp.float32)
        scores = jnp.where(keep, scores, -1e30)
        row_max = jnp.max(scores, axis=1, keepdims=True)
        exps = jnp.exp(scores - row_max)
        probs = exps * (1.0 / jnp.sum(exps, axis=1, keepdims=True))
        rounded = probs.astype(jnp.bfloat16)
        attended = jnp.dot(rounded, v, preferred_element_type=jnp.float32)
        attended = attended.astype(jnp.bfloat16).astype(jnp.float32)
        out = jnp.where(mine, attended, out)
        delta = jnp.sum(
            jnp.where(mine, g.astype(jnp.float32) * attended, 0.0), axis=1, keepdims=True
        )
        dots = lax.dot_general(g[:, lanes], v[:, lanes], rows, preferred_element_type=jnp.float32)
        slopes = (probs * (dots - delta)).astype(jnp.bfloat16)
        dq = jnp.where(
            mine, jnp.dot(slopes, k, preferred_element_type=jnp.float32) * score_scale, dq
        )
        dk_head = lax.dot_general(slopes, q_head, cols, preferred_element_type=jnp.float32)
        dv_head = lax.dot_general(rounded, g_head, cols, preferred_element_type=jnp.float32)
        dk = dk_head if dk is None else dk + dk_head
        dv = dv_head if dv is None else dv + dv_head
    o_ref[...] = out.astype(o_ref.dtype)
    dq_ref[...] = dq.astype(dq_ref.dtype)
    dkv_ref[0] = dk.astype(dkv_ref.dtype)
    dkv_ref[1] = dv.astype(dkv_ref.dtype)
    wide_ref[0, :own] = dk[:own]
    wide_ref[1, :own] = dv[:own]
    wide_ref[0, own:] = dk[first:last]
    wide_ref[1, own:] = dv[first:last]


def attention(queries, keys, values, global_keys, global_values, grad_attended, keep):
    tokens, model_width = queries.shape
    first = keys[0].shape[0] + keys[1].shape[0]
    last = first + global_keys.shape[0]
    key_count = last
    lanes = 2 * (model_width // HEADS)
    steps = model_width // lanes
    token_block = pl.BlockSpec((tokens, lanes), lambda i: (0, i))
    key_block = pl.BlockSpec((key_count, lanes), lambda i: (0, i))
    own_block = pl.BlockSpec((keys[0].shape[0], lanes), lambda i: (0, i))
    halo_block = pl.BlockSpec((keys[1].shape[0], lanes), lambda i: (0, i))
    global_block = pl.BlockSpec((last - first, lanes), lambda i: (0, i))
    mask_block = pl.BlockSpec((tokens, key_count), lambda i: (0, 0))
    grads_block = pl.BlockSpec((2, key_count, lanes), lambda i: (0, 0, i))
    wide_rows = tokens + last - first
    wide_block = pl.BlockSpec((2, wide_rows, lanes), lambda i: (0, 0, i))
    flops = 2 * 2 * 6 * tokens * key_count * model_width
    moved = 2 * (3 * tokens * model_width + 2 * key_count * model_width) + 4 * (
        tokens * key_count + 2 * key_count * model_width
    )
    return pl.pallas_call(
        functools.partial(attention_kernel, tokens, first, last),
        grid=(steps,),
        in_specs=[
            token_block,
            own_block,
            halo_block,
            global_block,
            own_block,
            halo_block,
            global_block,
            token_block,
            mask_block,
        ],
        out_specs=[token_block, token_block, grads_block, wide_block],
        out_shape=[
            jax.ShapeDtypeStruct((tokens, model_width), jnp.bfloat16),
            jax.ShapeDtypeStruct((tokens, model_width), jnp.bfloat16),
            jax.ShapeDtypeStruct((2, key_count, model_width), jnp.bfloat16),
            jax.ShapeDtypeStruct((2, wide_rows, model_width), jnp.float32),
        ],
        cost_estimate=pl.CostEstimate(
            flops=flops, transcendentals=HEADS * tokens * key_count, bytes_accessed=moved
        ),
    )(queries, *keys, global_keys, *values, global_values, grad_attended, keep)


def split_wide(x):
    high = x.astype(jnp.bfloat16)
    low = (x - high.astype(jnp.float32)).astype(jnp.bfloat16)
    return jnp.concatenate([high, low], axis=0)


def join_wide(pair):
    half = pair.shape[0] // 2
    return pair[:half].astype(jnp.float32) + pair[half:].astype(jnp.float32)


def shards(features, w_query, w_key, w_value, w_out, reg_pos, grad_out):
    tile_rows, tile_cols, model_width = features.shape
    row_count = lax.axis_size("rows")
    col_count = lax.axis_size("cols")
    row_index = lax.axis_index("rows")
    col_index = lax.axis_index("cols")
    band_rows = tile_rows * row_count
    band_cols = tile_cols * col_count
    first_row = row_index * tile_rows
    first_col = col_index * tile_cols
    tokens = tile_rows * tile_cols
    device_count = row_count * col_count
    col_bits = bits(col_count)
    all_bits = col_bits + bits(row_count)
    ext_rows = tile_rows + 2 * RAD
    band_keys = RAD * tile_cols
    strip_keys = ext_rows * RAD
    frame_keys = tokens + 2 * band_keys + 2 * strip_keys
    used = frame_keys + device_count
    key_count = -(-used // 128) * 128

    flat_tokens = features.reshape(-1, model_width)
    own_keys = jnp.dot(flat_tokens, w_key, preferred_element_type=jnp.float32).astype(jnp.bfloat16)
    own_values = jnp.dot(flat_tokens, w_value, preferred_element_type=jnp.float32).astype(
        jnp.bfloat16
    )

    own_index = row_index * col_count + col_index
    own_place = lax.dynamic_index_in_dim(reg_pos, own_index, 0, keepdims=False)
    own_local = (own_place // band_cols - first_row) * tile_cols + (own_place % band_cols - first_col)
    gathered = jnp.concatenate(
        [
            lax.dynamic_slice_in_dim(own_keys, own_local, 1, 0),
            lax.dynamic_slice_in_dim(own_values, own_local, 1, 0),
        ],
        axis=1,
    )
    order = [col_bits, 0] + list(range(1, col_bits)) + list(range(col_bits + 1, all_bits))

    from_above, from_below, got = exchange(
        features[:RAD].reshape(-1, model_width),
        features[tile_rows - RAD :].reshape(-1, model_width),
        "rows",
        gathered.reshape(-1, model_width),
    )
    gathered = gather_step(gathered, got.reshape(gathered.shape), order[0])
    extended = jnp.concatenate(
        [
            from_above.reshape(RAD, tile_cols, model_width),
            features,
            from_below.reshape(RAD, tile_cols, model_width),
        ],
        axis=0,
    )
    from_left, from_right, got = exchange(
        extended[:, :RAD].reshape(-1, model_width),
        extended[:, tile_cols - RAD :].reshape(-1, model_width),
        "cols",
        gathered.reshape(-1, model_width),
    )
    gathered = gather_step(gathered, got.reshape(gathered.shape), order[1])

    queries = jnp.dot(flat_tokens, w_query, preferred_element_type=jnp.float32).astype(jnp.bfloat16)
    grad_attended = jnp.dot(
        grad_out.reshape(-1, model_width), w_out.T, preferred_element_type=jnp.float32
    ).astype(jnp.bfloat16)

    halo_features = jnp.concatenate(
        [
            from_above,
            from_below,
            from_left,
            from_right,
            jnp.zeros((key_count - used, model_width), features.dtype),
        ],
        axis=0,
    )
    halo_keys = jnp.dot(halo_features, w_key, preferred_element_type=jnp.float32).astype(
        jnp.bfloat16
    )
    halo_values = jnp.dot(halo_features, w_value, preferred_element_type=jnp.float32).astype(
        jnp.bfloat16
    )

    for position in order[2:]:
        gathered = gather_step(gathered, partner(gathered, position), position)
    global_kv = jnp.take(gathered, jnp.asarray(gather_order(order, device_count)), axis=0)
    global_keys = global_kv[:, :model_width]
    global_values = global_kv[:, model_width:]

    def grid(height, width, row0, col0):
        a, b = np.meshgrid(np.arange(height) + row0, np.arange(width) + col0, indexing="ij")
        return a.reshape(-1), b.reshape(-1)

    parts = [
        grid(tile_rows, tile_cols, RAD, RAD),
        grid(RAD, tile_cols, 0, RAD),
        grid(RAD, tile_cols, RAD + tile_rows, RAD),
        grid(ext_rows, RAD, 0, 0),
        grid(ext_rows, RAD, 0, RAD + tile_cols),
    ]
    key_rows = np.zeros(key_count, np.int32)
    key_cols = np.zeros(key_count, np.int32)
    key_rows[:frame_keys] = np.concatenate([p[0] for p in parts])
    key_cols[:frame_keys] = np.concatenate([p[1] for p in parts])
    kind = np.full(key_count, 2, np.int32)
    kind[:frame_keys] = 0
    kind[key_count - device_count :] = 1

    query_rows = first_row + jnp.repeat(jnp.arange(tile_rows, dtype=jnp.int32), tile_cols)
    query_cols = first_col + jnp.tile(jnp.arange(tile_cols, dtype=jnp.int32), tile_rows)
    start_rows = jnp.clip(query_rows - RAD, 0, band_rows - KW)[:, None]
    start_cols = jnp.clip(query_cols - RAD, 0, band_cols - KW)[:, None]
    cell_rows = (first_row - RAD + jnp.asarray(key_rows))[None, :]
    cell_cols = (first_col - RAD + jnp.asarray(key_cols))[None, :]
    inside = (
        (cell_rows >= start_rows)
        & (cell_rows < start_rows + KW)
        & (cell_cols >= start_cols)
        & (cell_cols < start_cols + KW)
    )
    key_kind = jnp.asarray(kind)[None, :]
    keep = ((inside & (key_kind == 0)) | (key_kind == 1)).astype(jnp.float32)

    attended, query_grads, rounded_grads, wide_grads = attention(
        queries,
        (own_keys, halo_keys),
        (own_values, halo_values),
        global_keys,
        global_values,
        grad_attended,
        keep,
    )
    layer_out = (
        jnp.dot(attended, w_out, preferred_element_type=jnp.float32)
        .astype(jnp.bfloat16)
        .reshape(features.shape)
    )

    strips_from = tokens + 2 * band_keys

    def contribution(lo, hi):
        return jnp.dot(
            rounded_grads[0, lo:hi], w_key.T, preferred_element_type=jnp.float32
        ) + jnp.dot(rounded_grads[1, lo:hi], w_value.T, preferred_element_type=jnp.float32)

    strip_given = contribution(strips_from, frame_keys)
    rest_given = contribution(0, strips_from)

    def given(lo, hi):
        if lo >= strips_from:
            return strip_given[lo - strips_from : hi - strips_from]
        return rest_given[lo:hi]

    scatter = wide_grads[:, tokens:].reshape(
        (2,) + (2,) * all_bits + (model_width,)
    )
    left = list(range(all_bits - 1, -1, -1))
    back_order = [0, col_bits] + list(range(1, col_bits)) + list(range(col_bits + 1, all_bits))

    keep_part, send_part = scatter_split(scatter, left, back_order[0])
    strip_shape = (ext_rows, RAD, model_width)
    from_left, from_right, got = exchange(
        given(strips_from, strips_from + strip_keys).astype(jnp.bfloat16),
        given(strips_from + strip_keys, frame_keys).astype(jnp.bfloat16),
        "cols",
        split_wide(send_part.reshape(-1, model_width)),
    )
    scatter = keep_part + join_wide(got).reshape(keep_part.shape)
    received = jnp.pad(
        from_left.astype(jnp.float32).reshape(strip_shape), ((0, 0), (0, tile_cols - RAD), (0, 0))
    ) + jnp.pad(
        from_right.astype(jnp.float32).reshape(strip_shape), ((0, 0), (tile_cols - RAD, 0), (0, 0))
    )
    band_shape = (RAD, tile_cols, model_width)
    keep_part, send_part = scatter_split(scatter, left, back_order[1])
    from_above, from_below, got = exchange(
        (given(tokens, tokens + band_keys).reshape(band_shape) + received[:RAD])
        .reshape(-1, model_width)
        .astype(jnp.bfloat16),
        (given(tokens + band_keys, strips_from).reshape(band_shape) + received[RAD + tile_rows :])
        .reshape(-1, model_width)
        .astype(jnp.bfloat16),
        "rows",
        split_wide(send_part.reshape(-1, model_width)),
    )
    scatter = keep_part + join_wide(got).reshape(keep_part.shape)
    received = received[RAD : RAD + tile_rows]
    received = received + jnp.pad(
        from_above.astype(jnp.float32).reshape(band_shape), ((0, tile_rows - RAD), (0, 0), (0, 0))
    )
    received = received + jnp.pad(
        from_below.astype(jnp.float32).reshape(band_shape), ((tile_rows - RAD, 0), (0, 0), (0, 0))
    )
    for position in back_order[2:]:
        keep_part, send_part = scatter_split(scatter, left, position)
        scatter = keep_part + partner(send_part, position)
    own_grads = scatter.reshape(2, 1, model_width)

    own_given = given(0, tokens)
    own_row = (lax.dynamic_slice_in_dim(wide_grads, own_local, 1, 1) + own_grads).astype(
        jnp.bfloat16
    )
    own_row_given = jnp.dot(own_row[0], w_key.T, preferred_element_type=jnp.float32) + jnp.dot(
        own_row[1], w_value.T, preferred_element_type=jnp.float32
    )
    own_given = lax.dynamic_update_slice_in_dim(own_given, own_row_given, own_local, 0)

    grad_in = (
        jnp.dot(query_grads, w_query.T, preferred_element_type=jnp.float32)
        + own_given
        + received.reshape(tokens, model_width)
    )
    grad_in = grad_in.astype(jnp.bfloat16).reshape(features.shape)
    return (layer_out, grad_in)


def solution(mesh):
    placed = (P("rows", "cols", None), P(), P(), P(), P(), P(), P("rows", "cols", None))
    return jax.shard_map(
        shards,
        mesh=mesh,
        in_specs=placed,
        out_specs=(P("rows", "cols", None), P("rows", "cols", None)),
        check_vma=False,
    )
```

```python
import functools
import math

import jax
import jax.numpy as jnp
import numpy as np
from jax import lax
from jax.experimental import pallas as pl
from jax.sharding import PartitionSpec as P

HEADS = 16
KW = 13
RAD = 6


def bits(n):
    return n.bit_length() - 1


def device_bit(position):
    col_bits = bits(lax.axis_size("cols"))
    if position < col_bits:
        return "cols", position
    return "rows", position - col_bits


def own_bit(position):
    axis, bit = device_bit(position)
    return (lax.axis_index(axis) >> bit) % 2


def partner(x, position):
    axis, bit = device_bit(position)
    size = lax.axis_size(axis)
    return lax.ppermute(x, axis, [(i, i ^ (1 << bit)) for i in range(size)])


def exchange(to_lower, to_higher, axis, rider=None, rider_dim=0):
    size = lax.axis_size(axis)
    even = lax.axis_index(axis) % 2 == 0
    picked = None
    if isinstance(to_lower, tuple):
        source, dim, low_at, high_at, count = to_lower
        take = lambda at: lax.dynamic_slice_in_dim(source, at, count, dim)
        picked = (take(jnp.where(even, high_at, low_at)), take(jnp.where(even, low_at, high_at)))
        to_lower = to_higher = None
    first = picked[0] if picked else jnp.where(even, to_higher, to_lower)
    length = first.shape[rider_dim]
    if rider is not None:
        first = jnp.concatenate([first, rider], axis=rider_dim)
    got_first = lax.ppermute(first, axis, [(i, i ^ 1) for i in range(size)])
    links = [(i, i + 1) for i in range(1, size - 1, 2)] + [(i, i - 1) for i in range(2, size, 2)]
    second = picked[1] if picked else jnp.where(even, to_lower, to_higher)
    got_second = lax.ppermute(second, axis, links)
    rider_got = None
    if rider is not None:
        rider_got = lax.slice_in_dim(got_first, length, None, axis=rider_dim)
        got_first = lax.slice_in_dim(got_first, 0, length, axis=rider_dim)
    from_lower = jnp.where(even, got_second, got_first)
    from_higher = jnp.where(even, got_first, got_second)
    return from_lower, from_higher, rider_got


def gather_step(x, other, position):
    low = own_bit(position) == 0
    return jnp.where(low, jnp.concatenate([x, other]), jnp.concatenate([other, x]))


def gather_order(order, count):
    where = np.zeros(count, np.int32)
    for l in range(count):
        where[l] = sum(((l >> bit) & 1) << step for step, bit in enumerate(order))
    return where


def scatter_split(x, order_left, position):
    axis = 1 + order_left.index(position)
    high = own_bit(position) == 1
    lower = lax.index_in_dim(x, 0, axis, keepdims=False)
    upper = lax.index_in_dim(x, 1, axis, keepdims=False)
    order_left.remove(position)
    return jnp.where(high, upper, lower), jnp.where(high, lower, upper)


def attention_kernel(
    own, first, last, q_ref, ko_ref, kh_ref, kg_ref, vo_ref, vh_ref, vg_ref, g_ref, mask_ref,
    o_ref, dq_ref, dkv_ref, wide_ref,
):
    head_size = q_ref.shape[1] // 2
    score_scale = 1.0 / math.sqrt(head_size)
    q = (q_ref[...] * score_scale).astype(q_ref.dtype)
    k = jnp.concatenate([ko_ref[...], kh_ref[...], kg_ref[...]], axis=0)
    v = jnp.concatenate([vo_ref[...], vh_ref[...], vg_ref[...]], axis=0)
    g = g_ref[...]
    keep = mask_ref[...] > 0
    lane_head = lax.broadcasted_iota(jnp.int32, q.shape, 1) // head_size
    rows = (((1,), (1,)), ((), ()))
    cols = (((0,), (0,)), ((), ()))
    out = jnp.zeros(q.shape, jnp.float32)
    dq = jnp.zeros(q.shape, jnp.float32)
    dk = None
    dv = None
    for head in range(2):
        mine = lane_head == head
        q_head = jnp.where(mine, q, jnp.zeros_like(q))
        g_head = jnp.where(mine, g, jnp.zeros_like(g))
        scores = lax.dot_general(q_head, k, rows, preferred_element_type=jnp.float32)
        scores = jnp.where(keep, scores, -1e30)
        row_max = jnp.max(scores, axis=1, keepdims=True)
        exps = jnp.exp(scores - row_max)
        probs = exps * (1.0 / jnp.sum(exps, axis=1, keepdims=True))
        rounded = probs.astype(jnp.bfloat16)
        attended = jnp.dot(rounded, v, preferred_element_type=jnp.float32)
        attended = attended.astype(jnp.bfloat16).astype(jnp.float32)
        out = jnp.where(mine, attended, out)
        delta = jnp.sum(
            jnp.where(mine, g.astype(jnp.float32) * attended, 0.0), axis=1, keepdims=True
        )
        dots = lax.dot_general(g_head, v, rows, preferred_element_type=jnp.float32)
        slopes = (probs * (dots - delta)).astype(jnp.bfloat16)
        dq = jnp.where(
            mine, jnp.dot(slopes, k, preferred_element_type=jnp.float32) * score_scale, dq
        )
        dk_head = lax.dot_general(slopes, q_head, cols, preferred_element_type=jnp.float32)
        dv_head = lax.dot_general(rounded, g_head, cols, preferred_element_type=jnp.float32)
        dk = dk_head if dk is None else dk + dk_head
        dv = dv_head if dv is None else dv + dv_head
    o_ref[...] = out.astype(o_ref.dtype)
    dq_ref[...] = dq.astype(dq_ref.dtype)
    dkv_ref[0] = dk.astype(dkv_ref.dtype)
    dkv_ref[1] = dv.astype(dkv_ref.dtype)
    wide_ref[0, :own] = dk[:own]
    wide_ref[1, :own] = dv[:own]
    wide_ref[0, own:] = dk[first:last]
    wide_ref[1, own:] = dv[first:last]


def attention(queries, keys, values, global_keys, global_values, grad_attended, keep):
    tokens, model_width = queries.shape
    first = keys[0].shape[0] + keys[1].shape[0]
    last = first + global_keys.shape[0]
    key_count = last
    lanes = 2 * (model_width // HEADS)
    steps = model_width // lanes
    token_block = pl.BlockSpec((tokens, lanes), lambda i: (0, i))
    key_block = pl.BlockSpec((key_count, lanes), lambda i: (0, i))
    own_block = pl.BlockSpec((keys[0].shape[0], lanes), lambda i: (0, i))
    halo_block = pl.BlockSpec((keys[1].shape[0], lanes), lambda i: (0, i))
    global_block = pl.BlockSpec((last - first, lanes), lambda i: (0, i))
    mask_block = pl.BlockSpec((tokens, key_count), lambda i: (0, 0))
    grads_block = pl.BlockSpec((2, key_count, lanes), lambda i: (0, 0, i))
    wide_rows = tokens + last - first
    wide_block = pl.BlockSpec((2, wide_rows, lanes), lambda i: (0, 0, i))
    flops = 2 * 2 * 6 * tokens * key_count * model_width
    moved = 2 * (3 * tokens * model_width + 2 * key_count * model_width) + 4 * (
        tokens * key_count + 2 * key_count * model_width
    )
    return pl.pallas_call(
        functools.partial(attention_kernel, tokens, first, last),
        grid=(steps,),
        in_specs=[
            token_block,
            own_block,
            halo_block,
            global_block,
            own_block,
            halo_block,
            global_block,
            token_block,
            mask_block,
        ],
        out_specs=[token_block, token_block, grads_block, wide_block],
        out_shape=[
            jax.ShapeDtypeStruct((tokens, model_width), jnp.bfloat16),
            jax.ShapeDtypeStruct((tokens, model_width), jnp.bfloat16),
            jax.ShapeDtypeStruct((2, key_count, model_width), jnp.bfloat16),
            jax.ShapeDtypeStruct((2, wide_rows, model_width), jnp.float32),
        ],
        cost_estimate=pl.CostEstimate(
            flops=flops, transcendentals=HEADS * tokens * key_count, bytes_accessed=moved
        ),
    )(queries, *keys, global_keys, *values, global_values, grad_attended, keep)


def split_wide(x):
    high = x.astype(jnp.bfloat16)
    low = (x - high.astype(jnp.float32)).astype(jnp.bfloat16)
    return jnp.concatenate([high, low], axis=0)


def join_wide(pair):
    half = pair.shape[0] // 2
    return pair[:half].astype(jnp.float32) + pair[half:].astype(jnp.float32)


def shards(features, w_query, w_key, w_value, w_out, reg_pos, grad_out):
    tile_rows, tile_cols, model_width = features.shape
    row_count = lax.axis_size("rows")
    col_count = lax.axis_size("cols")
    row_index = lax.axis_index("rows")
    col_index = lax.axis_index("cols")
    band_rows = tile_rows * row_count
    band_cols = tile_cols * col_count
    first_row = row_index * tile_rows
    first_col = col_index * tile_cols
    tokens = tile_rows * tile_cols
    device_count = row_count * col_count
    col_bits = bits(col_count)
    all_bits = col_bits + bits(row_count)
    ext_rows = tile_rows + 2 * RAD
    band_keys = RAD * tile_cols
    strip_keys = ext_rows * RAD
    frame_keys = tokens + 2 * band_keys + 2 * strip_keys
    used = frame_keys + device_count
    key_count = -(-used // 128) * 128

    flat_tokens = features.reshape(-1, model_width)
    own_keys = jnp.dot(flat_tokens, w_key, preferred_element_type=jnp.float32).astype(jnp.bfloat16)
    own_values = jnp.dot(flat_tokens, w_value, preferred_element_type=jnp.float32).astype(
        jnp.bfloat16
    )

    own_index = row_index * col_count + col_index
    own_place = lax.dynamic_index_in_dim(reg_pos, own_index, 0, keepdims=False)
    own_local = (own_place // band_cols - first_row) * tile_cols + (own_place % band_cols - first_col)
    gathered = jnp.concatenate(
        [
            lax.dynamic_slice_in_dim(own_keys, own_local, 1, 0),
            lax.dynamic_slice_in_dim(own_values, own_local, 1, 0),
        ],
        axis=1,
    )
    order = [col_bits, 0] + list(range(1, col_bits)) + list(range(col_bits + 1, all_bits))

    from_above, from_below, got = exchange(
        (flat_tokens, 0, 0, (tile_rows - RAD) * tile_cols, RAD * tile_cols),
        None,
        "rows",
        gathered.reshape(-1, model_width),
    )
    gathered = gather_step(gathered, got.reshape(gathered.shape), order[0])
    extended = jnp.concatenate(
        [
            from_above.reshape(RAD, tile_cols, model_width),
            features,
            from_below.reshape(RAD, tile_cols, model_width),
        ],
        axis=0,
    )
    from_left, from_right, got = exchange(
        extended[:, :RAD].reshape(-1, model_width),
        extended[:, tile_cols - RAD :].reshape(-1, model_width),
        "cols",
        gathered.reshape(-1, model_width),
    )
    gathered = gather_step(gathered, got.reshape(gathered.shape), order[1])

    queries = jnp.dot(flat_tokens, w_query, preferred_element_type=jnp.float32).astype(jnp.bfloat16)
    grad_attended = jnp.dot(
        grad_out.reshape(-1, model_width), w_out.T, preferred_element_type=jnp.float32
    ).astype(jnp.bfloat16)

    halo_features = jnp.concatenate(
        [
            from_above,
            from_below,
            from_left,
            from_right,
            jnp.zeros((key_count - used, model_width), features.dtype),
        ],
        axis=0,
    )
    halo_keys = jnp.dot(halo_features, w_key, preferred_element_type=jnp.float32).astype(
        jnp.bfloat16
    )
    halo_values = jnp.dot(halo_features, w_value, preferred_element_type=jnp.float32).astype(
        jnp.bfloat16
    )

    for position in order[2:]:
        gathered = gather_step(gathered, partner(gathered, position), position)
    global_kv = jnp.take(gathered, jnp.asarray(gather_order(order, device_count)), axis=0)
    global_keys = global_kv[:, :model_width]
    global_values = global_kv[:, model_width:]

    def grid(height, width, row0, col0):
        a, b = np.meshgrid(np.arange(height) + row0, np.arange(width) + col0, indexing="ij")
        return a.reshape(-1), b.reshape(-1)

    parts = [
        grid(tile_rows, tile_cols, RAD, RAD),
        grid(RAD, tile_cols, 0, RAD),
        grid(RAD, tile_cols, RAD + tile_rows, RAD),
        grid(ext_rows, RAD, 0, 0),
        grid(ext_rows, RAD, 0, RAD + tile_cols),
    ]
    key_rows = np.zeros(key_count, np.int32)
    key_cols = np.zeros(key_count, np.int32)
    key_rows[:frame_keys] = np.concatenate([p[0] for p in parts])
    key_cols[:frame_keys] = np.concatenate([p[1] for p in parts])
    kind = np.full(key_count, 2, np.int32)
    kind[:frame_keys] = 0
    kind[key_count - device_count :] = 1

    query_rows = first_row + jnp.repeat(jnp.arange(tile_rows, dtype=jnp.int32), tile_cols)
    query_cols = first_col + jnp.tile(jnp.arange(tile_cols, dtype=jnp.int32), tile_rows)
    start_rows = jnp.clip(query_rows - RAD, 0, band_rows - KW)[:, None]
    start_cols = jnp.clip(query_cols - RAD, 0, band_cols - KW)[:, None]
    cell_rows = (first_row - RAD + jnp.asarray(key_rows))[None, :]
    cell_cols = (first_col - RAD + jnp.asarray(key_cols))[None, :]
    inside = (
        (cell_rows >= start_rows)
        & (cell_rows < start_rows + KW)
        & (cell_cols >= start_cols)
        & (cell_cols < start_cols + KW)
    )
    key_kind = jnp.asarray(kind)[None, :]
    keep = ((inside & (key_kind == 0)) | (key_kind == 1)).astype(jnp.float32)

    attended, query_grads, rounded_grads, wide_grads = attention(
        queries,
        (own_keys, halo_keys),
        (own_values, halo_values),
        global_keys,
        global_values,
        grad_attended,
        keep,
    )
    layer_out = (
        jnp.dot(attended, w_out, preferred_element_type=jnp.float32)
        .astype(jnp.bfloat16)
        .reshape(features.shape)
    )

    strips_from = tokens + 2 * band_keys

    def contribution(lo, hi):
        return jnp.dot(
            rounded_grads[0, lo:hi], w_key.T, preferred_element_type=jnp.float32
        ) + jnp.dot(rounded_grads[1, lo:hi], w_value.T, preferred_element_type=jnp.float32)

    strip_given = contribution(strips_from, frame_keys)
    rest_given = contribution(0, strips_from)

    def given(lo, hi):
        if lo >= strips_from:
            return strip_given[lo - strips_from : hi - strips_from]
        return rest_given[lo:hi]

    scatter = wide_grads[:, tokens:].reshape(
        (2,) + (2,) * all_bits + (model_width,)
    )
    left = list(range(all_bits - 1, -1, -1))
    back_order = [0, col_bits] + list(range(1, col_bits)) + list(range(col_bits + 1, all_bits))

    keep_part, send_part = scatter_split(scatter, left, back_order[0])
    strip_shape = (ext_rows, RAD, model_width)
    from_left, from_right, got = exchange(
        given(strips_from, strips_from + strip_keys).astype(jnp.bfloat16),
        given(strips_from + strip_keys, frame_keys).astype(jnp.bfloat16),
        "cols",
        split_wide(send_part.reshape(-1, model_width)),
    )
    scatter = keep_part + join_wide(got).reshape(keep_part.shape)
    received = jnp.pad(
        from_left.astype(jnp.float32).reshape(strip_shape), ((0, 0), (0, tile_cols - RAD), (0, 0))
    ) + jnp.pad(
        from_right.astype(jnp.float32).reshape(strip_shape), ((0, 0), (tile_cols - RAD, 0), (0, 0))
    )
    band_shape = (RAD, tile_cols, model_width)
    keep_part, send_part = scatter_split(scatter, left, back_order[1])
    from_above, from_below, got = exchange(
        (given(tokens, tokens + band_keys).reshape(band_shape) + received[:RAD])
        .reshape(-1, model_width)
        .astype(jnp.bfloat16),
        (given(tokens + band_keys, strips_from).reshape(band_shape) + received[RAD + tile_rows :])
        .reshape(-1, model_width)
        .astype(jnp.bfloat16),
        "rows",
        split_wide(send_part.reshape(-1, model_width)),
    )
    scatter = keep_part + join_wide(got).reshape(keep_part.shape)
    received = received[RAD : RAD + tile_rows]
    received = received + jnp.pad(
        from_above.astype(jnp.float32).reshape(band_shape), ((0, tile_rows - RAD), (0, 0), (0, 0))
    )
    received = received + jnp.pad(
        from_below.astype(jnp.float32).reshape(band_shape), ((tile_rows - RAD, 0), (0, 0), (0, 0))
    )
    for position in back_order[2:]:
        keep_part, send_part = scatter_split(scatter, left, position)
        scatter = keep_part + partner(send_part, position)
    own_grads = scatter.reshape(2, 1, model_width)

    own_given = given(0, tokens)
    own_row = (lax.dynamic_slice_in_dim(wide_grads, own_local, 1, 1) + own_grads).astype(
        jnp.bfloat16
    )
    own_row_given = jnp.dot(own_row[0], w_key.T, preferred_element_type=jnp.float32) + jnp.dot(
        own_row[1], w_value.T, preferred_element_type=jnp.float32
    )
    own_given = lax.dynamic_update_slice_in_dim(own_given, own_row_given, own_local, 0)

    grad_in = (
        jnp.dot(query_grads, w_query.T, preferred_element_type=jnp.float32)
        + own_given
        + received.reshape(tokens, model_width)
    )
    grad_in = grad_in.astype(jnp.bfloat16).reshape(features.shape)
    return (layer_out, grad_in)


def solution(mesh):
    placed = (P("rows", "cols", None), P(), P(), P(), P(), P(), P("rows", "cols", None))
    return jax.shard_map(
        shards,
        mesh=mesh,
        in_specs=placed,
        out_specs=(P("rows", "cols", None), P("rows", "cols", None)),
        check_vma=False,
    )
```

```python
import functools
import math

import jax
import jax.numpy as jnp
import numpy as np
from jax import lax
from jax.experimental import pallas as pl
from jax.sharding import PartitionSpec as P

HEADS = 16
KW = 13
RAD = 6


def bits(n):
    return n.bit_length() - 1


def device_bit(position):
    col_bits = bits(lax.axis_size("cols"))
    if position < col_bits:
        return "cols", position
    return "rows", position - col_bits


def own_bit(position):
    axis, bit = device_bit(position)
    return (lax.axis_index(axis) >> bit) % 2


def partner(x, position):
    axis, bit = device_bit(position)
    size = lax.axis_size(axis)
    return lax.ppermute(x, axis, [(i, i ^ (1 << bit)) for i in range(size)])


def exchange(to_lower, to_higher, axis, rider=None, rider_dim=0):
    size = lax.axis_size(axis)
    even = lax.axis_index(axis) % 2 == 0
    first = jnp.where(even, to_higher, to_lower)
    length = first.shape[rider_dim]
    if rider is not None:
        first = jnp.concatenate([first, rider], axis=rider_dim)
    got_first = lax.ppermute(first, axis, [(i, i ^ 1) for i in range(size)])
    links = [(i, i + 1) for i in range(1, size - 1, 2)] + [(i, i - 1) for i in range(2, size, 2)]
    got_second = lax.ppermute(jnp.where(even, to_lower, to_higher), axis, links)
    rider_got = None
    if rider is not None:
        rider_got = lax.slice_in_dim(got_first, length, None, axis=rider_dim)
        got_first = lax.slice_in_dim(got_first, 0, length, axis=rider_dim)
    from_lower = jnp.where(even, got_second, got_first)
    from_higher = jnp.where(even, got_first, got_second)
    return from_lower, from_higher, rider_got


def gather_step(x, other, position):
    low = own_bit(position) == 0
    return jnp.where(low, jnp.concatenate([x, other]), jnp.concatenate([other, x]))


def gather_order(order, count):
    where = np.zeros(count, np.int32)
    for l in range(count):
        where[l] = sum(((l >> bit) & 1) << step for step, bit in enumerate(order))
    return where


def scatter_split(x, order_left, position):
    axis = 1 + order_left.index(position)
    high = own_bit(position) == 1
    lower = lax.index_in_dim(x, 0, axis, keepdims=False)
    upper = lax.index_in_dim(x, 1, axis, keepdims=False)
    order_left.remove(position)
    return jnp.where(high, upper, lower), jnp.where(high, lower, upper)


def attention_kernel(
    own, first, last, q_ref, ko_ref, kh_ref, kg_ref, vo_ref, vh_ref, vg_ref, g_ref, mask_ref,
    o_ref, dq_ref, dkv_ref, wide_ref,
):
    head_size = q_ref.shape[1] // 2
    score_scale = 1.0 / math.sqrt(head_size)
    q = (q_ref[...] * score_scale).astype(q_ref.dtype)
    k = jnp.concatenate([ko_ref[...], kh_ref[...], kg_ref[...]], axis=0)
    v = jnp.concatenate([vo_ref[...], vh_ref[...], vg_ref[...]], axis=0)
    g = g_ref[...]
    keep = mask_ref[...] > 0
    lane_head = lax.broadcasted_iota(jnp.int32, q.shape, 1) // head_size
    rows = (((1,), (1,)), ((), ()))
    cols = (((0,), (0,)), ((), ()))
    out = jnp.zeros(q.shape, jnp.float32)
    dq = jnp.zeros(q.shape, jnp.float32)
    dk = None
    dv = None
    for head in range(2):
        mine = lane_head == head
        q_head = jnp.where(mine, q, jnp.zeros_like(q))
        g_head = jnp.where(mine, g, jnp.zeros_like(g))
        scores = lax.dot_general(q_head, k, rows, preferred_element_type=jnp.float32)
        scores = jnp.where(keep, scores, -1e30)
        row_max = jnp.max(scores, axis=1, keepdims=True)
        exps = jnp.exp(scores - row_max)
        probs = exps * (1.0 / jnp.sum(exps, axis=1, keepdims=True))
        rounded = probs.astype(jnp.bfloat16)
        attended = jnp.dot(rounded, v, preferred_element_type=jnp.float32)
        attended = attended.astype(jnp.bfloat16).astype(jnp.float32)
        out = jnp.where(mine, attended, out)
        delta = jnp.sum(
            jnp.where(mine, g.astype(jnp.float32) * attended, 0.0), axis=1, keepdims=True
        )
        dots = lax.dot_general(g_head, v, rows, preferred_element_type=jnp.float32)
        slopes = (probs * (dots - delta)).astype(jnp.bfloat16)
        dq = jnp.where(
            mine, jnp.dot(slopes, k, preferred_element_type=jnp.float32) * score_scale, dq
        )
        dk_head = lax.dot_general(slopes, q_head, cols, preferred_element_type=jnp.float32)
        dv_head = lax.dot_general(rounded, g_head, cols, preferred_element_type=jnp.float32)
        dk = dk_head if dk is None else dk + dk_head
        dv = dv_head if dv is None else dv + dv_head
    o_ref[...] = out.astype(o_ref.dtype)
    dq_ref[...] = dq.astype(dq_ref.dtype)
    dkv_ref[0] = dk.astype(dkv_ref.dtype)
    dkv_ref[1] = dv.astype(dkv_ref.dtype)
    wide_ref[0, :own] = dk[:own]
    wide_ref[1, :own] = dv[:own]
    wide_ref[0, own:] = dk[first:last]
    wide_ref[1, own:] = dv[first:last]


def attention(queries, keys, values, global_keys, global_values, grad_attended, keep):
    tokens, model_width = queries.shape
    first = keys[0].shape[0] + keys[1].shape[0]
    last = first + global_keys.shape[0]
    key_count = last
    lanes = 2 * (model_width // HEADS)
    steps = model_width // lanes
    token_block = pl.BlockSpec((tokens, lanes), lambda i: (0, i))
    key_block = pl.BlockSpec((key_count, lanes), lambda i: (0, i))
    own_block = pl.BlockSpec((keys[0].shape[0], lanes), lambda i: (0, i))
    halo_block = pl.BlockSpec((keys[1].shape[0], lanes), lambda i: (0, i))
    global_block = pl.BlockSpec((last - first, lanes), lambda i: (0, i))
    mask_block = pl.BlockSpec((tokens, key_count), lambda i: (0, 0))
    grads_block = pl.BlockSpec((2, key_count, lanes), lambda i: (0, 0, i))
    wide_rows = tokens + last - first
    wide_block = pl.BlockSpec((2, wide_rows, lanes), lambda i: (0, 0, i))
    flops = 2 * 2 * 6 * tokens * key_count * model_width
    moved = 2 * (3 * tokens * model_width + 2 * key_count * model_width) + 4 * (
        tokens * key_count + 2 * key_count * model_width
    )
    return pl.pallas_call(
        functools.partial(attention_kernel, tokens, first, last),
        grid=(steps,),
        in_specs=[
            token_block,
            own_block,
            halo_block,
            global_block,
            own_block,
            halo_block,
            global_block,
            token_block,
            mask_block,
        ],
        out_specs=[token_block, token_block, grads_block, wide_block],
        out_shape=[
            jax.ShapeDtypeStruct((tokens, model_width), jnp.bfloat16),
            jax.ShapeDtypeStruct((tokens, model_width), jnp.bfloat16),
            jax.ShapeDtypeStruct((2, key_count, model_width), jnp.bfloat16),
            jax.ShapeDtypeStruct((2, wide_rows, model_width), jnp.float32),
        ],
        cost_estimate=pl.CostEstimate(
            flops=flops, transcendentals=HEADS * tokens * key_count, bytes_accessed=moved
        ),
    )(queries, *keys, global_keys, *values, global_values, grad_attended, keep)


def split_wide(x):
    high = x.astype(jnp.bfloat16)
    low = (x - high.astype(jnp.float32)).astype(jnp.bfloat16)
    return jnp.concatenate([high, low], axis=0)


def join_wide(pair):
    half = pair.shape[0] // 2
    return pair[:half].astype(jnp.float32) + pair[half:].astype(jnp.float32)


def shards(features, w_query, w_key, w_value, w_out, reg_pos, grad_out):
    tile_rows, tile_cols, model_width = features.shape
    row_count = lax.axis_size("rows")
    col_count = lax.axis_size("cols")
    row_index = lax.axis_index("rows")
    col_index = lax.axis_index("cols")
    band_rows = tile_rows * row_count
    band_cols = tile_cols * col_count
    first_row = row_index * tile_rows
    first_col = col_index * tile_cols
    tokens = tile_rows * tile_cols
    device_count = row_count * col_count
    col_bits = bits(col_count)
    all_bits = col_bits + bits(row_count)
    ext_rows = tile_rows + 2 * RAD
    band_keys = RAD * tile_cols
    strip_keys = ext_rows * RAD
    frame_keys = tokens + 2 * band_keys + 2 * strip_keys
    used = frame_keys + device_count
    key_count = -(-used // 128) * 128

    flat_tokens = features.reshape(-1, model_width)
    own_keys = jnp.dot(flat_tokens, w_key, preferred_element_type=jnp.float32).astype(jnp.bfloat16)
    own_values = jnp.dot(flat_tokens, w_value, preferred_element_type=jnp.float32).astype(
        jnp.bfloat16
    )

    own_index = row_index * col_count + col_index
    own_place = lax.dynamic_index_in_dim(reg_pos, own_index, 0, keepdims=False)
    own_local = (own_place // band_cols - first_row) * tile_cols + (own_place % band_cols - first_col)
    gathered = jnp.concatenate(
        [
            lax.dynamic_slice_in_dim(own_keys, own_local, 1, 0),
            lax.dynamic_slice_in_dim(own_values, own_local, 1, 0),
        ],
        axis=1,
    )
    order = [col_bits, 0] + list(range(1, col_bits)) + list(range(col_bits + 1, all_bits))

    from_above, from_below, got = exchange(
        features[:RAD].reshape(-1, model_width),
        features[tile_rows - RAD :].reshape(-1, model_width),
        "rows",
        gathered.reshape(-1, model_width),
    )
    gathered = gather_step(gathered, got.reshape(gathered.shape), order[0])
    extended = jnp.concatenate(
        [
            from_above.reshape(RAD, tile_cols, model_width),
            features,
            from_below.reshape(RAD, tile_cols, model_width),
        ],
        axis=0,
    )
    from_left, from_right, got = exchange(
        extended[:, :RAD].reshape(-1, model_width),
        extended[:, tile_cols - RAD :].reshape(-1, model_width),
        "cols",
        gathered.reshape(-1, model_width),
    )
    gathered = gather_step(gathered, got.reshape(gathered.shape), order[1])

    queries = jnp.dot(flat_tokens, w_query, preferred_element_type=jnp.float32).astype(jnp.bfloat16)
    grad_attended = jnp.dot(
        grad_out.reshape(-1, model_width), w_out.T, preferred_element_type=jnp.float32
    ).astype(jnp.bfloat16)

    halo_features = jnp.concatenate(
        [
            from_above,
            from_below,
            from_left,
            from_right,
            jnp.zeros((key_count - used, model_width), features.dtype),
        ],
        axis=0,
    )
    halo_keys = jnp.dot(halo_features, w_key, preferred_element_type=jnp.float32).astype(
        jnp.bfloat16
    )
    halo_values = jnp.dot(halo_features, w_value, preferred_element_type=jnp.float32).astype(
        jnp.bfloat16
    )

    for position in order[2:]:
        gathered = gather_step(gathered, partner(gathered, position), position)
    global_kv = jnp.take(gathered, jnp.asarray(gather_order(order, device_count)), axis=0)
    global_keys = global_kv[:, :model_width]
    global_values = global_kv[:, model_width:]

    def grid(height, width, row0, col0):
        a, b = np.meshgrid(np.arange(height) + row0, np.arange(width) + col0, indexing="ij")
        return a.reshape(-1), b.reshape(-1)

    parts = [
        grid(tile_rows, tile_cols, RAD, RAD),
        grid(RAD, tile_cols, 0, RAD),
        grid(RAD, tile_cols, RAD + tile_rows, RAD),
        grid(ext_rows, RAD, 0, 0),
        grid(ext_rows, RAD, 0, RAD + tile_cols),
    ]
    key_rows = np.zeros(key_count, np.int32)
    key_cols = np.zeros(key_count, np.int32)
    key_rows[:frame_keys] = np.concatenate([p[0] for p in parts])
    key_cols[:frame_keys] = np.concatenate([p[1] for p in parts])
    kind = np.full(key_count, 2, np.int32)
    kind[:frame_keys] = 0
    kind[key_count - device_count :] = 1

    query_rows = first_row + jnp.repeat(jnp.arange(tile_rows, dtype=jnp.int32), tile_cols)
    query_cols = first_col + jnp.tile(jnp.arange(tile_cols, dtype=jnp.int32), tile_rows)
    start_rows = jnp.clip(query_rows - RAD, 0, band_rows - KW)[:, None]
    start_cols = jnp.clip(query_cols - RAD, 0, band_cols - KW)[:, None]
    cell_rows = (first_row - RAD + jnp.asarray(key_rows))[None, :]
    cell_cols = (first_col - RAD + jnp.asarray(key_cols))[None, :]
    inside = (
        (cell_rows >= start_rows)
        & (cell_rows < start_rows + KW)
        & (cell_cols >= start_cols)
        & (cell_cols < start_cols + KW)
    )
    key_kind = jnp.asarray(kind)[None, :]
    keep = ((inside & (key_kind == 0)) | (key_kind == 1)).astype(jnp.float32)

    attended, query_grads, rounded_grads, wide_grads = attention(
        queries,
        (own_keys, halo_keys),
        (own_values, halo_values),
        global_keys,
        global_values,
        grad_attended,
        keep,
    )
    layer_out = (
        jnp.dot(attended, w_out, preferred_element_type=jnp.float32)
        .astype(jnp.bfloat16)
        .reshape(features.shape)
    )

    strips_from = tokens + 2 * band_keys

    def contribution(lo, hi):
        return jnp.dot(
            rounded_grads[0, lo:hi], w_key.T, preferred_element_type=jnp.float32
        ) + jnp.dot(rounded_grads[1, lo:hi], w_value.T, preferred_element_type=jnp.float32)

    strip_given = contribution(strips_from, frame_keys)
    rest_given = contribution(0, strips_from)

    def given(lo, hi):
        if lo >= strips_from:
            return strip_given[lo - strips_from : hi - strips_from]
        return rest_given[lo:hi]

    scatter = wide_grads[:, tokens:].reshape(
        (2,) + (2,) * all_bits + (model_width,)
    )
    left = list(range(all_bits - 1, -1, -1))
    back_order = [0, col_bits] + list(range(1, col_bits)) + list(range(col_bits + 1, all_bits))

    keep_part, send_part = scatter_split(scatter, left, back_order[0])
    strip_shape = (ext_rows, RAD, model_width)
    from_left, from_right, got = exchange(
        given(strips_from, strips_from + strip_keys).astype(jnp.bfloat16),
        given(strips_from + strip_keys, frame_keys).astype(jnp.bfloat16),
        "cols",
        split_wide(send_part.reshape(-1, model_width)),
    )
    scatter = keep_part + join_wide(got).reshape(keep_part.shape)
    received = jnp.pad(
        from_left.astype(jnp.float32).reshape(strip_shape), ((0, 0), (0, tile_cols - RAD), (0, 0))
    ) + jnp.pad(
        from_right.astype(jnp.float32).reshape(strip_shape), ((0, 0), (tile_cols - RAD, 0), (0, 0))
    )
    band_shape = (RAD, tile_cols, model_width)
    keep_part, send_part = scatter_split(scatter, left, back_order[1])
    from_above, from_below, got = exchange(
        (given(tokens, tokens + band_keys).reshape(band_shape) + received[:RAD])
        .reshape(-1, model_width)
        .astype(jnp.bfloat16),
        (given(tokens + band_keys, strips_from).reshape(band_shape) + received[RAD + tile_rows :])
        .reshape(-1, model_width)
        .astype(jnp.bfloat16),
        "rows",
        split_wide(send_part.reshape(-1, model_width)),
    )
    scatter = keep_part + join_wide(got).reshape(keep_part.shape)
    received = received[RAD : RAD + tile_rows]
    received = received + jnp.pad(
        from_above.astype(jnp.float32).reshape(band_shape), ((0, tile_rows - RAD), (0, 0), (0, 0))
    )
    received = received + jnp.pad(
        from_below.astype(jnp.float32).reshape(band_shape), ((tile_rows - RAD, 0), (0, 0), (0, 0))
    )
    for position in back_order[2:]:
        keep_part, send_part = scatter_split(scatter, left, position)
        scatter = keep_part + partner(send_part, position)
    own_grads = scatter.reshape(2, 1, model_width)

    query_part = jnp.dot(query_grads, w_query.T, preferred_element_type=jnp.float32)
    base = query_part + given(0, tokens)
    own_row = (lax.dynamic_slice_in_dim(wide_grads, own_local, 1, 1) + own_grads).astype(
        jnp.bfloat16
    )
    own_row_given = (
        lax.dynamic_slice_in_dim(query_part, own_local, 1, 0)
        + jnp.dot(own_row[0], w_key.T, preferred_element_type=jnp.float32)
        + jnp.dot(own_row[1], w_value.T, preferred_element_type=jnp.float32)
    )
    base = lax.dynamic_update_slice_in_dim(base, own_row_given, own_local, 0)
    grad_in = base + received.reshape(tokens, model_width)
    grad_in = grad_in.astype(jnp.bfloat16).reshape(features.shape)
    return (layer_out, grad_in)


def solution(mesh):
    placed = (P("rows", "cols", None), P(), P(), P(), P(), P(), P("rows", "cols", None))
    return jax.shard_map(
        shards,
        mesh=mesh,
        in_specs=placed,
        out_specs=(P("rows", "cols", None), P("rows", "cols", None)),
        check_vma=False,
    )
```

```python
import functools
import math

import jax
import jax.numpy as jnp
import numpy as np
from jax import lax
from jax.experimental import pallas as pl
from jax.sharding import PartitionSpec as P

HEADS = 16
KW = 13
RAD = 6


def bits(n):
    return n.bit_length() - 1


def device_bit(position):
    col_bits = bits(lax.axis_size("cols"))
    if position < col_bits:
        return "cols", position
    return "rows", position - col_bits


def own_bit(position):
    axis, bit = device_bit(position)
    return (lax.axis_index(axis) >> bit) % 2


def partner(x, position):
    axis, bit = device_bit(position)
    size = lax.axis_size(axis)
    return lax.ppermute(x, axis, [(i, i ^ (1 << bit)) for i in range(size)])


def exchange(to_lower, to_higher, axis, rider=None, rider_dim=0):
    size = lax.axis_size(axis)
    even = lax.axis_index(axis) % 2 == 0
    first = jnp.where(even, to_higher, to_lower)
    length = first.shape[rider_dim]
    if rider is not None:
        first = jnp.concatenate([first, rider], axis=rider_dim)
    got_first = lax.ppermute(first, axis, [(i, i ^ 1) for i in range(size)])
    links = [(i, i + 1) for i in range(1, size - 1, 2)] + [(i, i - 1) for i in range(2, size, 2)]
    got_second = lax.ppermute(jnp.where(even, to_lower, to_higher), axis, links)
    rider_got = None
    if rider is not None:
        rider_got = lax.slice_in_dim(got_first, length, None, axis=rider_dim)
        got_first = lax.slice_in_dim(got_first, 0, length, axis=rider_dim)
    from_lower = jnp.where(even, got_second, got_first)
    from_higher = jnp.where(even, got_first, got_second)
    return from_lower, from_higher, rider_got


def gather_step(x, other, position):
    low = own_bit(position) == 0
    return jnp.where(low, jnp.concatenate([x, other]), jnp.concatenate([other, x]))


def gather_order(order, count):
    where = np.zeros(count, np.int32)
    for l in range(count):
        where[l] = sum(((l >> bit) & 1) << step for step, bit in enumerate(order))
    return where


def scatter_split(x, order_left, position):
    axis = 1 + order_left.index(position)
    high = own_bit(position) == 1
    lower = lax.index_in_dim(x, 0, axis, keepdims=False)
    upper = lax.index_in_dim(x, 1, axis, keepdims=False)
    order_left.remove(position)
    return jnp.where(high, upper, lower), jnp.where(high, lower, upper)


def attention_kernel(
    own, first, last, q_ref, ko_ref, kh_ref, kg_ref, vo_ref, vh_ref, vg_ref, g_ref, mask_ref,
    o_ref, dq_ref, dkv_ref, wide_ref,
):
    head_size = q_ref.shape[1] // 2
    score_scale = 1.0 / math.sqrt(head_size)
    q = (q_ref[...] * score_scale).astype(q_ref.dtype)
    k = jnp.concatenate([ko_ref[...], kh_ref[...], kg_ref[...]], axis=0)
    v = jnp.concatenate([vo_ref[...], vh_ref[...], vg_ref[...]], axis=0)
    g = g_ref[...]
    keep = mask_ref[...] > 0
    lane_head = lax.broadcasted_iota(jnp.int32, q.shape, 1) // head_size
    rows = (((1,), (1,)), ((), ()))
    cols = (((0,), (0,)), ((), ()))
    out = jnp.zeros(q.shape, jnp.float32)
    dq = jnp.zeros(q.shape, jnp.float32)
    dk = None
    dv = None
    for head in range(2):
        mine = lane_head == head
        q_head = jnp.where(mine, q, jnp.zeros_like(q))
        g_head = jnp.where(mine, g, jnp.zeros_like(g))
        scores = lax.dot_general(q_head, k, rows, preferred_element_type=jnp.float32)
        scores = jnp.where(keep, scores, -1e30)
        row_max = jnp.max(scores, axis=1, keepdims=True)
        exps = jnp.exp(scores - row_max)
        probs = exps * (1.0 / jnp.sum(exps, axis=1, keepdims=True))
        rounded = probs.astype(jnp.bfloat16)
        attended = jnp.dot(rounded, v, preferred_element_type=jnp.float32)
        attended = attended.astype(jnp.bfloat16).astype(jnp.float32)
        out = jnp.where(mine, attended, out)
        delta = jnp.sum(
            jnp.where(mine, g.astype(jnp.float32) * attended, 0.0), axis=1, keepdims=True
        )
        dots = lax.dot_general(g_head, v, rows, preferred_element_type=jnp.float32)
        slopes = (probs * (dots - delta)).astype(jnp.bfloat16)
        dq = jnp.where(
            mine, jnp.dot(slopes, k, preferred_element_type=jnp.float32) * score_scale, dq
        )
        dk_head = lax.dot_general(slopes, q_head, cols, preferred_element_type=jnp.float32)
        dv_head = lax.dot_general(rounded, g_head, cols, preferred_element_type=jnp.float32)
        dk = dk_head if dk is None else dk + dk_head
        dv = dv_head if dv is None else dv + dv_head
    o_ref[...] = out.astype(o_ref.dtype)
    dq_ref[...] = dq.astype(dq_ref.dtype)
    dkv_ref[0] = dk.astype(dkv_ref.dtype)
    dkv_ref[1] = dv.astype(dkv_ref.dtype)
    wide_ref[0, :own] = dk[:own]
    wide_ref[1, :own] = dv[:own]
    wide_ref[0, own:] = dk[first:last]
    wide_ref[1, own:] = dv[first:last]


def attention(queries, keys, values, global_keys, global_values, grad_attended, keep):
    tokens, model_width = queries.shape
    first = keys[0].shape[0] + keys[1].shape[0]
    last = first + global_keys.shape[0]
    key_count = last
    lanes = 2 * (model_width // HEADS)
    steps = model_width // lanes
    token_block = pl.BlockSpec((tokens, lanes), lambda i: (0, i))
    key_block = pl.BlockSpec((key_count, lanes), lambda i: (0, i))
    own_block = pl.BlockSpec((keys[0].shape[0], lanes), lambda i: (0, i))
    halo_block = pl.BlockSpec((keys[1].shape[0], lanes), lambda i: (0, i))
    global_block = pl.BlockSpec((last - first, lanes), lambda i: (0, i))
    mask_block = pl.BlockSpec((tokens, key_count), lambda i: (0, 0))
    grads_block = pl.BlockSpec((2, key_count, lanes), lambda i: (0, 0, i))
    wide_rows = tokens + last - first
    wide_block = pl.BlockSpec((2, wide_rows, lanes), lambda i: (0, 0, i))
    flops = 2 * 2 * 6 * tokens * key_count * model_width
    moved = 2 * (3 * tokens * model_width + 2 * key_count * model_width) + 4 * (
        tokens * key_count + 2 * key_count * model_width
    )
    return pl.pallas_call(
        functools.partial(attention_kernel, tokens, first, last),
        grid=(steps,),
        in_specs=[
            token_block,
            own_block,
            halo_block,
            global_block,
            own_block,
            halo_block,
            global_block,
            token_block,
            mask_block,
        ],
        out_specs=[token_block, token_block, grads_block, wide_block],
        out_shape=[
            jax.ShapeDtypeStruct((tokens, model_width), jnp.bfloat16),
            jax.ShapeDtypeStruct((tokens, model_width), jnp.bfloat16),
            jax.ShapeDtypeStruct((2, key_count, model_width), jnp.bfloat16),
            jax.ShapeDtypeStruct((2, wide_rows, model_width), jnp.float32),
        ],
        cost_estimate=pl.CostEstimate(
            flops=flops, transcendentals=HEADS * tokens * key_count, bytes_accessed=moved
        ),
    )(queries, *keys, global_keys, *values, global_values, grad_attended, keep)


def split_wide(x):
    high = x.astype(jnp.bfloat16)
    low = (x - high.astype(jnp.float32)).astype(jnp.bfloat16)
    return jnp.concatenate([high, low], axis=0)


def join_wide(pair):
    half = pair.shape[0] // 2
    return pair[:half].astype(jnp.float32) + pair[half:].astype(jnp.float32)


def shards(features, w_query, w_key, w_value, w_out, reg_pos, grad_out):
    tile_rows, tile_cols, model_width = features.shape
    row_count = lax.axis_size("rows")
    col_count = lax.axis_size("cols")
    row_index = lax.axis_index("rows")
    col_index = lax.axis_index("cols")
    band_rows = tile_rows * row_count
    band_cols = tile_cols * col_count
    first_row = row_index * tile_rows
    first_col = col_index * tile_cols
    tokens = tile_rows * tile_cols
    device_count = row_count * col_count
    col_bits = bits(col_count)
    all_bits = col_bits + bits(row_count)
    ext_rows = tile_rows + 2 * RAD
    band_keys = RAD * tile_cols
    strip_keys = ext_rows * RAD
    frame_keys = tokens + 2 * band_keys + 2 * strip_keys
    used = frame_keys + device_count
    key_count = -(-used // 128) * 128

    flat_tokens = features.reshape(-1, model_width)
    own_keys = jnp.dot(flat_tokens, w_key, preferred_element_type=jnp.float32).astype(jnp.bfloat16)
    own_values = jnp.dot(flat_tokens, w_value, preferred_element_type=jnp.float32).astype(
        jnp.bfloat16
    )

    own_index = row_index * col_count + col_index
    own_place = lax.dynamic_index_in_dim(reg_pos, own_index, 0, keepdims=False)
    own_local = (own_place // band_cols - first_row) * tile_cols + (own_place % band_cols - first_col)
    gathered = jnp.concatenate(
        [
            lax.dynamic_slice_in_dim(own_keys, own_local, 1, 0),
            lax.dynamic_slice_in_dim(own_values, own_local, 1, 0),
        ],
        axis=1,
    )
    order = [col_bits, 0] + list(range(1, col_bits)) + list(range(col_bits + 1, all_bits))

    from_above, from_below, got = exchange(
        features[:RAD].reshape(-1, model_width),
        features[tile_rows - RAD :].reshape(-1, model_width),
        "rows",
        gathered.reshape(-1, model_width),
    )
    gathered = gather_step(gathered, got.reshape(gathered.shape), order[0])
    extended = jnp.concatenate(
        [
            from_above.reshape(RAD, tile_cols, model_width),
            features,
            from_below.reshape(RAD, tile_cols, model_width),
        ],
        axis=0,
    )
    from_left, from_right, got = exchange(
        extended[:, :RAD].reshape(-1, model_width),
        extended[:, tile_cols - RAD :].reshape(-1, model_width),
        "cols",
        gathered.reshape(-1, model_width),
    )
    gathered = gather_step(gathered, got.reshape(gathered.shape), order[1])

    queries = jnp.dot(flat_tokens, w_query, preferred_element_type=jnp.float32).astype(jnp.bfloat16)
    grad_attended = jnp.dot(
        grad_out.reshape(-1, model_width), w_out.T, preferred_element_type=jnp.float32
    ).astype(jnp.bfloat16)

    halo_features = jnp.concatenate(
        [
            from_above,
            from_below,
            from_left,
            from_right,
            jnp.zeros((key_count - used, model_width), features.dtype),
        ],
        axis=0,
    )
    halo_keys = jnp.dot(halo_features, w_key, preferred_element_type=jnp.float32).astype(
        jnp.bfloat16
    )
    halo_values = jnp.dot(halo_features, w_value, preferred_element_type=jnp.float32).astype(
        jnp.bfloat16
    )

    for position in order[2:]:
        gathered = gather_step(gathered, partner(gathered, position), position)
    global_kv = jnp.take(gathered, jnp.asarray(gather_order(order, device_count)), axis=0)
    global_keys = global_kv[:, :model_width]
    global_values = global_kv[:, model_width:]

    def grid(height, width, row0, col0):
        a, b = np.meshgrid(np.arange(height) + row0, np.arange(width) + col0, indexing="ij")
        return a.reshape(-1), b.reshape(-1)

    parts = [
        grid(tile_rows, tile_cols, RAD, RAD),
        grid(RAD, tile_cols, 0, RAD),
        grid(RAD, tile_cols, RAD + tile_rows, RAD),
        grid(ext_rows, RAD, 0, 0),
        grid(ext_rows, RAD, 0, RAD + tile_cols),
    ]
    key_rows = np.zeros(key_count, np.int32)
    key_cols = np.zeros(key_count, np.int32)
    key_rows[:frame_keys] = np.concatenate([p[0] for p in parts])
    key_cols[:frame_keys] = np.concatenate([p[1] for p in parts])
    kind = np.full(key_count, 2, np.int32)
    kind[:frame_keys] = 0
    kind[key_count - device_count :] = 1

    query_rows = first_row + jnp.repeat(jnp.arange(tile_rows, dtype=jnp.int32), tile_cols)
    query_cols = first_col + jnp.tile(jnp.arange(tile_cols, dtype=jnp.int32), tile_rows)
    start_rows = jnp.clip(query_rows - RAD, 0, band_rows - KW)[:, None]
    start_cols = jnp.clip(query_cols - RAD, 0, band_cols - KW)[:, None]
    cell_rows = (first_row - RAD + jnp.asarray(key_rows))[None, :]
    cell_cols = (first_col - RAD + jnp.asarray(key_cols))[None, :]
    inside = (
        (cell_rows >= start_rows)
        & (cell_rows < start_rows + KW)
        & (cell_cols >= start_cols)
        & (cell_cols < start_cols + KW)
    )
    key_kind = jnp.asarray(kind)[None, :]
    keep = ((inside & (key_kind == 0)) | (key_kind == 1)).astype(jnp.bfloat16)

    attended, query_grads, rounded_grads, wide_grads = attention(
        queries,
        (own_keys, halo_keys),
        (own_values, halo_values),
        global_keys,
        global_values,
        grad_attended,
        keep,
    )
    layer_out = (
        jnp.dot(attended, w_out, preferred_element_type=jnp.float32)
        .astype(jnp.bfloat16)
        .reshape(features.shape)
    )

    strips_from = tokens + 2 * band_keys

    def contribution(lo, hi):
        return jnp.dot(
            rounded_grads[0, lo:hi], w_key.T, preferred_element_type=jnp.float32
        ) + jnp.dot(rounded_grads[1, lo:hi], w_value.T, preferred_element_type=jnp.float32)

    strip_given = contribution(strips_from, frame_keys)
    rest_given = contribution(0, strips_from)

    def given(lo, hi):
        if lo >= strips_from:
            return strip_given[lo - strips_from : hi - strips_from]
        return rest_given[lo:hi]

    scatter = wide_grads[:, tokens:].reshape(
        (2,) + (2,) * all_bits + (model_width,)
    )
    left = list(range(all_bits - 1, -1, -1))
    back_order = [0, col_bits] + list(range(1, col_bits)) + list(range(col_bits + 1, all_bits))

    keep_part, send_part = scatter_split(scatter, left, back_order[0])
    strip_shape = (ext_rows, RAD, model_width)
    from_left, from_right, got = exchange(
        given(strips_from, strips_from + strip_keys).astype(jnp.bfloat16),
        given(strips_from + strip_keys, frame_keys).astype(jnp.bfloat16),
        "cols",
        split_wide(send_part.reshape(-1, model_width)),
    )
    scatter = keep_part + join_wide(got).reshape(keep_part.shape)
    received = jnp.pad(
        from_left.astype(jnp.float32).reshape(strip_shape), ((0, 0), (0, tile_cols - RAD), (0, 0))
    ) + jnp.pad(
        from_right.astype(jnp.float32).reshape(strip_shape), ((0, 0), (tile_cols - RAD, 0), (0, 0))
    )
    band_shape = (RAD, tile_cols, model_width)
    keep_part, send_part = scatter_split(scatter, left, back_order[1])
    from_above, from_below, got = exchange(
        (given(tokens, tokens + band_keys).reshape(band_shape) + received[:RAD])
        .reshape(-1, model_width)
        .astype(jnp.bfloat16),
        (given(tokens + band_keys, strips_from).reshape(band_shape) + received[RAD + tile_rows :])
        .reshape(-1, model_width)
        .astype(jnp.bfloat16),
        "rows",
        split_wide(send_part.reshape(-1, model_width)),
    )
    scatter = keep_part + join_wide(got).reshape(keep_part.shape)
    received = received[RAD : RAD + tile_rows]
    received = received + jnp.pad(
        from_above.astype(jnp.float32).reshape(band_shape), ((0, tile_rows - RAD), (0, 0), (0, 0))
    )
    received = received + jnp.pad(
        from_below.astype(jnp.float32).reshape(band_shape), ((tile_rows - RAD, 0), (0, 0), (0, 0))
    )
    for position in back_order[2:]:
        keep_part, send_part = scatter_split(scatter, left, position)
        scatter = keep_part + partner(send_part, position)
    own_grads = scatter.reshape(2, 1, model_width)

    own_given = given(0, tokens)
    own_row = (lax.dynamic_slice_in_dim(wide_grads, own_local, 1, 1) + own_grads).astype(
        jnp.bfloat16
    )
    own_row_given = jnp.dot(own_row[0], w_key.T, preferred_element_type=jnp.float32) + jnp.dot(
        own_row[1], w_value.T, preferred_element_type=jnp.float32
    )
    own_given = lax.dynamic_update_slice_in_dim(own_given, own_row_given, own_local, 0)

    grad_in = (
        jnp.dot(query_grads, w_query.T, preferred_element_type=jnp.float32)
        + own_given
        + received.reshape(tokens, model_width)
    )
    grad_in = grad_in.astype(jnp.bfloat16).reshape(features.shape)
    return (layer_out, grad_in)


def solution(mesh):
    placed = (P("rows", "cols", None), P(), P(), P(), P(), P(), P("rows", "cols", None))
    return jax.shard_map(
        shards,
        mesh=mesh,
        in_specs=placed,
        out_specs=(P("rows", "cols", None), P("rows", "cols", None)),
        check_vma=False,
    )
```
